128 devices in a mesh: gx: 8 (over x, z_lo), gy: 4 (over z_hi, core), gz: 4 (over y).
Axes of the slice: x: 4, y: 4, z: 4 (z_hi: 2, z_lo: 2; z = z_hi * 2 + z_lo), core: 2. Of those that a mesh axis runs over, the one named last changes fastest.
Arguments:
- e_forward: float32 [3, 128, 64, 4096], P(None, 'gx', 'gy', 'gz'), may hold values from -6 to 6
- e_adjoint: float32 [3, 128, 64, 4096], P(None, 'gx', 'gy', 'gz'), may hold values from -6 to 6
- h_adjoint: float32 [3, 128, 64, 4096], P(None, 'gx', 'gy', 'gz'), may hold values from -6 to 6
- inv_perm: float32 [128, 64, 4096], P('gx', 'gy', 'gz'), may hold values from 0.08 to 1
- voxel_cell: int32 [8, 4, 4, 1024], P('gx', 'gy', 'gz'), may hold values from 0 to 262143
- voxel_owner: int32 [8, 4, 4, 1024, 1], P('gx', 'gy', 'gz'), may hold values from 0 to 127; in each aligned block of 1024 rows (0 to 1023, 1024 to 2047, ..., all dimensions but the last counted through in order) at most 16 rows name the same one
- voxel_slot: int32 [8, 4, 4, 1024], P('gx', 'gy', 'gz'), may hold values from 0 to 255
Outputs:
- e_adjoint_new: float32 [3, 128, 64, 4096], P(None, 'gx', 'gy', 'gz')
- h_adjoint_new: float32 [3, 128, 64, 4096], P(None, 'gx', 'gy', 'gz')
- gradient: float32 [32768], P(('gx', 'gy', 'gz'))
The draws below stay inside these ranges and needn't reach their ends.
Inputs may be any that keep to these rules, and one draw needn't show every extreme that they name: `voxel_owner`: among the 1024 design voxels of one device, at most 16 name the same owner.
All inputs are finite; a program needn't handle non-finite values.
Results may differ from the reference program's by a relative error of at most 0.00014.
Values sent between devices are 32-bit elements; how exact they have to be, the bound alone decides.
No kernel may reach another device: no remote copies, remote signals or barrier semaphores. Data moves between devices by JAX's collectives and lax.ppermute only.
A program may use at most 576 MiB of HBM per device.

```python
import math
import jax
import jax.numpy as jnp
import numpy as np
from jax import lax

CX = 16
CY = 16
CZ = 1024
STEPS = 2
DV = 1024
P_DEV = 256
CAP = 16
NX = 128
NY = 64
NZ = 4096
N_GX = 8
N_GY = 4
N_GZ = 4
DEVICES = 128


def with_ends(array, key, least, high):
    place = [jax.random.randint(jax.random.fold_in(key, axis), (), 0, length) for axis, length in enumerate(array.shape)]
    widest = array.shape.index(max(array.shape))
    beside = place[:widest] + [(place[widest] + 1) % array.shape[widest]] + place[widest + 1:]
    return array.at[tuple(place)].set(least).at[tuple(beside)].set(high)


def shard_levels(rng, dims, pieces, smallest, largest):
    loudness, own = 1.0, jax.random.fold_in(rng, 6)
    for axis_at, shards_of in pieces:
        steps = jnp.exp(jax.random.uniform(jax.random.fold_in(own, axis_at), (shards_of,), jnp.float32, smallest / len(pieces), largest / len(pieces)))
        loudness = loudness * jnp.repeat(steps, dims[axis_at] // shards_of).reshape([-1 if axis == axis_at else 1 for axis in range(len(dims))])
    return loudness


def assign_block(stream_key, own, number, rows, number_of, top, most, slope):
    sequence = jax.random.permutation(stream_key, number_of)
    heavy_load, usual = shares(number_of, rows * top, most, slope, True), shares(number_of, rows * top, most, slope, False)
    places = jnp.arange(number_of)

    def named(tallies, offset_by):
        used = int((tallies > 0).sum())
        fixed = max(1, used // 4)
        shifted = fixed + (places - fixed + offset_by * (used - fixed)) % max(1, number_of - fixed)
        return jnp.zeros((number_of,), jnp.int32).at[sequence[jnp.where(places < fixed, places, shifted)]].set(jnp.asarray(tallies, jnp.int32))

    tallies = jnp.where(number % 4 == 0, named(heavy_load, number // 4), named(usual, number - number // 4 - 1))
    mixed = jax.random.permutation(jax.random.fold_in(own, 3), number_of)
    source_of, receiver = mixed[0:number_of // 2 * 2:2], mixed[1:number_of // 2 * 2:2]
    room = jnp.minimum(tallies[source_of] - 1, most - tallies[receiver]) // 2
    room = jnp.where((source_of == sequence[0]) | (receiver == sequence[0]) | (tallies[receiver] == 0), 0, jnp.maximum(room, 0))
    shifted = jax.random.randint(jax.random.fold_in(own, 4), (number_of // 2,), 0, 1 << 20) % (room + 1)
    tallies = tallies.at[source_of].add(-shifted).at[receiver].add(shifted)
    members = jnp.searchsorted(jnp.cumsum(tallies), jnp.arange(rows * top), side="right").astype(jnp.int32)
    listing = members.reshape(top, rows).T
    listing = listing[jax.random.permutation(jax.random.fold_in(own, 1), rows)]
    offset_by = jax.random.randint(jax.random.fold_in(own, 2), (rows, 1), 0, top)
    return jnp.take_along_axis(listing, (jnp.arange(top)[None, :] + offset_by) % top, axis=1)


def shares(amount, total, bound, slope, full):
    weights = [(1 << 20) // math.isqrt(standing ** slope) + 1 for standing in range(1, amount + 1)]
    largest = bound if full else min(bound, max(-(-total // amount), total * weights[0] // sum(weights)))
    least = 1 if total - largest >= amount - 1 else 0
    holding, surplus = [largest] + [least] * (amount - 1), total - largest - least * (amount - 1)
    while surplus > 0:
        movable = [i for i in range(1, amount) if holding[i] < largest] or [i for i in range(1, amount) if holding[i] < bound]
        pool, remaining = sum([weights[i] for i in movable]), surplus
        for i in movable:
            addition = min(bound - holding[i], max(1, remaining * weights[i] // pool), surplus)
            holding[i] = holding[i] + addition
            surplus = surplus - addition
    return np.array(holding)


def normal_values(rng, dims, spread, bound, split=(), kind=jnp.bfloat16):
    entries = jax.random.normal(rng, dims, jnp.float32) * spread
    if len(split) > 0:
        entries = shard_levels(rng, dims, split, -0.22, 0.18) * entries
    return jnp.clip(entries, min=-bound, max=bound).astype(kind)


def setup_inputs(seed: int = 0) -> dict:
    key_of = jax.random.split(jax.random.key(seed), 8)
    e_forward = normal_values(key_of[0], (3, NX, NY, NZ), 1.0, 6.0, ((1, 8), (2, 4), (3, 4)), jnp.float32)
    e_adjoint = normal_values(key_of[1], (3, NX, NY, NZ), 1.0, 6.0, ((1, 8), (2, 4), (3, 4)), jnp.float32)
    h_adjoint = normal_values(key_of[2], (3, NX, NY, NZ), 1.0, 6.0, ((1, 8), (2, 4), (3, 4)), jnp.float32)
    inv_perm = jnp.clip(jnp.exp(math.log(1.0) - 2.5257287 * jax.random.uniform(key_of[3], (NX, NY, NZ), jnp.float32) ** shard_levels(key_of[3], (NX, NY, NZ), ((0, 8), (1, 4), (2, 4)), -0.2, 0.2)), 0.08, 1.0)
    voxel_cell = with_ends(jax.random.randint(key_of[4], (N_GX, N_GY, N_GZ, DV), 0, CX * CY * CZ), jax.random.fold_in(key_of[4], 1), 0, (CX * CY * CZ) - 1).astype(jnp.int32)
    voxel_owner_keys = jax.random.split(jax.random.fold_in(key_of[5], 1), N_GX * N_GY * N_GZ * DV // DV)
    voxel_owner_turns = jax.random.permutation(jax.random.fold_in(key_of[5], 3), N_GX * N_GY * N_GZ * DV // DV)
    voxel_owner = jax.vmap(lambda own, number: assign_block(jax.random.fold_in(key_of[5], 2), own, number, DV, DEVICES, 1, CAP, 2))(voxel_owner_keys, voxel_owner_turns).reshape((N_GX, N_GY, N_GZ, DV, 1))
    voxel_slot = with_ends(jax.random.randint(key_of[6], (N_GX, N_GY, N_GZ, DV), 0, P_DEV), jax.random.fold_in(key_of[6], 1), 0, P_DEV - 1).astype(jnp.int32)
    return {"e_forward": e_forward, "e_adjoint": e_adjoint, "h_adjoint": h_adjoint, "inv_perm": inv_perm, "voxel_cell": voxel_cell, "voxel_owner": voxel_owner, "voxel_slot": voxel_slot}


courant = 0.5


def forward_diff(field, axis):
    widths = [(0, 1) if index == axis else (0, 0) for index in range(3)]
    padded = jnp.pad(field, widths)
    return lax.slice_in_dim(padded, 1, field.shape[axis] + 1, axis=axis) - field


def backward_diff(field, axis):
    widths = [(1, 0) if index == axis else (0, 0) for index in range(3)]
    padded = jnp.pad(field, widths)
    return field - lax.slice_in_dim(padded, 0, field.shape[axis], axis=axis)


def reference(e_forward, e_adjoint, h_adjoint, inv_perm, voxel_cell, voxel_owner, voxel_slot):
    elec_x, elec_y, elec_z = e_adjoint[0], e_adjoint[1], e_adjoint[2]
    magn_x, magn_y, magn_z = h_adjoint[0], h_adjoint[1], h_adjoint[2]
    for repeat in range(STEPS):
        magn_x = magn_x - courant * (forward_diff(elec_z, 1) - forward_diff(elec_y, 2))
        magn_y = magn_y - courant * (forward_diff(elec_x, 2) - forward_diff(elec_z, 0))
        magn_z = magn_z - courant * (forward_diff(elec_y, 0) - forward_diff(elec_x, 1))
        elec_x = elec_x + courant * inv_perm * (backward_diff(magn_z, 1) - backward_diff(magn_y, 2))
        elec_y = elec_y + courant * inv_perm * (backward_diff(magn_x, 2) - backward_diff(magn_z, 0))
        elec_z = elec_z + courant * inv_perm * (backward_diff(magn_y, 0) - backward_diff(magn_x, 1))
    intersection = e_forward[0] * elec_x + e_forward[1] * elec_y + e_forward[2] * elec_z
    block_x = jnp.arange(N_GX, dtype=jnp.int32)[:, None, None, None]
    block_y = jnp.arange(N_GY, dtype=jnp.int32)[None, :, None, None]
    block_z = jnp.arange(N_GZ, dtype=jnp.int32)[None, None, :, None]
    cells = voxel_cell.astype(jnp.int32)
    glob_x = block_x * CX + cells // (CY * CZ)
    glob_y = block_y * CY + (cells // CZ) % CY
    glob_z = block_z * CZ + cells % CZ
    flat = ((glob_x * NY + glob_y) * NZ + glob_z).reshape(-1).astype(jnp.int32)
    terms = intersection.reshape(-1)[flat]
    owners = voxel_owner[..., 0].reshape(-1).astype(jnp.int32)
    params = owners * P_DEV + voxel_slot.reshape(-1).astype(jnp.int32)
    gradient = jax.ops.segment_sum(terms, params, num_segments=P_DEV * N_GX * N_GY * N_GZ)
    e_new = jnp.stack([elec_x, elec_y, elec_z])
    h_new = jnp.stack([magn_x, magn_y, magn_z])
    return (e_new, h_new, gradient)
```

```python
import jax
import jax.numpy as jnp
from jax import lax
from jax.sharding import PartitionSpec as P

STEPS = 2
P_DEV = 256


courant = 0.5


def extended(x, sides, width):
    for axis, dim in sides:
        peers, length = (lax.axis_size(axis), x.shape[dim])
        up = [(i, (i + 1) % peers) for i in range(peers - 1)]
        down = [(j, i) for i, j in up]
        last = lax.slice_in_dim(x, length - width, length, axis=dim)
        initial = lax.slice_in_dim(x, 0, width, axis=dim)
        before = lax.ppermute(last, axis, up)
        after = lax.ppermute(initial, axis, down)
        x = jnp.concatenate([before, x, after], axis=dim)
    return x


def inside(position, total, count, first, extent):
    coords = position * extent + first + jnp.arange(count, dtype=jnp.int32)
    return ((coords >= 0) & (coords < extent * total)).astype(jnp.float32)


def region_mask(counts, first, extents):
    along_x = inside(lax.axis_index("gx"), lax.axis_size("gx"), counts[0], first, extents[0])
    along_y = inside(lax.axis_index("gy"), lax.axis_size("gy"), counts[1], first, extents[1])
    along_z = inside(lax.axis_index("gz"), lax.axis_size("gz"), counts[2], first, extents[2])
    return along_x[:, None, None] * along_y[None, :, None] * along_z[None, None, :]


def leapfrog(fields, inv_region, first, extents):
    elec_x, elec_y, elec_z = (fields[0], fields[1], fields[2])
    magn_x, magn_y, magn_z = (fields[3], fields[4], fields[5])
    sizes = fields.shape[1:]
    core = (slice(0, -1), slice(0, -1), slice(0, -1))
    up_x = (slice(1, None), slice(0, -1), slice(0, -1))
    up_y = (slice(0, -1), slice(1, None), slice(0, -1))
    up_z = (slice(0, -1), slice(0, -1), slice(1, None))
    h_mask = region_mask((sizes[0] - 1, sizes[1] - 1, sizes[2] - 1), first, extents)
    new_hx = (
        magn_x[core] - courant * (elec_z[up_y] - elec_z[core] - (elec_y[up_z] - elec_y[core]))
    ) * h_mask
    new_hy = (
        magn_y[core] - courant * (elec_x[up_z] - elec_x[core] - (elec_z[up_x] - elec_z[core]))
    ) * h_mask
    new_hz = (
        magn_z[core] - courant * (elec_y[up_x] - elec_y[core] - (elec_x[up_y] - elec_x[core]))
    ) * h_mask
    here = (slice(1, None), slice(1, None), slice(1, None))
    low_x = (slice(0, -1), slice(1, None), slice(1, None))
    low_y = (slice(1, None), slice(0, -1), slice(1, None))
    low_z = (slice(1, None), slice(1, None), slice(0, -1))
    inner = (slice(1, -1), slice(1, -1), slice(1, -1))
    e_mask = region_mask((sizes[0] - 2, sizes[1] - 2, sizes[2] - 2), first + 1, extents)
    new_ex = (
        elec_x[inner]
        + courant * inv_region * (new_hz[here] - new_hz[low_y] - (new_hy[here] - new_hy[low_z]))
    ) * e_mask
    new_ey = (
        elec_y[inner]
        + courant * inv_region * (new_hx[here] - new_hx[low_z] - (new_hz[here] - new_hz[low_x]))
    ) * e_mask
    new_ez = (
        elec_z[inner]
        + courant * inv_region * (new_hy[here] - new_hy[low_x] - (new_hx[here] - new_hx[low_y]))
    ) * e_mask
    return jnp.stack([new_ex, new_ey, new_ez, new_hx[here], new_hy[here], new_hz[here]])


def body(e_forward, e_adjoint, h_adjoint, inv_perm, voxel_cell, voxel_owner, voxel_slot):
    extents = e_adjoint.shape[1:]
    fields = jnp.concatenate([e_adjoint, h_adjoint], axis=0)
    for repeat in range(STEPS):
        padded = extended(fields, (("gx", 1), ("gy", 2), ("gz", 3)), 1)
        fields = leapfrog(padded, inv_perm, -1, extents)
    intersection = e_forward[0] * fields[0] + e_forward[1] * fields[1] + e_forward[2] * fields[2]
    count = voxel_cell.shape[-1]
    voxel_rows = voxel_cell.reshape(count)
    owners = voxel_owner.reshape(count)
    slot_ids = voxel_slot.reshape(count)
    terms = intersection.reshape(-1)[voxel_rows]
    devices = lax.axis_size("gx") * lax.axis_size("gy") * lax.axis_size("gz")
    params = owners * P_DEV + slot_ids
    dense_terms = jax.ops.segment_sum(terms, params, num_segments=devices * P_DEV)
    per_owner = dense_terms.reshape(devices, P_DEV)
    received = lax.all_to_all(per_owner, ("gx", "gy", "gz"), 0, 0, tiled=True)
    gradient = received.sum(axis=0)
    return (fields[:3], fields[3:], gradient)


def solution(mesh):
    return jax.shard_map(
        body,
        mesh=mesh,
        in_specs=(
            P(None, "gx", "gy", "gz"),
            P(None, "gx", "gy", "gz"),
            P(None, "gx", "gy", "gz"),
            P("gx", "gy", "gz"),
            P("gx", "gy", "gz", None),
            P("gx", "gy", "gz", None, None),
            P("gx", "gy", "gz", None),
        ),
        out_specs=(P(None, "gx", "gy", "gz"), P(None, "gx", "gy", "gz"), P(("gx", "gy", "gz"))),
        check_vma=False,
    )
```

```python
import functools

import jax
import jax.numpy as jnp
from jax import lax
from jax.experimental import pallas as pl
from jax.experimental.pallas import tpu as pltpu
from jax.sharding import PartitionSpec as P

STEPS = 2
P_DEV = 256
CHUNK = 4

courant = 0.5


def toward_lower(x, axis):
    peers = lax.axis_size(axis)
    return lax.ppermute(x, axis, [(j, j - 1) for j in range(1, peers)])


def toward_upper(x, axis):
    peers = lax.axis_size(axis)
    return lax.ppermute(x, axis, [(j, j + 1) for j in range(peers - 1)])


def fwd_y(a, row):
    rolled = pltpu.roll(a, a.shape[1] - 1, 1)
    at = lax.broadcasted_iota(jnp.int32, a.shape, 1)
    return jnp.where(at == a.shape[1] - 1, row, rolled)


def fwd_z(a, col):
    rolled = pltpu.roll(a, a.shape[2] - 1, 2)
    at = lax.broadcasted_iota(jnp.int32, a.shape, 2)
    return jnp.where(at == a.shape[2] - 1, col, rolled)


def bwd_y(a, row):
    rolled = pltpu.roll(a, 1, 1)
    at = lax.broadcasted_iota(jnp.int32, a.shape, 1)
    return jnp.where(at == 0, row, rolled)


def bwd_z(a, col):
    rolled = pltpu.roll(a, 1, 2)
    at = lax.broadcasted_iota(jnp.int32, a.shape, 2)
    return jnp.where(at == 0, col, rolled)


def fwd_x(a, nxt):
    if a.shape[0] == 1:
        return nxt
    return jnp.concatenate([a[1:], nxt], axis=0)


def bwd_x(a, prv):
    if a.shape[0] == 1:
        return prv
    return jnp.concatenate([prv, a[:-1]], axis=0)


def h_kernel(e_ref, en_ref, h_ref, hx_ref, hy_ref, hz_ref, out_ref):
    last = pl.program_id(0) == pl.num_programs(0) - 1
    ex, ey, ez = e_ref[0], e_ref[1], e_ref[2]
    nxt_y = jnp.where(last, hx_ref[0], en_ref[1])
    nxt_z = jnp.where(last, hx_ref[1], en_ref[2])
    ez_yp = fwd_y(ez, hy_ref[1])
    ex_yp = fwd_y(ex, hy_ref[0])
    ey_zp = fwd_z(ey, hz_ref[1])
    ex_zp = fwd_z(ex, hz_ref[0])
    ez_xp = fwd_x(ez, nxt_z)
    ey_xp = fwd_x(ey, nxt_y)
    out_ref[0] = h_ref[0] - courant * ((ez_yp - ez) - (ey_zp - ey))
    out_ref[1] = h_ref[1] - courant * ((ex_zp - ex) - (ez_xp - ez))
    out_ref[2] = h_ref[2] - courant * ((ey_xp - ey) - (ex_yp - ex))


def e_update(e_ref, h_ref, hp_ref, inv_ref, hx_ref, hy_ref, hz_ref):
    first = pl.program_id(0) == 0
    hx, hy, hz = h_ref[0], h_ref[1], h_ref[2]
    prv_y = jnp.where(first, hx_ref[0], hp_ref[1])
    prv_z = jnp.where(first, hx_ref[1], hp_ref[2])
    hz_ym = bwd_y(hz, hy_ref[1])
    hx_ym = bwd_y(hx, hy_ref[0])
    hy_zm = bwd_z(hy, hz_ref[1])
    hx_zm = bwd_z(hx, hz_ref[0])
    hz_xm = bwd_x(hz, prv_z)
    hy_xm = bwd_x(hy, prv_y)
    scale = courant * inv_ref[...]
    new_x = e_ref[0] + scale * ((hz - hz_ym) - (hy - hy_zm))
    new_y = e_ref[1] + scale * ((hx - hx_zm) - (hz - hz_xm))
    new_z = e_ref[2] + scale * ((hy - hy_xm) - (hx - hx_ym))
    return new_x, new_y, new_z


def e_kernel(e_ref, h_ref, hp_ref, inv_ref, hx_ref, hy_ref, hz_ref, out_ref):
    new_x, new_y, new_z = e_update(e_ref, h_ref, hp_ref, inv_ref, hx_ref, hy_ref, hz_ref)
    out_ref[0] = new_x
    out_ref[1] = new_y
    out_ref[2] = new_z


def e_last_kernel(e_ref, h_ref, hp_ref, inv_ref, hx_ref, hy_ref, hz_ref, ef_ref, out_ref, inter_ref):
    new_x, new_y, new_z = e_update(e_ref, h_ref, hp_ref, inv_ref, hx_ref, hy_ref, hz_ref)
    out_ref[0] = new_x
    out_ref[1] = new_y
    out_ref[2] = new_z
    inter_ref[...] = ef_ref[0] * new_x + ef_ref[1] * new_y + ef_ref[2] * new_z


def field_spec(nx, ny, nz, chunk):
    return pl.BlockSpec((3, chunk, ny, nz), lambda i: (0, i, 0, 0))


def h_step(e, h):
    _, nx, ny, nz = e.shape
    chunk = CHUNK
    faces_x = toward_lower(e[1:3, 0], "gx")
    faces_y = toward_lower(e[0::2, :, 0:1, :], "gy")
    faces_z = toward_lower(e[0:2, :, :, 0:1], "gz")
    return pl.pallas_call(
        h_kernel,
        grid=(nx // chunk,),
        in_specs=[
            field_spec(nx, ny, nz, chunk),
            pl.BlockSpec((3, 1, ny, nz), lambda i: (0, jnp.minimum((i + 1) * chunk, nx - 1), 0, 0)),
            field_spec(nx, ny, nz, chunk),
            pl.BlockSpec((2, 1, ny, nz), lambda i: (0, 0, 0, 0)),
            pl.BlockSpec((2, chunk, 1, nz), lambda i: (0, i, 0, 0)),
            pl.BlockSpec((2, chunk, ny, 1), lambda i: (0, i, 0, 0)),
        ],
        out_specs=field_spec(nx, ny, nz, chunk),
        out_shape=jax.ShapeDtypeStruct(h.shape, h.dtype),
    )(e, e, h, faces_x[:, None], faces_y, faces_z)


def e_step(e, h, inv, ef=None):
    _, nx, ny, nz = e.shape
    chunk = CHUNK
    faces_x = toward_upper(h[1:3, nx - 1], "gx")
    faces_y = toward_upper(h[0::2, :, ny - 1:ny, :], "gy")
    faces_z = toward_upper(h[0:2, :, :, nz - 1:nz], "gz")
    in_specs = [
        field_spec(nx, ny, nz, chunk),
        field_spec(nx, ny, nz, chunk),
        pl.BlockSpec((3, 1, ny, nz), lambda i: (0, jnp.maximum(i * chunk - 1, 0), 0, 0)),
        pl.BlockSpec((chunk, ny, nz), lambda i: (i, 0, 0)),
        pl.BlockSpec((2, 1, ny, nz), lambda i: (0, 0, 0, 0)),
        pl.BlockSpec((2, chunk, 1, nz), lambda i: (0, i, 0, 0)),
        pl.BlockSpec((2, chunk, ny, 1), lambda i: (0, i, 0, 0)),
    ]
    args = [e, h, h, inv, faces_x[:, None], faces_y, faces_z]
    if ef is None:
        return pl.pallas_call(
            e_kernel,
            grid=(nx // chunk,),
            in_specs=in_specs,
            out_specs=field_spec(nx, ny, nz, chunk),
            out_shape=jax.ShapeDtypeStruct(e.shape, e.dtype),
        )(*args)
    return pl.pallas_call(
        e_last_kernel,
        grid=(nx // chunk,),
        in_specs=in_specs + [field_spec(nx, ny, nz, chunk)],
        out_specs=[field_spec(nx, ny, nz, chunk), pl.BlockSpec((chunk, ny, nz), lambda i: (i, 0, 0))],
        out_shape=[jax.ShapeDtypeStruct(e.shape, e.dtype), jax.ShapeDtypeStruct(e.shape[1:], e.dtype)],
    )(*args, ef)


def body(e_forward, e_adjoint, h_adjoint, inv_perm, voxel_cell, voxel_owner, voxel_slot):
    e, h = e_adjoint, h_adjoint
    intersection = None
    for repeat in range(STEPS):
        h = h_step(e, h)
        if repeat == STEPS - 1:
            e, intersection = e_step(e, h, inv_perm, e_forward)
        else:
            e = e_step(e, h, inv_perm)
    count = voxel_cell.shape[-1]
    voxel_rows = voxel_cell.reshape(count)
    owners = voxel_owner.reshape(count)
    slot_ids = voxel_slot.reshape(count)
    terms = intersection.reshape(-1)[voxel_rows]
    devices = lax.axis_size("gx") * lax.axis_size("gy") * lax.axis_size("gz")
    params = owners * P_DEV + slot_ids
    dense_terms = jax.ops.segment_sum(terms, params, num_segments=devices * P_DEV)
    per_owner = dense_terms.reshape(devices, P_DEV)
    received = lax.all_to_all(per_owner, ("gx", "gy", "gz"), 0, 0, tiled=True)
    gradient = received.sum(axis=0)
    return (e, h, gradient)


def solution(mesh):
    return jax.shard_map(
        body,
        mesh=mesh,
        in_specs=(
            P(None, "gx", "gy", "gz"),
            P(None, "gx", "gy", "gz"),
            P(None, "gx", "gy", "gz"),
            P("gx", "gy", "gz"),
            P("gx", "gy", "gz", None),
            P("gx", "gy", "gz", None, None),
            P("gx", "gy", "gz", None),
        ),
        out_specs=(P(None, "gx", "gy", "gz"), P(None, "gx", "gy", "gz"), P(("gx", "gy", "gz"))),
        check_vma=False,
    )
```

```python
import functools

import jax
import jax.numpy as jnp
from jax import lax
from jax.experimental import pallas as pl
from jax.experimental.pallas import tpu as pltpu
from jax.sharding import PartitionSpec as P

STEPS = 2
P_DEV = 256
CHUNK = 4

courant = 0.5


def toward_lower(x, axis):
    peers = lax.axis_size(axis)
    return lax.ppermute(x, axis, [(j, j - 1) for j in range(1, peers)])


def toward_upper(x, axis):
    peers = lax.axis_size(axis)
    return lax.ppermute(x, axis, [(j, j + 1) for j in range(peers - 1)])


def fwd_y(a, row):
    rolled = pltpu.roll(a, a.shape[1] - 1, 1)
    at = lax.broadcasted_iota(jnp.int32, a.shape, 1)
    return jnp.where(at == a.shape[1] - 1, row, rolled)


def fwd_z(a, col):
    rolled = pltpu.roll(a, a.shape[2] - 1, 2)
    at = lax.broadcasted_iota(jnp.int32, a.shape, 2)
    return jnp.where(at == a.shape[2] - 1, col, rolled)


def bwd_y(a, row):
    rolled = pltpu.roll(a, 1, 1)
    at = lax.broadcasted_iota(jnp.int32, a.shape, 1)
    return jnp.where(at == 0, row, rolled)


def bwd_z(a, col):
    rolled = pltpu.roll(a, 1, 2)
    at = lax.broadcasted_iota(jnp.int32, a.shape, 2)
    return jnp.where(at == 0, col, rolled)


def fwd_x(a, nxt):
    if a.shape[0] == 1:
        return nxt
    return jnp.concatenate([a[1:], nxt], axis=0)


def bwd_x(a, prv):
    if a.shape[0] == 1:
        return prv
    return jnp.concatenate([prv, a[:-1]], axis=0)


def h_kernel(e_ref, en_ref, h_ref, hx_ref, hy_ref, hz_ref, out_ref, fx_ref, fy_ref, fz_ref):
    last = pl.program_id(0) == pl.num_programs(0) - 1
    ex, ey, ez = e_ref[0], e_ref[1], e_ref[2]
    nxt_y = jnp.where(last, hx_ref[0], en_ref[1])
    nxt_z = jnp.where(last, hx_ref[1], en_ref[2])
    ez_yp = fwd_y(ez, hy_ref[1])
    ex_yp = fwd_y(ex, hy_ref[0])
    ey_zp = fwd_z(ey, hz_ref[1])
    ex_zp = fwd_z(ex, hz_ref[0])
    ez_xp = fwd_x(ez, nxt_z)
    ey_xp = fwd_x(ey, nxt_y)
    out_ref[0] = h_ref[0] - courant * ((ez_yp - ez) - (ey_zp - ey))
    out_ref[1] = h_ref[1] - courant * ((ex_zp - ex) - (ez_xp - ez))
    out_ref[2] = h_ref[2] - courant * ((ey_xp - ey) - (ex_yp - ex))
    b, ny, nz = ex.shape

    @pl.when(last)
    def _():
        fx_ref[0] = out_ref[1, b - 1:b]
        fx_ref[1] = out_ref[2, b - 1:b]

    fy_ref[0] = out_ref[0, :, ny - 1:ny, :]
    fy_ref[1] = out_ref[2, :, ny - 1:ny, :]
    fz_ref[0] = out_ref[0, :, :, nz - 1:nz]
    fz_ref[1] = out_ref[1, :, :, nz - 1:nz]


def e_update(e_ref, h_ref, hp_ref, inv_ref, hx_ref, hy_ref, hz_ref):
    first = pl.program_id(0) == 0
    hx, hy, hz = h_ref[0], h_ref[1], h_ref[2]
    prv_y = jnp.where(first, hx_ref[0], hp_ref[1])
    prv_z = jnp.where(first, hx_ref[1], hp_ref[2])
    hz_ym = bwd_y(hz, hy_ref[1])
    hx_ym = bwd_y(hx, hy_ref[0])
    hy_zm = bwd_z(hy, hz_ref[1])
    hx_zm = bwd_z(hx, hz_ref[0])
    hz_xm = bwd_x(hz, prv_z)
    hy_xm = bwd_x(hy, prv_y)
    scale = courant * inv_ref[...]
    new_x = e_ref[0] + scale * ((hz - hz_ym) - (hy - hy_zm))
    new_y = e_ref[1] + scale * ((hx - hx_zm) - (hz - hz_xm))
    new_z = e_ref[2] + scale * ((hy - hy_xm) - (hx - hx_ym))
    return new_x, new_y, new_z


def e_kernel(e_ref, h_ref, hp_ref, inv_ref, hx_ref, hy_ref, hz_ref, out_ref, fx_ref, fy_ref, fz_ref):
    new_x, new_y, new_z = e_update(e_ref, h_ref, hp_ref, inv_ref, hx_ref, hy_ref, hz_ref)
    out_ref[0] = new_x
    out_ref[1] = new_y
    out_ref[2] = new_z

    @pl.when(pl.program_id(0) == 0)
    def _():
        fx_ref[0] = out_ref[1, 0:1]
        fx_ref[1] = out_ref[2, 0:1]

    fy_ref[0] = out_ref[0, :, 0:1, :]
    fy_ref[1] = out_ref[2, :, 0:1, :]
    fz_ref[0] = out_ref[0, :, :, 0:1]
    fz_ref[1] = out_ref[1, :, :, 0:1]


def e_last_kernel(e_ref, h_ref, hp_ref, inv_ref, hx_ref, hy_ref, hz_ref, ef_ref, out_ref, inter_ref):
    new_x, new_y, new_z = e_update(e_ref, h_ref, hp_ref, inv_ref, hx_ref, hy_ref, hz_ref)
    out_ref[0] = new_x
    out_ref[1] = new_y
    out_ref[2] = new_z
    inter_ref[...] = ef_ref[0] * new_x + ef_ref[1] * new_y + ef_ref[2] * new_z


def field_spec(nx, ny, nz, chunk):
    return pl.BlockSpec((3, chunk, ny, nz), lambda i: (0, i, 0, 0))


def face_specs(nx, ny, nz, chunk):
    return [
        pl.BlockSpec((2, 1, ny, nz), lambda i: (0, 0, 0, 0)),
        pl.BlockSpec((2, chunk, 1, nz), lambda i: (0, i, 0, 0)),
        pl.BlockSpec((2, chunk, ny, 1), lambda i: (0, i, 0, 0)),
    ]


def face_shapes(nx, ny, nz, dtype):
    return [
        jax.ShapeDtypeStruct((2, 1, ny, nz), dtype),
        jax.ShapeDtypeStruct((2, nx, 1, nz), dtype),
        jax.ShapeDtypeStruct((2, nx, ny, 1), dtype),
    ]


def lower_faces_of(e):
    return e[1:3, 0:1], e[0::2, :, 0:1, :], e[0:2, :, :, 0:1]


def h_step(e, h, faces):
    _, nx, ny, nz = e.shape
    chunk = CHUNK
    faces_x = toward_lower(faces[0], "gx")
    faces_y = toward_lower(faces[1], "gy")
    faces_z = toward_lower(faces[2], "gz")
    return pl.pallas_call(
        h_kernel,
        grid=(nx // chunk,),
        in_specs=[
            field_spec(nx, ny, nz, chunk),
            pl.BlockSpec((3, 1, ny, nz), lambda i: (0, jnp.minimum((i + 1) * chunk, nx - 1), 0, 0)),
            field_spec(nx, ny, nz, chunk),
            pl.BlockSpec((2, 1, ny, nz), lambda i: (0, 0, 0, 0)),
            pl.BlockSpec((2, chunk, 1, nz), lambda i: (0, i, 0, 0)),
            pl.BlockSpec((2, chunk, ny, 1), lambda i: (0, i, 0, 0)),
        ],
        out_specs=[field_spec(nx, ny, nz, chunk)] + face_specs(nx, ny, nz, chunk),
        out_shape=[jax.ShapeDtypeStruct(h.shape, h.dtype)] + face_shapes(nx, ny, nz, h.dtype),
    )(e, e, h, faces_x, faces_y, faces_z)


def e_step(e, h, faces, inv, ef=None):
    _, nx, ny, nz = e.shape
    chunk = CHUNK
    faces_x = toward_upper(faces[0], "gx")
    faces_y = toward_upper(faces[1], "gy")
    faces_z = toward_upper(faces[2], "gz")
    in_specs = [
        field_spec(nx, ny, nz, chunk),
        field_spec(nx, ny, nz, chunk),
        pl.BlockSpec((3, 1, ny, nz), lambda i: (0, jnp.maximum(i * chunk - 1, 0), 0, 0)),
        pl.BlockSpec((chunk, ny, nz), lambda i: (i, 0, 0)),
        pl.BlockSpec((2, 1, ny, nz), lambda i: (0, 0, 0, 0)),
        pl.BlockSpec((2, chunk, 1, nz), lambda i: (0, i, 0, 0)),
        pl.BlockSpec((2, chunk, ny, 1), lambda i: (0, i, 0, 0)),
    ]
    args = [e, h, h, inv, faces_x, faces_y, faces_z]
    if ef is None:
        outs = pl.pallas_call(
            e_kernel,
            grid=(nx // chunk,),
            in_specs=in_specs,
            out_specs=[field_spec(nx, ny, nz, chunk)] + face_specs(nx, ny, nz, chunk),
            out_shape=[jax.ShapeDtypeStruct(e.shape, e.dtype)] + face_shapes(nx, ny, nz, e.dtype),
        )(*args)
        return outs[0], outs[1:]
    return pl.pallas_call(
        e_last_kernel,
        grid=(nx // chunk,),
        in_specs=in_specs + [field_spec(nx, ny, nz, chunk)],
        out_specs=[field_spec(nx, ny, nz, chunk), pl.BlockSpec((chunk, ny, nz), lambda i: (i, 0, 0))],
        out_shape=[jax.ShapeDtypeStruct(e.shape, e.dtype), jax.ShapeDtypeStruct(e.shape[1:], e.dtype)],
    )(*args, ef)


def body(e_forward, e_adjoint, h_adjoint, inv_perm, voxel_cell, voxel_owner, voxel_slot):
    e, h = e_adjoint, h_adjoint
    e_faces = lower_faces_of(e)
    intersection = None
    for repeat in range(STEPS):
        h, *h_faces = h_step(e, h, e_faces)
        if repeat == STEPS - 1:
            e, intersection = e_step(e, h, h_faces, inv_perm, e_forward)
        else:
            e, e_faces = e_step(e, h, h_faces, inv_perm)
    count = voxel_cell.shape[-1]
    voxel_rows = voxel_cell.reshape(count)
    owners = voxel_owner.reshape(count)
    slot_ids = voxel_slot.reshape(count)
    nx, ny, nz = intersection.shape
    rows = intersection.reshape(nx * ny, nz)[voxel_rows // nz]
    lanes = lax.broadcasted_iota(jnp.int32, rows.shape, 1)
    terms = jnp.sum(jnp.where(lanes == (voxel_rows % nz)[:, None], rows, 0.0), axis=1)
    devices = lax.axis_size("gx") * lax.axis_size("gy") * lax.axis_size("gz")
    owner_hot = (owners[:, None] == lax.broadcasted_iota(jnp.int32, (count, devices), 1)).astype(jnp.float32)
    slot_hot = jnp.where(slot_ids[:, None] == lax.broadcasted_iota(jnp.int32, (count, P_DEV), 1), terms[:, None], 0.0)
    per_owner = jnp.dot(owner_hot.T, slot_hot, precision=lax.Precision.HIGHEST, preferred_element_type=jnp.float32)
    received = lax.all_to_all(per_owner, ("gx", "gy", "gz"), 0, 0, tiled=True)
    gradient = received.sum(axis=0)
    return (e, h, gradient)


def solution(mesh):
    return jax.shard_map(
        body,
        mesh=mesh,
        in_specs=(
            P(None, "gx", "gy", "gz"),
            P(None, "gx", "gy", "gz"),
            P(None, "gx", "gy", "gz"),
            P("gx", "gy", "gz"),
            P("gx", "gy", "gz", None),
            P("gx", "gy", "gz", None, None),
            P("gx", "gy", "gz", None),
        ),
        out_specs=(P(None, "gx", "gy", "gz"), P(None, "gx", "gy", "gz"), P(("gx", "gy", "gz"))),
        check_vma=False,
    )
```

```python
import functools

import jax
import jax.numpy as jnp
from jax import lax
from jax.experimental import pallas as pl
from jax.experimental.pallas import tpu as pltpu
from jax.sharding import PartitionSpec as P

STEPS = 2
P_DEV = 256
CHUNK = 4

courant = 0.5


def toward_lower(x, axis):
    peers = lax.axis_size(axis)
    return lax.ppermute(x, axis, [(j, j - 1) for j in range(1, peers)])


def toward_upper(x, axis):
    peers = lax.axis_size(axis)
    return lax.ppermute(x, axis, [(j, j + 1) for j in range(peers - 1)])


def fwd_y(a, row):
    rolled = pltpu.roll(a, a.shape[1] - 1, 1)
    at = lax.broadcasted_iota(jnp.int32, a.shape, 1)
    return jnp.where(at == a.shape[1] - 1, row, rolled)


def fwd_z(a, col):
    rolled = pltpu.roll(a, a.shape[2] - 1, 2)
    at = lax.broadcasted_iota(jnp.int32, a.shape, 2)
    return jnp.where(at == a.shape[2] - 1, col, rolled)


def bwd_y(a, row):
    rolled = pltpu.roll(a, 1, 1)
    at = lax.broadcasted_iota(jnp.int32, a.shape, 1)
    return jnp.where(at == 0, row, rolled)


def bwd_z(a, col):
    rolled = pltpu.roll(a, 1, 2)
    at = lax.broadcasted_iota(jnp.int32, a.shape, 2)
    return jnp.where(at == 0, col, rolled)


def fwd_x(a, nxt):
    if a.shape[0] == 1:
        return nxt
    return jnp.concatenate([a[1:], nxt], axis=0)


def bwd_x(a, prv):
    if a.shape[0] == 1:
        return prv
    return jnp.concatenate([prv, a[:-1]], axis=0)


def h_kernel(e_ref, en_ref, h_ref, hx_ref, hy_ref, hz_ref, out_ref, fx_ref, fy_ref, fz_ref):
    last = pl.program_id(0) == pl.num_programs(0) - 1
    ex, ey, ez = e_ref[0], e_ref[1], e_ref[2]
    nxt_y = jnp.where(last, hx_ref[0], en_ref[1])
    nxt_z = jnp.where(last, hx_ref[1], en_ref[2])
    ez_yp = fwd_y(ez, hy_ref[1])
    ex_yp = fwd_y(ex, hy_ref[0])
    ey_zp = fwd_z(ey, hz_ref[1])
    ex_zp = fwd_z(ex, hz_ref[0])
    ez_xp = fwd_x(ez, nxt_z)
    ey_xp = fwd_x(ey, nxt_y)
    out_ref[0] = h_ref[0] - courant * ((ez_yp - ez) - (ey_zp - ey))
    out_ref[1] = h_ref[1] - courant * ((ex_zp - ex) - (ez_xp - ez))
    out_ref[2] = h_ref[2] - courant * ((ey_xp - ey) - (ex_yp - ex))
    b, ny, nz = ex.shape

    @pl.when(last)
    def _():
        fx_ref[0] = out_ref[1, b - 1:b]
        fx_ref[1] = out_ref[2, b - 1:b]

    fy_ref[0] = out_ref[0, :, ny - 1:ny, :]
    fy_ref[1] = out_ref[2, :, ny - 1:ny, :]
    fz_ref[0] = out_ref[0, :, :, nz - 1:nz]
    fz_ref[1] = out_ref[1, :, :, nz - 1:nz]


def e_update(e_ref, h_ref, hp_ref, inv_ref, hx_ref, hy_ref, hz_ref):
    first = pl.program_id(0) == 0
    hx, hy, hz = h_ref[0], h_ref[1], h_ref[2]
    prv_y = jnp.where(first, hx_ref[0], hp_ref[1])
    prv_z = jnp.where(first, hx_ref[1], hp_ref[2])
    hz_ym = bwd_y(hz, hy_ref[1])
    hx_ym = bwd_y(hx, hy_ref[0])
    hy_zm = bwd_z(hy, hz_ref[1])
    hx_zm = bwd_z(hx, hz_ref[0])
    hz_xm = bwd_x(hz, prv_z)
    hy_xm = bwd_x(hy, prv_y)
    scale = courant * inv_ref[...]
    new_x = e_ref[0] + scale * ((hz - hz_ym) - (hy - hy_zm))
    new_y = e_ref[1] + scale * ((hx - hx_zm) - (hz - hz_xm))
    new_z = e_ref[2] + scale * ((hy - hy_xm) - (hx - hx_ym))
    return new_x, new_y, new_z


def e_kernel(e_ref, h_ref, hp_ref, inv_ref, hx_ref, hy_ref, hz_ref, out_ref, fx_ref, fy_ref, fz_ref):
    new_x, new_y, new_z = e_update(e_ref, h_ref, hp_ref, inv_ref, hx_ref, hy_ref, hz_ref)
    out_ref[0] = new_x
    out_ref[1] = new_y
    out_ref[2] = new_z

    @pl.when(pl.program_id(0) == 0)
    def _():
        fx_ref[0] = out_ref[1, 0:1]
        fx_ref[1] = out_ref[2, 0:1]

    fy_ref[0] = out_ref[0, :, 0:1, :]
    fy_ref[1] = out_ref[2, :, 0:1, :]
    fz_ref[0] = out_ref[0, :, :, 0:1]
    fz_ref[1] = out_ref[1, :, :, 0:1]


def e_last_kernel(e_ref, h_ref, hp_ref, inv_ref, hx_ref, hy_ref, hz_ref, ef_ref, out_ref, inter_ref):
    new_x, new_y, new_z = e_update(e_ref, h_ref, hp_ref, inv_ref, hx_ref, hy_ref, hz_ref)
    out_ref[0] = new_x
    out_ref[1] = new_y
    out_ref[2] = new_z
    inter_ref[...] = ef_ref[0] * new_x + ef_ref[1] * new_y + ef_ref[2] * new_z


def field_spec(nx, ny, nz, chunk):
    return pl.BlockSpec((3, chunk, ny, nz), lambda i: (0, i, 0, 0))


def face_specs(nx, ny, nz, chunk):
    return [
        pl.BlockSpec((2, 1, ny, nz), lambda i: (0, 0, 0, 0)),
        pl.BlockSpec((2, chunk, 1, nz), lambda i: (0, i, 0, 0)),
        pl.BlockSpec((2, chunk, ny, 1), lambda i: (0, i, 0, 0)),
    ]


def face_shapes(nx, ny, nz, dtype):
    return [
        jax.ShapeDtypeStruct((2, 1, ny, nz), dtype),
        jax.ShapeDtypeStruct((2, nx, 1, nz), dtype),
        jax.ShapeDtypeStruct((2, nx, ny, 1), dtype),
    ]


def lower_faces_of(e):
    return e[1:3, 0:1], e[0::2, :, 0:1, :], e[0:2, :, :, 0:1]


def h_step(e, h, faces):
    _, nx, ny, nz = e.shape
    chunk = CHUNK
    faces_x = toward_lower(faces[0], "gx")
    faces_y = toward_lower(faces[1], "gy")
    faces_z = toward_lower(faces[2].reshape(2, nx * ny), "gz").reshape(2, nx, ny, 1)
    return pl.pallas_call(
        h_kernel,
        grid=(nx // chunk,),
        in_specs=[
            field_spec(nx, ny, nz, chunk),
            pl.BlockSpec((3, 1, ny, nz), lambda i: (0, jnp.minimum((i + 1) * chunk, nx - 1), 0, 0)),
            field_spec(nx, ny, nz, chunk),
            pl.BlockSpec((2, 1, ny, nz), lambda i: (0, 0, 0, 0)),
            pl.BlockSpec((2, chunk, 1, nz), lambda i: (0, i, 0, 0)),
            pl.BlockSpec((2, chunk, ny, 1), lambda i: (0, i, 0, 0)),
        ],
        out_specs=[field_spec(nx, ny, nz, chunk)] + face_specs(nx, ny, nz, chunk),
        out_shape=[jax.ShapeDtypeStruct(h.shape, h.dtype)] + face_shapes(nx, ny, nz, h.dtype),
    )(e, e, h, faces_x, faces_y, faces_z)


def e_step(e, h, faces, inv, ef=None):
    _, nx, ny, nz = e.shape
    chunk = CHUNK
    faces_x = toward_upper(faces[0], "gx")
    faces_y = toward_upper(faces[1], "gy")
    faces_z = toward_upper(faces[2].reshape(2, nx * ny), "gz").reshape(2, nx, ny, 1)
    in_specs = [
        field_spec(nx, ny, nz, chunk),
        field_spec(nx, ny, nz, chunk),
        pl.BlockSpec((3, 1, ny, nz), lambda i: (0, jnp.maximum(i * chunk - 1, 0), 0, 0)),
        pl.BlockSpec((chunk, ny, nz), lambda i: (i, 0, 0)),
        pl.BlockSpec((2, 1, ny, nz), lambda i: (0, 0, 0, 0)),
        pl.BlockSpec((2, chunk, 1, nz), lambda i: (0, i, 0, 0)),
        pl.BlockSpec((2, chunk, ny, 1), lambda i: (0, i, 0, 0)),
    ]
    args = [e, h, h, inv, faces_x, faces_y, faces_z]
    if ef is None:
        outs = pl.pallas_call(
            e_kernel,
            grid=(nx // chunk,),
            in_specs=in_specs,
            out_specs=[field_spec(nx, ny, nz, chunk)] + face_specs(nx, ny, nz, chunk),
            out_shape=[jax.ShapeDtypeStruct(e.shape, e.dtype)] + face_shapes(nx, ny, nz, e.dtype),
        )(*args)
        return outs[0], outs[1:]
    return pl.pallas_call(
        e_last_kernel,
        grid=(nx // chunk,),
        in_specs=in_specs + [field_spec(nx, ny, nz, chunk)],
        out_specs=[field_spec(nx, ny, nz, chunk), pl.BlockSpec((chunk, ny, nz), lambda i: (i, 0, 0))],
        out_shape=[jax.ShapeDtypeStruct(e.shape, e.dtype), jax.ShapeDtypeStruct(e.shape[1:], e.dtype)],
    )(*args, ef)


def body(e_forward, e_adjoint, h_adjoint, inv_perm, voxel_cell, voxel_owner, voxel_slot):
    e, h = e_adjoint, h_adjoint
    e_faces = lower_faces_of(e)
    intersection = None
    for repeat in range(STEPS):
        h, *h_faces = h_step(e, h, e_faces)
        if repeat == STEPS - 1:
            e, intersection = e_step(e, h, h_faces, inv_perm, e_forward)
        else:
            e, e_faces = e_step(e, h, h_faces, inv_perm)
    count = voxel_cell.shape[-1]
    voxel_rows = voxel_cell.reshape(count)
    owners = voxel_owner.reshape(count)
    slot_ids = voxel_slot.reshape(count)
    nx, ny, nz = intersection.shape
    rows = intersection.reshape(nx * ny, nz)[voxel_rows // nz]
    lanes = lax.broadcasted_iota(jnp.int32, rows.shape, 1)
    terms = jnp.sum(jnp.where(lanes == (voxel_rows % nz)[:, None], rows, 0.0), axis=1)
    devices = lax.axis_size("gx") * lax.axis_size("gy") * lax.axis_size("gz")
    owner_hot = (owners[:, None] == lax.broadcasted_iota(jnp.int32, (count, devices), 1)).astype(jnp.float32)
    slot_hot = jnp.where(slot_ids[:, None] == lax.broadcasted_iota(jnp.int32, (count, P_DEV), 1), terms[:, None], 0.0)
    per_owner = jnp.dot(owner_hot.T, slot_hot, precision=lax.Precision.HIGHEST, preferred_element_type=jnp.float32)
    received = lax.all_to_all(per_owner, ("gx", "gy", "gz"), 0, 0, tiled=True)
    gradient = received.sum(axis=0)
    return (e, h, gradient)


def solution(mesh):
    return jax.shard_map(
        body,
        mesh=mesh,
        in_specs=(
            P(None, "gx", "gy", "gz"),
            P(None, "gx", "gy", "gz"),
            P(None, "gx", "gy", "gz"),
            P("gx", "gy", "gz"),
            P("gx", "gy", "gz", None),
            P("gx", "gy", "gz", None, None),
            P("gx", "gy", "gz", None),
        ),
        out_specs=(P(None, "gx", "gy", "gz"), P(None, "gx", "gy", "gz"), P(("gx", "gy", "gz"))),
        check_vma=False,
    )
```

```python
import functools

import jax
import jax.numpy as jnp
from jax import lax
from jax.experimental import pallas as pl
from jax.experimental.pallas import tpu as pltpu
from jax.sharding import PartitionSpec as P

STEPS = 2
P_DEV = 256
CHUNK = 4

courant = 0.5


def toward_lower(x, axis):
    peers = lax.axis_size(axis)
    return lax.ppermute(x, axis, [(j, j - 1) for j in range(1, peers)])


def toward_upper(x, axis):
    peers = lax.axis_size(axis)
    return lax.ppermute(x, axis, [(j, j + 1) for j in range(peers - 1)])


def fwd_y(a, row):
    rolled = pltpu.roll(a, a.shape[1] - 1, 1)
    at = lax.broadcasted_iota(jnp.int32, a.shape, 1)
    return jnp.where(at == a.shape[1] - 1, row, rolled)


def fwd_z(a, col):
    rolled = pltpu.roll(a, a.shape[2] - 1, 2)
    at = lax.broadcasted_iota(jnp.int32, a.shape, 2)
    return jnp.where(at == a.shape[2] - 1, col, rolled)


def bwd_y(a, row):
    rolled = pltpu.roll(a, 1, 1)
    at = lax.broadcasted_iota(jnp.int32, a.shape, 1)
    return jnp.where(at == 0, row, rolled)


def bwd_z(a, col):
    rolled = pltpu.roll(a, 1, 2)
    at = lax.broadcasted_iota(jnp.int32, a.shape, 2)
    return jnp.where(at == 0, col, rolled)


def fwd_x(a, nxt):
    if a.shape[0] == 1:
        return nxt
    return jnp.concatenate([a[1:], nxt], axis=0)


def bwd_x(a, prv):
    if a.shape[0] == 1:
        return prv
    return jnp.concatenate([prv, a[:-1]], axis=0)


def h_kernel(e_ref, en_ref, h_ref, hx_ref, hy_ref, hz_ref, out_ref, fx_ref, fy_ref, fz_ref):
    last = pl.program_id(0) == pl.num_programs(0) - 1
    ex, ey, ez = e_ref[0], e_ref[1], e_ref[2]
    nxt_y = jnp.where(last, hx_ref[0], en_ref[1])
    nxt_z = jnp.where(last, hx_ref[1], en_ref[2])
    ez_yp = fwd_y(ez, hy_ref[1])
    ex_yp = fwd_y(ex, hy_ref[0])
    ey_zp = fwd_z(ey, hz_ref[1])
    ex_zp = fwd_z(ex, hz_ref[0])
    ez_xp = fwd_x(ez, nxt_z)
    ey_xp = fwd_x(ey, nxt_y)
    out_ref[0] = h_ref[0] - courant * ((ez_yp - ez) - (ey_zp - ey))
    out_ref[1] = h_ref[1] - courant * ((ex_zp - ex) - (ez_xp - ez))
    out_ref[2] = h_ref[2] - courant * ((ey_xp - ey) - (ex_yp - ex))
    b, ny, nz = ex.shape

    @pl.when(last)
    def _():
        fx_ref[0] = out_ref[1, b - 1:b]
        fx_ref[1] = out_ref[2, b - 1:b]

    fy_ref[0] = out_ref[0, :, ny - 1:ny, :]
    fy_ref[1] = out_ref[2, :, ny - 1:ny, :]
    fz_ref[0] = out_ref[0, :, :, nz - 1:nz]
    fz_ref[1] = out_ref[1, :, :, nz - 1:nz]


def e_update(e_ref, h_ref, hp_ref, inv_ref, hx_ref, hy_ref, hz_ref):
    first = pl.program_id(0) == 0
    hx, hy, hz = h_ref[0], h_ref[1], h_ref[2]
    prv_y = jnp.where(first, hx_ref[0], hp_ref[1])
    prv_z = jnp.where(first, hx_ref[1], hp_ref[2])
    hz_ym = bwd_y(hz, hy_ref[1])
    hx_ym = bwd_y(hx, hy_ref[0])
    hy_zm = bwd_z(hy, hz_ref[1])
    hx_zm = bwd_z(hx, hz_ref[0])
    hz_xm = bwd_x(hz, prv_z)
    hy_xm = bwd_x(hy, prv_y)
    scale = courant * inv_ref[...]
    new_x = e_ref[0] + scale * ((hz - hz_ym) - (hy - hy_zm))
    new_y = e_ref[1] + scale * ((hx - hx_zm) - (hz - hz_xm))
    new_z = e_ref[2] + scale * ((hy - hy_xm) - (hx - hx_ym))
    return new_x, new_y, new_z


def e_kernel(e_ref, h_ref, hp_ref, inv_ref, hx_ref, hy_ref, hz_ref, out_ref, fx_ref, fy_ref, fz_ref):
    new_x, new_y, new_z = e_update(e_ref, h_ref, hp_ref, inv_ref, hx_ref, hy_ref, hz_ref)
    out_ref[0] = new_x
    out_ref[1] = new_y
    out_ref[2] = new_z

    @pl.when(pl.program_id(0) == 0)
    def _():
        fx_ref[0] = out_ref[1, 0:1]
        fx_ref[1] = out_ref[2, 0:1]

    fy_ref[0] = out_ref[0, :, 0:1, :]
    fy_ref[1] = out_ref[2, :, 0:1, :]
    fz_ref[0] = out_ref[0, :, :, 0:1]
    fz_ref[1] = out_ref[1, :, :, 0:1]


def e_last_kernel(cell_ref, e_ref, h_ref, hp_ref, inv_ref, hx_ref, hy_ref, hz_ref, ef_ref, out_ref, picked_ref, inter_ref):
    new_x, new_y, new_z = e_update(e_ref, h_ref, hp_ref, inv_ref, hx_ref, hy_ref, hz_ref)
    out_ref[0] = new_x
    out_ref[1] = new_y
    out_ref[2] = new_z
    b = new_x.shape[0]
    step = pl.program_id(0)
    inter_ref[pl.ds(step * b, b)] = ef_ref[0] * new_x + ef_ref[1] * new_y + ef_ref[2] * new_z
    _, ny, nz = inter_ref.shape
    lanes = picked_ref.shape[1]

    @pl.when(step == pl.num_programs(0) - 1)
    def _():
        lane_at = lax.broadcasted_iota(jnp.int32, (8, lanes), 1)
        sub_at = lax.broadcasted_iota(jnp.int32, (8, lanes), 0)

        def pick(g, carry):
            group = jnp.zeros((8, lanes), jnp.float32)
            for j in range(8):
                c = cell_ref[g * 8 + j]
                x = c // (ny * nz)
                y = (c // nz) % ny
                z = c % nz
                rows = pl.multiple_of((y // 8) * 8, 8)
                start = pl.multiple_of((z // lanes) * lanes, lanes)
                tile = inter_ref[x, pl.ds(rows, 8), pl.ds(start, lanes)]
                hit = (sub_at == y % 8) & (lane_at == z % lanes)
                row = jnp.sum(jnp.where(hit, tile, 0.0), axis=0, keepdims=True)
                group = jnp.where(sub_at == j, row, group)
            picked_ref[pl.ds(pl.multiple_of(g * 8, 8), 8), :] = group
            return carry

        lax.fori_loop(0, picked_ref.shape[0] // 8, pick, 0)


def field_spec(nx, ny, nz, chunk):
    return pl.BlockSpec((3, chunk, ny, nz), lambda i: (0, i, 0, 0))


def face_specs(nx, ny, nz, chunk):
    return [
        pl.BlockSpec((2, 1, ny, nz), lambda i: (0, 0, 0, 0)),
        pl.BlockSpec((2, chunk, 1, nz), lambda i: (0, i, 0, 0)),
        pl.BlockSpec((2, chunk, ny, 1), lambda i: (0, i, 0, 0)),
    ]


def face_shapes(nx, ny, nz, dtype):
    return [
        jax.ShapeDtypeStruct((2, 1, ny, nz), dtype),
        jax.ShapeDtypeStruct((2, nx, 1, nz), dtype),
        jax.ShapeDtypeStruct((2, nx, ny, 1), dtype),
    ]


def lower_faces_of(e):
    return e[1:3, 0:1], e[0::2, :, 0:1, :], e[0:2, :, :, 0:1]


def h_step(e, h, faces):
    _, nx, ny, nz = e.shape
    chunk = CHUNK
    faces_x = toward_lower(faces[0], "gx")
    faces_y = toward_lower(faces[1], "gy")
    faces_z = toward_lower(faces[2].reshape(2, nx * ny), "gz").reshape(2, nx, ny, 1)
    return pl.pallas_call(
        h_kernel,
        grid=(nx // chunk,),
        in_specs=[
            field_spec(nx, ny, nz, chunk),
            pl.BlockSpec((3, 1, ny, nz), lambda i: (0, jnp.minimum((i + 1) * chunk, nx - 1), 0, 0)),
            field_spec(nx, ny, nz, chunk),
            pl.BlockSpec((2, 1, ny, nz), lambda i: (0, 0, 0, 0)),
            pl.BlockSpec((2, chunk, 1, nz), lambda i: (0, i, 0, 0)),
            pl.BlockSpec((2, chunk, ny, 1), lambda i: (0, i, 0, 0)),
        ],
        out_specs=[field_spec(nx, ny, nz, chunk)] + face_specs(nx, ny, nz, chunk),
        out_shape=[jax.ShapeDtypeStruct(h.shape, h.dtype)] + face_shapes(nx, ny, nz, h.dtype),
    )(e, e, h, faces_x, faces_y, faces_z)


def e_step(e, h, faces, inv, ef=None, cells=None):
    _, nx, ny, nz = e.shape
    chunk = CHUNK
    faces_x = toward_upper(faces[0], "gx")
    faces_y = toward_upper(faces[1], "gy")
    faces_z = toward_upper(faces[2].reshape(2, nx * ny), "gz").reshape(2, nx, ny, 1)
    in_specs = [
        field_spec(nx, ny, nz, chunk),
        field_spec(nx, ny, nz, chunk),
        pl.BlockSpec((3, 1, ny, nz), lambda i: (0, jnp.maximum(i * chunk - 1, 0), 0, 0)),
        pl.BlockSpec((chunk, ny, nz), lambda i: (i, 0, 0)),
        pl.BlockSpec((2, 1, ny, nz), lambda i: (0, 0, 0, 0)),
        pl.BlockSpec((2, chunk, 1, nz), lambda i: (0, i, 0, 0)),
        pl.BlockSpec((2, chunk, ny, 1), lambda i: (0, i, 0, 0)),
    ]
    args = [e, h, h, inv, faces_x, faces_y, faces_z]
    if ef is None:
        outs = pl.pallas_call(
            e_kernel,
            grid=(nx // chunk,),
            in_specs=in_specs,
            out_specs=[field_spec(nx, ny, nz, chunk)] + face_specs(nx, ny, nz, chunk),
            out_shape=[jax.ShapeDtypeStruct(e.shape, e.dtype)] + face_shapes(nx, ny, nz, e.dtype),
        )(*args)
        return outs[0], outs[1:]
    count = cells.shape[0]
    return pl.pallas_call(
        e_last_kernel,
        grid=(nx // chunk,),
        in_specs=[pl.BlockSpec(memory_space=pltpu.SMEM)] + in_specs + [field_spec(nx, ny, nz, chunk)],
        out_specs=[field_spec(nx, ny, nz, chunk), pl.BlockSpec((count, 128), lambda i: (0, 0))],
        out_shape=[jax.ShapeDtypeStruct(e.shape, e.dtype), jax.ShapeDtypeStruct((count, 128), e.dtype)],
        scratch_shapes=[pltpu.VMEM((nx, ny, nz), jnp.float32)],
    )(cells, *args, ef)


def body(e_forward, e_adjoint, h_adjoint, inv_perm, voxel_cell, voxel_owner, voxel_slot):
    count = voxel_cell.shape[-1]
    voxel_rows = voxel_cell.reshape(count)
    owners = voxel_owner.reshape(count)
    slot_ids = voxel_slot.reshape(count)
    e, h = e_adjoint, h_adjoint
    e_faces = lower_faces_of(e)
    picked = None
    for repeat in range(STEPS):
        h, *h_faces = h_step(e, h, e_faces)
        if repeat == STEPS - 1:
            e, picked = e_step(e, h, h_faces, inv_perm, e_forward, voxel_rows)
        else:
            e, e_faces = e_step(e, h, h_faces, inv_perm)
    terms = jnp.sum(picked, axis=1)
    devices = lax.axis_size("gx") * lax.axis_size("gy") * lax.axis_size("gz")
    owner_hot = (owners[:, None] == lax.broadcasted_iota(jnp.int32, (count, devices), 1)).astype(jnp.float32)
    slot_hot = jnp.where(slot_ids[:, None] == lax.broadcasted_iota(jnp.int32, (count, P_DEV), 1), terms[:, None], 0.0)
    per_owner = jnp.dot(owner_hot.T, slot_hot, precision=lax.Precision.HIGHEST, preferred_element_type=jnp.float32)
    received = lax.all_to_all(per_owner, ("gx", "gy", "gz"), 0, 0, tiled=True)
    gradient = received.sum(axis=0)
    return (e, h, gradient)


def solution(mesh):
    return jax.shard_map(
        body,
        mesh=mesh,
        in_specs=(
            P(None, "gx", "gy", "gz"),
            P(None, "gx", "gy", "gz"),
            P(None, "gx", "gy", "gz"),
            P("gx", "gy", "gz"),
            P("gx", "gy", "gz", None),
            P("gx", "gy", "gz", None, None),
            P("gx", "gy", "gz", None),
        ),
        out_specs=(P(None, "gx", "gy", "gz"), P(None, "gx", "gy", "gz"), P(("gx", "gy", "gz"))),
        check_vma=False,
    )
```

```python
import functools

import jax
import jax.numpy as jnp
from jax import lax
from jax.experimental import pallas as pl
from jax.experimental.pallas import tpu as pltpu
from jax.sharding import PartitionSpec as P

STEPS = 2
P_DEV = 256
CHUNK = 4

courant = 0.5


def toward_lower(x, axis):
    peers = lax.axis_size(axis)
    return lax.ppermute(x, axis, [(j, j - 1) for j in range(1, peers)])


def toward_upper(x, axis):
    peers = lax.axis_size(axis)
    return lax.ppermute(x, axis, [(j, j + 1) for j in range(peers - 1)])


def fwd_y(a, row):
    rolled = pltpu.roll(a, a.shape[1] - 1, 1)
    at = lax.broadcasted_iota(jnp.int32, a.shape, 1)
    return jnp.where(at == a.shape[1] - 1, row, rolled)


def fwd_z(a, col):
    rolled = pltpu.roll(a, a.shape[2] - 1, 2)
    at = lax.broadcasted_iota(jnp.int32, a.shape, 2)
    return jnp.where(at == a.shape[2] - 1, col, rolled)


def bwd_y(a, row):
    rolled = pltpu.roll(a, 1, 1)
    at = lax.broadcasted_iota(jnp.int32, a.shape, 1)
    return jnp.where(at == 0, row, rolled)


def bwd_z(a, col):
    rolled = pltpu.roll(a, 1, 2)
    at = lax.broadcasted_iota(jnp.int32, a.shape, 2)
    return jnp.where(at == 0, col, rolled)


def fwd_x(a, nxt):
    if a.shape[0] == 1:
        return nxt
    return jnp.concatenate([a[1:], nxt], axis=0)


def bwd_x(a, prv):
    if a.shape[0] == 1:
        return prv
    return jnp.concatenate([prv, a[:-1]], axis=0)


def h_kernel(e_ref, en_ref, h_ref, hx_ref, hy_ref, hz_ref, out_ref, fx_ref, fy_ref, fz_ref):
    last = pl.program_id(0) == pl.num_programs(0) - 1
    ex, ey, ez = e_ref[0], e_ref[1], e_ref[2]
    nxt_y = jnp.where(last, hx_ref[0], en_ref[1])
    nxt_z = jnp.where(last, hx_ref[1], en_ref[2])
    ez_yp = fwd_y(ez, hy_ref[1])
    ex_yp = fwd_y(ex, hy_ref[0])
    ey_zp = fwd_z(ey, hz_ref[1])
    ex_zp = fwd_z(ex, hz_ref[0])
    ez_xp = fwd_x(ez, nxt_z)
    ey_xp = fwd_x(ey, nxt_y)
    out_ref[0] = h_ref[0] - courant * ((ez_yp - ez) - (ey_zp - ey))
    out_ref[1] = h_ref[1] - courant * ((ex_zp - ex) - (ez_xp - ez))
    out_ref[2] = h_ref[2] - courant * ((ey_xp - ey) - (ex_yp - ex))
    b, ny, nz = ex.shape

    @pl.when(last)
    def _():
        fx_ref[0] = out_ref[1, b - 1:b]
        fx_ref[1] = out_ref[2, b - 1:b]

    fy_ref[0] = out_ref[0, :, ny - 1:ny, :]
    fy_ref[1] = out_ref[2, :, ny - 1:ny, :]
    fz_ref[0] = out_ref[0, :, :, nz - 1:nz]
    fz_ref[1] = out_ref[1, :, :, nz - 1:nz]


def e_update(e_ref, h_ref, hp_ref, inv_ref, hx_ref, hy_ref, hz_ref):
    first = pl.program_id(0) == 0
    hx, hy, hz = h_ref[0], h_ref[1], h_ref[2]
    prv_y = jnp.where(first, hx_ref[0], hp_ref[1])
    prv_z = jnp.where(first, hx_ref[1], hp_ref[2])
    hz_ym = bwd_y(hz, hy_ref[1])
    hx_ym = bwd_y(hx, hy_ref[0])
    hy_zm = bwd_z(hy, hz_ref[1])
    hx_zm = bwd_z(hx, hz_ref[0])
    hz_xm = bwd_x(hz, prv_z)
    hy_xm = bwd_x(hy, prv_y)
    scale = courant * inv_ref[...]
    new_x = e_ref[0] + scale * ((hz - hz_ym) - (hy - hy_zm))
    new_y = e_ref[1] + scale * ((hx - hx_zm) - (hz - hz_xm))
    new_z = e_ref[2] + scale * ((hy - hy_xm) - (hx - hx_ym))
    return new_x, new_y, new_z


def e_kernel(e_ref, h_ref, hp_ref, inv_ref, hx_ref, hy_ref, hz_ref, out_ref, fx_ref, fy_ref, fz_ref):
    new_x, new_y, new_z = e_update(e_ref, h_ref, hp_ref, inv_ref, hx_ref, hy_ref, hz_ref)
    out_ref[0] = new_x
    out_ref[1] = new_y
    out_ref[2] = new_z

    @pl.when(pl.program_id(0) == 0)
    def _():
        fx_ref[0] = out_ref[1, 0:1]
        fx_ref[1] = out_ref[2, 0:1]

    fy_ref[0] = out_ref[0, :, 0:1, :]
    fy_ref[1] = out_ref[2, :, 0:1, :]
    fz_ref[0] = out_ref[0, :, :, 0:1]
    fz_ref[1] = out_ref[1, :, :, 0:1]


def e_last_kernel(
    e_ref, h_ref, hp_ref, inv_ref, hx_ref, hy_ref, hz_ref, ef_ref, zrow_ref, rrow_ref, out_ref, terms_ref, zhot_ref
):
    new_x, new_y, new_z = e_update(e_ref, h_ref, hp_ref, inv_ref, hx_ref, hy_ref, hz_ref)
    out_ref[0] = new_x
    out_ref[1] = new_y
    out_ref[2] = new_z
    step = pl.program_id(0)
    b, ny, nz = new_x.shape
    count = zhot_ref.shape[1]

    @pl.when(step == 0)
    def _():
        zhot_ref[...] = (lax.broadcasted_iota(jnp.int32, (nz, count), 0) == zrow_ref[...]).astype(jnp.bfloat16)
        terms_ref[...] = jnp.zeros_like(terms_ref)

    inter = (ef_ref[0] * new_x + ef_ref[1] * new_y + ef_ref[2] * new_z).reshape(b * ny, nz)
    hi = inter.astype(jnp.bfloat16)
    rest = inter - hi.astype(jnp.float32)
    mid = rest.astype(jnp.bfloat16)
    lo = (rest - mid.astype(jnp.float32)).astype(jnp.bfloat16)
    zhot = zhot_ref[...]
    picked = (
        jnp.dot(hi, zhot, preferred_element_type=jnp.float32)
        + jnp.dot(mid, zhot, preferred_element_type=jnp.float32)
    ) + jnp.dot(lo, zhot, preferred_element_type=jnp.float32)
    row_at = step * (b * ny) + lax.broadcasted_iota(jnp.int32, picked.shape, 0)
    terms_ref[...] += jnp.sum(jnp.where(row_at == rrow_ref[...], picked, 0.0), axis=0, keepdims=True)


def field_spec(nx, ny, nz, chunk):
    return pl.BlockSpec((3, chunk, ny, nz), lambda i: (0, i, 0, 0))


def face_specs(nx, ny, nz, chunk):
    return [
        pl.BlockSpec((2, 1, ny, nz), lambda i: (0, 0, 0, 0)),
        pl.BlockSpec((2, chunk, 1, nz), lambda i: (0, i, 0, 0)),
        pl.BlockSpec((2, chunk, ny, 1), lambda i: (0, i, 0, 0)),
    ]


def face_shapes(nx, ny, nz, dtype):
    return [
        jax.ShapeDtypeStruct((2, 1, ny, nz), dtype),
        jax.ShapeDtypeStruct((2, nx, 1, nz), dtype),
        jax.ShapeDtypeStruct((2, nx, ny, 1), dtype),
    ]


def lower_faces_of(e):
    return e[1:3, 0:1], e[0::2, :, 0:1, :], e[0:2, :, :, 0:1]


def h_step(e, h, faces):
    _, nx, ny, nz = e.shape
    chunk = CHUNK
    faces_x = toward_lower(faces[0], "gx")
    faces_y = toward_lower(faces[1], "gy")
    faces_z = toward_lower(faces[2].reshape(2, nx * ny), "gz").reshape(2, nx, ny, 1)
    return pl.pallas_call(
        h_kernel,
        grid=(nx // chunk,),
        in_specs=[
            field_spec(nx, ny, nz, chunk),
            pl.BlockSpec((3, 1, ny, nz), lambda i: (0, jnp.minimum((i + 1) * chunk, nx - 1), 0, 0)),
            field_spec(nx, ny, nz, chunk),
            pl.BlockSpec((2, 1, ny, nz), lambda i: (0, 0, 0, 0)),
            pl.BlockSpec((2, chunk, 1, nz), lambda i: (0, i, 0, 0)),
            pl.BlockSpec((2, chunk, ny, 1), lambda i: (0, i, 0, 0)),
        ],
        out_specs=[field_spec(nx, ny, nz, chunk)] + face_specs(nx, ny, nz, chunk),
        out_shape=[jax.ShapeDtypeStruct(h.shape, h.dtype)] + face_shapes(nx, ny, nz, h.dtype),
    )(e, e, h, faces_x, faces_y, faces_z)


def e_step(e, h, faces, inv, ef=None, cells=None):
    _, nx, ny, nz = e.shape
    chunk = CHUNK
    faces_x = toward_upper(faces[0], "gx")
    faces_y = toward_upper(faces[1], "gy")
    faces_z = toward_upper(faces[2].reshape(2, nx * ny), "gz").reshape(2, nx, ny, 1)
    in_specs = [
        field_spec(nx, ny, nz, chunk),
        field_spec(nx, ny, nz, chunk),
        pl.BlockSpec((3, 1, ny, nz), lambda i: (0, jnp.maximum(i * chunk - 1, 0), 0, 0)),
        pl.BlockSpec((chunk, ny, nz), lambda i: (i, 0, 0)),
        pl.BlockSpec((2, 1, ny, nz), lambda i: (0, 0, 0, 0)),
        pl.BlockSpec((2, chunk, 1, nz), lambda i: (0, i, 0, 0)),
        pl.BlockSpec((2, chunk, ny, 1), lambda i: (0, i, 0, 0)),
    ]
    args = [e, h, h, inv, faces_x, faces_y, faces_z]
    if ef is None:
        outs = pl.pallas_call(
            e_kernel,
            grid=(nx // chunk,),
            in_specs=in_specs,
            out_specs=[field_spec(nx, ny, nz, chunk)] + face_specs(nx, ny, nz, chunk),
            out_shape=[jax.ShapeDtypeStruct(e.shape, e.dtype)] + face_shapes(nx, ny, nz, e.dtype),
        )(*args)
        return outs[0], outs[1:]
    count = cells.shape[0]
    zrow = (cells % nz).reshape(1, count)
    rrow = (cells // nz).reshape(1, count)
    return pl.pallas_call(
        e_last_kernel,
        grid=(nx // chunk,),
        in_specs=in_specs
        + [
            field_spec(nx, ny, nz, chunk),
            pl.BlockSpec((1, count), lambda i: (0, 0)),
            pl.BlockSpec((1, count), lambda i: (0, 0)),
        ],
        out_specs=[field_spec(nx, ny, nz, chunk), pl.BlockSpec((1, count), lambda i: (0, 0))],
        out_shape=[jax.ShapeDtypeStruct(e.shape, e.dtype), jax.ShapeDtypeStruct((1, count), jnp.float32)],
        scratch_shapes=[pltpu.VMEM((nz, count), jnp.bfloat16)],
    )(*args, ef, zrow, rrow)


def body(e_forward, e_adjoint, h_adjoint, inv_perm, voxel_cell, voxel_owner, voxel_slot):
    count = voxel_cell.shape[-1]
    voxel_rows = voxel_cell.reshape(count)
    owners = voxel_owner.reshape(count)
    slot_ids = voxel_slot.reshape(count)
    e, h = e_adjoint, h_adjoint
    e_faces = lower_faces_of(e)
    terms = None
    for repeat in range(STEPS):
        h, *h_faces = h_step(e, h, e_faces)
        if repeat == STEPS - 1:
            e, terms = e_step(e, h, h_faces, inv_perm, e_forward, voxel_rows)
        else:
            e, e_faces = e_step(e, h, h_faces, inv_perm)
    terms = terms.reshape(count)
    devices = lax.axis_size("gx") * lax.axis_size("gy") * lax.axis_size("gz")
    owner_hot = (owners[:, None] == lax.broadcasted_iota(jnp.int32, (count, devices), 1)).astype(jnp.float32)
    slot_hot = jnp.where(slot_ids[:, None] == lax.broadcasted_iota(jnp.int32, (count, P_DEV), 1), terms[:, None], 0.0)
    per_owner = jnp.dot(owner_hot.T, slot_hot, precision=lax.Precision.HIGHEST, preferred_element_type=jnp.float32)
    received = lax.all_to_all(per_owner, ("gx", "gy", "gz"), 0, 0, tiled=True)
    gradient = received.sum(axis=0)
    return (e, h, gradient)


def solution(mesh):
    return jax.shard_map(
        body,
        mesh=mesh,
        in_specs=(
            P(None, "gx", "gy", "gz"),
            P(None, "gx", "gy", "gz"),
            P(None, "gx", "gy", "gz"),
            P("gx", "gy", "gz"),
            P("gx", "gy", "gz", None),
            P("gx", "gy", "gz", None, None),
            P("gx", "gy", "gz", None),
        ),
        out_specs=(P(None, "gx", "gy", "gz"), P(None, "gx", "gy", "gz"), P(("gx", "gy", "gz"))),
        check_vma=False,
    )
```

```python
import functools

import jax
import jax.numpy as jnp
from jax import lax
from jax.experimental import pallas as pl
from jax.experimental.pallas import tpu as pltpu
from jax.sharding import PartitionSpec as P

STEPS = 2
P_DEV = 256
CHUNK = 8

courant = 0.5


def toward_lower(x, axis):
    peers = lax.axis_size(axis)
    return lax.ppermute(x, axis, [(j, j - 1) for j in range(1, peers)])


def toward_upper(x, axis):
    peers = lax.axis_size(axis)
    return lax.ppermute(x, axis, [(j, j + 1) for j in range(peers - 1)])


def fwd_y(a, row):
    rolled = pltpu.roll(a, a.shape[1] - 1, 1)
    at = lax.broadcasted_iota(jnp.int32, a.shape, 1)
    return jnp.where(at == a.shape[1] - 1, row, rolled)


def fwd_z(a, col):
    rolled = pltpu.roll(a, a.shape[2] - 1, 2)
    at = lax.broadcasted_iota(jnp.int32, a.shape, 2)
    return jnp.where(at == a.shape[2] - 1, col, rolled)


def bwd_y(a, row):
    rolled = pltpu.roll(a, 1, 1)
    at = lax.broadcasted_iota(jnp.int32, a.shape, 1)
    return jnp.where(at == 0, row, rolled)


def bwd_z(a, col):
    rolled = pltpu.roll(a, 1, 2)
    at = lax.broadcasted_iota(jnp.int32, a.shape, 2)
    return jnp.where(at == 0, col, rolled)


def fwd_x(a, nxt):
    if a.shape[0] == 1:
        return nxt
    return jnp.concatenate([a[1:], nxt], axis=0)


def bwd_x(a, prv):
    if a.shape[0] == 1:
        return prv
    return jnp.concatenate([prv, a[:-1]], axis=0)


def h_kernel(e_ref, en_ref, h_ref, hx_ref, hy_ref, hz_ref, out_ref, fx_ref, fy_ref, fz_ref):
    last = pl.program_id(0) == pl.num_programs(0) - 1
    ex, ey, ez = e_ref[0], e_ref[1], e_ref[2]
    nxt_y = jnp.where(last, hx_ref[0], en_ref[1])
    nxt_z = jnp.where(last, hx_ref[1], en_ref[2])
    ez_yp = fwd_y(ez, hy_ref[1])
    ex_yp = fwd_y(ex, hy_ref[0])
    ey_zp = fwd_z(ey, hz_ref[1])
    ex_zp = fwd_z(ex, hz_ref[0])
    ez_xp = fwd_x(ez, nxt_z)
    ey_xp = fwd_x(ey, nxt_y)
    out_ref[0] = h_ref[0] - courant * ((ez_yp - ez) - (ey_zp - ey))
    out_ref[1] = h_ref[1] - courant * ((ex_zp - ex) - (ez_xp - ez))
    out_ref[2] = h_ref[2] - courant * ((ey_xp - ey) - (ex_yp - ex))
    b, ny, nz = ex.shape

    @pl.when(last)
    def _():
        fx_ref[0] = out_ref[1, b - 1:b]
        fx_ref[1] = out_ref[2, b - 1:b]

    fy_ref[0] = out_ref[0, :, ny - 1:ny, :]
    fy_ref[1] = out_ref[2, :, ny - 1:ny, :]
    fz_ref[0] = out_ref[0, :, :, nz - 1:nz]
    fz_ref[1] = out_ref[1, :, :, nz - 1:nz]


def e_update(e_ref, h_ref, hp_ref, inv_ref, hx_ref, hy_ref, hz_ref):
    first = pl.program_id(0) == 0
    hx, hy, hz = h_ref[0], h_ref[1], h_ref[2]
    prv_y = jnp.where(first, hx_ref[0], hp_ref[1])
    prv_z = jnp.where(first, hx_ref[1], hp_ref[2])
    hz_ym = bwd_y(hz, hy_ref[1])
    hx_ym = bwd_y(hx, hy_ref[0])
    hy_zm = bwd_z(hy, hz_ref[1])
    hx_zm = bwd_z(hx, hz_ref[0])
    hz_xm = bwd_x(hz, prv_z)
    hy_xm = bwd_x(hy, prv_y)
    scale = courant * inv_ref[...]
    new_x = e_ref[0] + scale * ((hz - hz_ym) - (hy - hy_zm))
    new_y = e_ref[1] + scale * ((hx - hx_zm) - (hz - hz_xm))
    new_z = e_ref[2] + scale * ((hy - hy_xm) - (hx - hx_ym))
    return new_x, new_y, new_z


def e_kernel(e_ref, h_ref, hp_ref, inv_ref, hx_ref, hy_ref, hz_ref, out_ref, fx_ref, fy_ref, fz_ref):
    new_x, new_y, new_z = e_update(e_ref, h_ref, hp_ref, inv_ref, hx_ref, hy_ref, hz_ref)
    out_ref[0] = new_x
    out_ref[1] = new_y
    out_ref[2] = new_z

    @pl.when(pl.program_id(0) == 0)
    def _():
        fx_ref[0] = out_ref[1, 0:1]
        fx_ref[1] = out_ref[2, 0:1]

    fy_ref[0] = out_ref[0, :, 0:1, :]
    fy_ref[1] = out_ref[2, :, 0:1, :]
    fz_ref[0] = out_ref[0, :, :, 0:1]
    fz_ref[1] = out_ref[1, :, :, 0:1]


def e_last_kernel(
    e_ref, h_ref, hp_ref, inv_ref, hx_ref, hy_ref, hz_ref, ef_ref, zrow_ref, rrow_ref, out_ref, terms_ref, zhot_ref
):
    new_x, new_y, new_z = e_update(e_ref, h_ref, hp_ref, inv_ref, hx_ref, hy_ref, hz_ref)
    out_ref[0] = new_x
    out_ref[1] = new_y
    out_ref[2] = new_z
    step = pl.program_id(0)
    b, ny, nz = new_x.shape
    count = zhot_ref.shape[1]

    @pl.when(step == 0)
    def _():
        zhot_ref[...] = (lax.broadcasted_iota(jnp.int32, (nz, count), 0) == zrow_ref[...]).astype(jnp.bfloat16)
        terms_ref[...] = jnp.zeros_like(terms_ref)

    inter = (ef_ref[0] * new_x + ef_ref[1] * new_y + ef_ref[2] * new_z).reshape(b * ny, nz)
    hi = inter.astype(jnp.bfloat16)
    rest = inter - hi.astype(jnp.float32)
    mid = rest.astype(jnp.bfloat16)
    lo = (rest - mid.astype(jnp.float32)).astype(jnp.bfloat16)
    zhot = zhot_ref[...]
    picked = (
        jnp.dot(hi, zhot, preferred_element_type=jnp.float32)
        + jnp.dot(mid, zhot, preferred_element_type=jnp.float32)
    ) + jnp.dot(lo, zhot, preferred_element_type=jnp.float32)
    row_at = step * (b * ny) + lax.broadcasted_iota(jnp.int32, picked.shape, 0)
    terms_ref[...] += jnp.sum(jnp.where(row_at == rrow_ref[...], picked, 0.0), axis=0, keepdims=True)


def field_spec(nx, ny, nz, chunk):
    return pl.BlockSpec((3, chunk, ny, nz), lambda i: (0, i, 0, 0))


def face_specs(nx, ny, nz, chunk):
    return [
        pl.BlockSpec((2, 1, ny, nz), lambda i: (0, 0, 0, 0)),
        pl.BlockSpec((2, chunk, 1, nz), lambda i: (0, i, 0, 0)),
        pl.BlockSpec((2, chunk, ny, 1), lambda i: (0, i, 0, 0)),
    ]


def face_shapes(nx, ny, nz, dtype):
    return [
        jax.ShapeDtypeStruct((2, 1, ny, nz), dtype),
        jax.ShapeDtypeStruct((2, nx, 1, nz), dtype),
        jax.ShapeDtypeStruct((2, nx, ny, 1), dtype),
    ]


def lower_faces_of(e):
    return e[1:3, 0:1], e[0::2, :, 0:1, :], e[0:2, :, :, 0:1]


def h_step(e, h, faces):
    _, nx, ny, nz = e.shape
    chunk = CHUNK
    faces_x = toward_lower(faces[0], "gx")
    faces_y = toward_lower(faces[1], "gy")
    faces_z = toward_lower(faces[2].reshape(2, nx * ny), "gz").reshape(2, nx, ny, 1)
    return pl.pallas_call(
        h_kernel,
        grid=(nx // chunk,),
        in_specs=[
            field_spec(nx, ny, nz, chunk),
            pl.BlockSpec((3, 1, ny, nz), lambda i: (0, jnp.minimum((i + 1) * chunk, nx - 1), 0, 0)),
            field_spec(nx, ny, nz, chunk),
            pl.BlockSpec((2, 1, ny, nz), lambda i: (0, 0, 0, 0)),
            pl.BlockSpec((2, chunk, 1, nz), lambda i: (0, i, 0, 0)),
            pl.BlockSpec((2, chunk, ny, 1), lambda i: (0, i, 0, 0)),
        ],
        out_specs=[field_spec(nx, ny, nz, chunk)] + face_specs(nx, ny, nz, chunk),
        out_shape=[jax.ShapeDtypeStruct(h.shape, h.dtype)] + face_shapes(nx, ny, nz, h.dtype),
    )(e, e, h, faces_x, faces_y, faces_z)


def e_step(e, h, faces, inv, ef=None, cells=None):
    _, nx, ny, nz = e.shape
    chunk = CHUNK
    faces_x = toward_upper(faces[0], "gx")
    faces_y = toward_upper(faces[1], "gy")
    faces_z = toward_upper(faces[2].reshape(2, nx * ny), "gz").reshape(2, nx, ny, 1)
    in_specs = [
        field_spec(nx, ny, nz, chunk),
        field_spec(nx, ny, nz, chunk),
        pl.BlockSpec((3, 1, ny, nz), lambda i: (0, jnp.maximum(i * chunk - 1, 0), 0, 0)),
        pl.BlockSpec((chunk, ny, nz), lambda i: (i, 0, 0)),
        pl.BlockSpec((2, 1, ny, nz), lambda i: (0, 0, 0, 0)),
        pl.BlockSpec((2, chunk, 1, nz), lambda i: (0, i, 0, 0)),
        pl.BlockSpec((2, chunk, ny, 1), lambda i: (0, i, 0, 0)),
    ]
    args = [e, h, h, inv, faces_x, faces_y, faces_z]
    if ef is None:
        outs = pl.pallas_call(
            e_kernel,
            grid=(nx // chunk,),
            in_specs=in_specs,
            out_specs=[field_spec(nx, ny, nz, chunk)] + face_specs(nx, ny, nz, chunk),
            out_shape=[jax.ShapeDtypeStruct(e.shape, e.dtype)] + face_shapes(nx, ny, nz, e.dtype),
        )(*args)
        return outs[0], outs[1:]
    count = cells.shape[0]
    zrow = (cells % nz).reshape(1, count)
    rrow = (cells // nz).reshape(1, count)
    return pl.pallas_call(
        e_last_kernel,
        grid=(nx // chunk,),
        in_specs=in_specs
        + [
            field_spec(nx, ny, nz, chunk),
            pl.BlockSpec((1, count), lambda i: (0, 0)),
            pl.BlockSpec((1, count), lambda i: (0, 0)),
        ],
        out_specs=[field_spec(nx, ny, nz, chunk), pl.BlockSpec((1, count), lambda i: (0, 0))],
        out_shape=[jax.ShapeDtypeStruct(e.shape, e.dtype), jax.ShapeDtypeStruct((1, count), jnp.float32)],
        scratch_shapes=[pltpu.VMEM((nz, count), jnp.bfloat16)],
    )(*args, ef, zrow, rrow)


def body(e_forward, e_adjoint, h_adjoint, inv_perm, voxel_cell, voxel_owner, voxel_slot):
    count = voxel_cell.shape[-1]
    voxel_rows = voxel_cell.reshape(count)
    owners = voxel_owner.reshape(count)
    slot_ids = voxel_slot.reshape(count)
    e, h = e_adjoint, h_adjoint
    e_faces = lower_faces_of(e)
    terms = None
    for repeat in range(STEPS):
        h, *h_faces = h_step(e, h, e_faces)
        if repeat == STEPS - 1:
            e, terms = e_step(e, h, h_faces, inv_perm, e_forward, voxel_rows)
        else:
            e, e_faces = e_step(e, h, h_faces, inv_perm)
    terms = terms.reshape(count)
    devices = lax.axis_size("gx") * lax.axis_size("gy") * lax.axis_size("gz")
    owner_hot = (owners[:, None] == lax.broadcasted_iota(jnp.int32, (count, devices), 1)).astype(jnp.float32)
    slot_hot = jnp.where(slot_ids[:, None] == lax.broadcasted_iota(jnp.int32, (count, P_DEV), 1), terms[:, None], 0.0)
    per_owner = jnp.dot(owner_hot.T, slot_hot, precision=lax.Precision.HIGHEST, preferred_element_type=jnp.float32)
    received = lax.all_to_all(per_owner, ("gx", "gy", "gz"), 0, 0, tiled=True)
    gradient = received.sum(axis=0)
    return (e, h, gradient)


def solution(mesh):
    return jax.shard_map(
        body,
        mesh=mesh,
        in_specs=(
            P(None, "gx", "gy", "gz"),
            P(None, "gx", "gy", "gz"),
            P(None, "gx", "gy", "gz"),
            P("gx", "gy", "gz"),
            P("gx", "gy", "gz", None),
            P("gx", "gy", "gz", None, None),
            P("gx", "gy", "gz", None),
        ),
        out_specs=(P(None, "gx", "gy", "gz"), P(None, "gx", "gy", "gz"), P(("gx", "gy", "gz"))),
        check_vma=False,
    )
```

```python
import functools

import jax
import jax.numpy as jnp
from jax import lax
from jax.experimental import pallas as pl
from jax.experimental.pallas import tpu as pltpu
from jax.sharding import PartitionSpec as P

STEPS = 2
P_DEV = 256
CHUNK = 8

courant = 0.5


def toward_lower(x, axis):
    peers = lax.axis_size(axis)
    return lax.ppermute(x, axis, [(j, j - 1) for j in range(1, peers)])


def toward_upper(x, axis):
    peers = lax.axis_size(axis)
    return lax.ppermute(x, axis, [(j, j + 1) for j in range(peers - 1)])


def fwd_y(a, row):
    rolled = pltpu.roll(a, a.shape[1] - 1, 1)
    at = lax.broadcasted_iota(jnp.int32, a.shape, 1)
    return jnp.where(at == a.shape[1] - 1, row, rolled)


def fwd_z(a, col):
    rolled = pltpu.roll(a, a.shape[2] - 1, 2)
    at = lax.broadcasted_iota(jnp.int32, a.shape, 2)
    return jnp.where(at == a.shape[2] - 1, col, rolled)


def bwd_y(a, row):
    rolled = pltpu.roll(a, 1, 1)
    at = lax.broadcasted_iota(jnp.int32, a.shape, 1)
    return jnp.where(at == 0, row, rolled)


def bwd_z(a, col):
    rolled = pltpu.roll(a, 1, 2)
    at = lax.broadcasted_iota(jnp.int32, a.shape, 2)
    return jnp.where(at == 0, col, rolled)


def column_of(row, b, ny):
    tile = jnp.broadcast_to(row, (128, b * ny))
    return jnp.transpose(tile).reshape(b, ny, 128)[:, :, 0:1]


def row_of(a, lanes):
    b, ny, _ = a.shape
    tile = jnp.transpose(a[:, :, lanes].reshape(b * ny, 128))
    return tile


def fwd_x(a, nxt):
    if a.shape[0] == 1:
        return nxt
    return jnp.concatenate([a[1:], nxt], axis=0)


def bwd_x(a, prv):
    if a.shape[0] == 1:
        return prv
    return jnp.concatenate([prv, a[:-1]], axis=0)


def h_kernel(e_ref, en_ref, h_ref, hx_ref, hy_ref, hz_ref, out_ref, fx_ref, fy_ref, fz_ref):
    last = pl.program_id(0) == pl.num_programs(0) - 1
    ex, ey, ez = e_ref[0], e_ref[1], e_ref[2]
    nxt_y = jnp.where(last, hx_ref[0], en_ref[1])
    nxt_z = jnp.where(last, hx_ref[1], en_ref[2])
    ez_yp = fwd_y(ez, hy_ref[1])
    ex_yp = fwd_y(ex, hy_ref[0])
    b, ny, nz = ex.shape
    ey_zp = fwd_z(ey, column_of(hz_ref[1, 0], b, ny))
    ex_zp = fwd_z(ex, column_of(hz_ref[0, 0], b, ny))
    ez_xp = fwd_x(ez, nxt_z)
    ey_xp = fwd_x(ey, nxt_y)
    out_ref[0] = h_ref[0] - courant * ((ez_yp - ez) - (ey_zp - ey))
    out_ref[1] = h_ref[1] - courant * ((ex_zp - ex) - (ez_xp - ez))
    out_ref[2] = h_ref[2] - courant * ((ey_xp - ey) - (ex_yp - ex))

    @pl.when(last)
    def _():
        fx_ref[0] = out_ref[1, b - 1:b]
        fx_ref[1] = out_ref[2, b - 1:b]

    fy_ref[0] = out_ref[0, :, ny - 1:ny, :]
    fy_ref[1] = out_ref[2, :, ny - 1:ny, :]
    top = slice(nz - 128, nz)
    fz_ref[0, 0] = row_of(out_ref[0], top)[127:128]
    fz_ref[1, 0] = row_of(out_ref[1], top)[127:128]


def e_update(e_ref, h_ref, hp_ref, inv_ref, hx_ref, hy_ref, hz_ref):
    first = pl.program_id(0) == 0
    hx, hy, hz = h_ref[0], h_ref[1], h_ref[2]
    prv_y = jnp.where(first, hx_ref[0], hp_ref[1])
    prv_z = jnp.where(first, hx_ref[1], hp_ref[2])
    hz_ym = bwd_y(hz, hy_ref[1])
    hx_ym = bwd_y(hx, hy_ref[0])
    b, ny, nz = hx.shape
    hy_zm = bwd_z(hy, column_of(hz_ref[1, 0], b, ny))
    hx_zm = bwd_z(hx, column_of(hz_ref[0, 0], b, ny))
    hz_xm = bwd_x(hz, prv_z)
    hy_xm = bwd_x(hy, prv_y)
    scale = courant * inv_ref[...]
    new_x = e_ref[0] + scale * ((hz - hz_ym) - (hy - hy_zm))
    new_y = e_ref[1] + scale * ((hx - hx_zm) - (hz - hz_xm))
    new_z = e_ref[2] + scale * ((hy - hy_xm) - (hx - hx_ym))
    return new_x, new_y, new_z


def e_kernel(e_ref, h_ref, hp_ref, inv_ref, hx_ref, hy_ref, hz_ref, out_ref, fx_ref, fy_ref, fz_ref):
    new_x, new_y, new_z = e_update(e_ref, h_ref, hp_ref, inv_ref, hx_ref, hy_ref, hz_ref)
    out_ref[0] = new_x
    out_ref[1] = new_y
    out_ref[2] = new_z

    @pl.when(pl.program_id(0) == 0)
    def _():
        fx_ref[0] = out_ref[1, 0:1]
        fx_ref[1] = out_ref[2, 0:1]

    fy_ref[0] = out_ref[0, :, 0:1, :]
    fy_ref[1] = out_ref[2, :, 0:1, :]
    fz_ref[0, 0] = row_of(out_ref[0], slice(0, 128))[0:1]
    fz_ref[1, 0] = row_of(out_ref[1], slice(0, 128))[0:1]


def e_last_kernel(
    e_ref, h_ref, hp_ref, inv_ref, hx_ref, hy_ref, hz_ref, ef_ref, zrow_ref, rrow_ref, out_ref, terms_ref, zhot_ref
):
    new_x, new_y, new_z = e_update(e_ref, h_ref, hp_ref, inv_ref, hx_ref, hy_ref, hz_ref)
    out_ref[0] = new_x
    out_ref[1] = new_y
    out_ref[2] = new_z
    step = pl.program_id(0)
    b, ny, nz = new_x.shape
    count = zhot_ref.shape[1]

    @pl.when(step == 0)
    def _():
        zhot_ref[...] = (lax.broadcasted_iota(jnp.int32, (nz, count), 0) == zrow_ref[...]).astype(jnp.bfloat16)
        terms_ref[...] = jnp.zeros_like(terms_ref)

    inter = (ef_ref[0] * new_x + ef_ref[1] * new_y + ef_ref[2] * new_z).reshape(b * ny, nz)
    hi = inter.astype(jnp.bfloat16)
    rest = inter - hi.astype(jnp.float32)
    mid = rest.astype(jnp.bfloat16)
    lo = (rest - mid.astype(jnp.float32)).astype(jnp.bfloat16)
    zhot = zhot_ref[...]
    picked = (
        jnp.dot(hi, zhot, preferred_element_type=jnp.float32)
        + jnp.dot(mid, zhot, preferred_element_type=jnp.float32)
    ) + jnp.dot(lo, zhot, preferred_element_type=jnp.float32)
    row_at = step * (b * ny) + lax.broadcasted_iota(jnp.int32, picked.shape, 0)
    terms_ref[...] += jnp.sum(jnp.where(row_at == rrow_ref[...], picked, 0.0), axis=0, keepdims=True)


def field_spec(nx, ny, nz, chunk):
    return pl.BlockSpec((3, chunk, ny, nz), lambda i: (0, i, 0, 0))


def face_specs(nx, ny, nz, chunk):
    return [
        pl.BlockSpec((2, 1, ny, nz), lambda i: (0, 0, 0, 0)),
        pl.BlockSpec((2, chunk, 1, nz), lambda i: (0, i, 0, 0)),
        pl.BlockSpec((2, 1, 1, chunk * ny), lambda i: (0, i, 0, 0)),
    ]


def face_shapes(nx, ny, nz, dtype):
    return [
        jax.ShapeDtypeStruct((2, 1, ny, nz), dtype),
        jax.ShapeDtypeStruct((2, nx, 1, nz), dtype),
        jax.ShapeDtypeStruct((2, nx // CHUNK, 1, CHUNK * ny), dtype),
    ]


def lower_faces_of(e):
    _, nx, ny, _ = e.shape
    return e[1:3, 0:1], e[0::2, :, 0:1, :], e[0:2, :, :, 0].reshape(2, nx // CHUNK, 1, CHUNK * ny)


def h_step(e, h, faces):
    _, nx, ny, nz = e.shape
    chunk = CHUNK
    faces_x = toward_lower(faces[0], "gx")
    faces_y = toward_lower(faces[1], "gy")
    faces_z = toward_lower(faces[2], "gz")
    return pl.pallas_call(
        h_kernel,
        grid=(nx // chunk,),
        in_specs=[
            field_spec(nx, ny, nz, chunk),
            pl.BlockSpec((3, 1, ny, nz), lambda i: (0, jnp.minimum((i + 1) * chunk, nx - 1), 0, 0)),
            field_spec(nx, ny, nz, chunk),
            pl.BlockSpec((2, 1, ny, nz), lambda i: (0, 0, 0, 0)),
            pl.BlockSpec((2, chunk, 1, nz), lambda i: (0, i, 0, 0)),
            pl.BlockSpec((2, 1, 1, chunk * ny), lambda i: (0, i, 0, 0)),
        ],
        out_specs=[field_spec(nx, ny, nz, chunk)] + face_specs(nx, ny, nz, chunk),
        out_shape=[jax.ShapeDtypeStruct(h.shape, h.dtype)] + face_shapes(nx, ny, nz, h.dtype),
    )(e, e, h, faces_x, faces_y, faces_z)


def e_step(e, h, faces, inv, ef=None, cells=None):
    _, nx, ny, nz = e.shape
    chunk = CHUNK
    faces_x = toward_upper(faces[0], "gx")
    faces_y = toward_upper(faces[1], "gy")
    faces_z = toward_upper(faces[2], "gz")
    in_specs = [
        field_spec(nx, ny, nz, chunk),
        field_spec(nx, ny, nz, chunk),
        pl.BlockSpec((3, 1, ny, nz), lambda i: (0, jnp.maximum(i * chunk - 1, 0), 0, 0)),
        pl.BlockSpec((chunk, ny, nz), lambda i: (i, 0, 0)),
        pl.BlockSpec((2, 1, ny, nz), lambda i: (0, 0, 0, 0)),
        pl.BlockSpec((2, chunk, 1, nz), lambda i: (0, i, 0, 0)),
        pl.BlockSpec((2, 1, 1, chunk * ny), lambda i: (0, i, 0, 0)),
    ]
    args = [e, h, h, inv, faces_x, faces_y, faces_z]
    if ef is None:
        outs = pl.pallas_call(
            e_kernel,
            grid=(nx // chunk,),
            in_specs=in_specs,
            out_specs=[field_spec(nx, ny, nz, chunk)] + face_specs(nx, ny, nz, chunk),
            out_shape=[jax.ShapeDtypeStruct(e.shape, e.dtype)] + face_shapes(nx, ny, nz, e.dtype),
        )(*args)
        return outs[0], outs[1:]
    count = cells.shape[0]
    zrow = (cells % nz).reshape(1, count)
    rrow = (cells // nz).reshape(1, count)
    return pl.pallas_call(
        e_last_kernel,
        grid=(nx // chunk,),
        in_specs=in_specs
        + [
            field_spec(nx, ny, nz, chunk),
            pl.BlockSpec((1, count), lambda i: (0, 0)),
            pl.BlockSpec((1, count), lambda i: (0, 0)),
        ],
        out_specs=[field_spec(nx, ny, nz, chunk), pl.BlockSpec((1, count), lambda i: (0, 0))],
        out_shape=[jax.ShapeDtypeStruct(e.shape, e.dtype), jax.ShapeDtypeStruct((1, count), jnp.float32)],
        scratch_shapes=[pltpu.VMEM((nz, count), jnp.bfloat16)],
    )(*args, ef, zrow, rrow)


def body(e_forward, e_adjoint, h_adjoint, inv_perm, voxel_cell, voxel_owner, voxel_slot):
    count = voxel_cell.shape[-1]
    voxel_rows = voxel_cell.reshape(count)
    owners = voxel_owner.reshape(count)
    slot_ids = voxel_slot.reshape(count)
    e, h = e_adjoint, h_adjoint
    e_faces = lower_faces_of(e)
    terms = None
    for repeat in range(STEPS):
        h, *h_faces = h_step(e, h, e_faces)
        if repeat == STEPS - 1:
            e, terms = e_step(e, h, h_faces, inv_perm, e_forward, voxel_rows)
        else:
            e, e_faces = e_step(e, h, h_faces, inv_perm)
    terms = terms.reshape(count)
    devices = lax.axis_size("gx") * lax.axis_size("gy") * lax.axis_size("gz")
    owner_hot = (owners[:, None] == lax.broadcasted_iota(jnp.int32, (count, devices), 1)).astype(jnp.float32)
    slot_hot = jnp.where(slot_ids[:, None] == lax.broadcasted_iota(jnp.int32, (count, P_DEV), 1), terms[:, None], 0.0)
    per_owner = jnp.dot(owner_hot.T, slot_hot, precision=lax.Precision.HIGHEST, preferred_element_type=jnp.float32)
    received = lax.all_to_all(per_owner, ("gx", "gy", "gz"), 0, 0, tiled=True)
    gradient = received.sum(axis=0)
    return (e, h, gradient)


def solution(mesh):
    return jax.shard_map(
        body,
        mesh=mesh,
        in_specs=(
            P(None, "gx", "gy", "gz"),
            P(None, "gx", "gy", "gz"),
            P(None, "gx", "gy", "gz"),
            P("gx", "gy", "gz"),
            P("gx", "gy", "gz", None),
            P("gx", "gy", "gz", None, None),
            P("gx", "gy", "gz", None),
        ),
        out_specs=(P(None, "gx", "gy", "gz"), P(None, "gx", "gy", "gz"), P(("gx", "gy", "gz"))),
        check_vma=False,
    )
```

```python
import functools

import jax
import jax.numpy as jnp
from jax import lax
from jax.experimental import pallas as pl
from jax.experimental.pallas import tpu as pltpu
from jax.sharding import PartitionSpec as P

STEPS = 2
P_DEV = 256
CHUNK = 8

courant = 0.5


def toward_lower(x, axis):
    peers = lax.axis_size(axis)
    return lax.ppermute(x, axis, [(j, j - 1) for j in range(1, peers)])


def toward_upper(x, axis):
    peers = lax.axis_size(axis)
    return lax.ppermute(x, axis, [(j, j + 1) for j in range(peers - 1)])


def fwd_y(a, row):
    rolled = pltpu.roll(a, a.shape[1] - 1, 1)
    at = lax.broadcasted_iota(jnp.int32, a.shape, 1)
    return jnp.where(at == a.shape[1] - 1, row, rolled)


def fwd_z(a, col):
    rolled = pltpu.roll(a, a.shape[2] - 1, 2)
    at = lax.broadcasted_iota(jnp.int32, a.shape, 2)
    return jnp.where(at == a.shape[2] - 1, col, rolled)


def bwd_y(a, row):
    rolled = pltpu.roll(a, 1, 1)
    at = lax.broadcasted_iota(jnp.int32, a.shape, 1)
    return jnp.where(at == 0, row, rolled)


def bwd_z(a, col):
    rolled = pltpu.roll(a, 1, 2)
    at = lax.broadcasted_iota(jnp.int32, a.shape, 2)
    return jnp.where(at == 0, col, rolled)


def column_of(row, b, ny):
    tile = jnp.broadcast_to(row, (128, b * ny))
    return jnp.transpose(tile).reshape(b, ny, 128)[:, :, 0:1]


def row_of(a, lanes):
    b, ny, _ = a.shape
    tile = jnp.transpose(a[:, :, lanes].reshape(b * ny, 128))
    return tile


def fwd_x(a, nxt):
    if a.shape[0] == 1:
        return nxt
    return jnp.concatenate([a[1:], nxt], axis=0)


def bwd_x(a, prv):
    if a.shape[0] == 1:
        return prv
    return jnp.concatenate([prv, a[:-1]], axis=0)


def h_kernel(e_ref, en_ref, h_ref, hx_ref, hy_ref, hz_ref, out_ref, fx_ref, fy_ref, fz_ref):
    last = pl.program_id(0) == pl.num_programs(0) - 1
    ex, ey, ez = e_ref[0], e_ref[1], e_ref[2]
    nxt_y = jnp.where(last, hx_ref[0], en_ref[1])
    nxt_z = jnp.where(last, hx_ref[1], en_ref[2])
    ez_yp = fwd_y(ez, hy_ref[1])
    ex_yp = fwd_y(ex, hy_ref[0])
    b, ny, nz = ex.shape
    ey_zp = fwd_z(ey, column_of(hz_ref[1, 0], b, ny))
    ex_zp = fwd_z(ex, column_of(hz_ref[0, 0], b, ny))
    ez_xp = fwd_x(ez, nxt_z)
    ey_xp = fwd_x(ey, nxt_y)
    out_ref[0] = h_ref[0] - courant * ((ez_yp - ez) - (ey_zp - ey))
    out_ref[1] = h_ref[1] - courant * ((ex_zp - ex) - (ez_xp - ez))
    out_ref[2] = h_ref[2] - courant * ((ey_xp - ey) - (ex_yp - ex))

    @pl.when(last)
    def _():
        fx_ref[0] = out_ref[1, b - 1:b]
        fx_ref[1] = out_ref[2, b - 1:b]

    fy_ref[0] = out_ref[0, :, ny - 1:ny, :]
    fy_ref[1] = out_ref[2, :, ny - 1:ny, :]
    top = slice(nz - 128, nz)
    fz_ref[0, 0] = row_of(out_ref[0], top)[127:128]
    fz_ref[1, 0] = row_of(out_ref[1], top)[127:128]


def e_update(e_ref, h_ref, hp_ref, inv_ref, hx_ref, hy_ref, hz_ref):
    first = pl.program_id(0) == 0
    hx, hy, hz = h_ref[0], h_ref[1], h_ref[2]
    prv_y = jnp.where(first, hx_ref[0], hp_ref[1])
    prv_z = jnp.where(first, hx_ref[1], hp_ref[2])
    hz_ym = bwd_y(hz, hy_ref[1])
    hx_ym = bwd_y(hx, hy_ref[0])
    b, ny, nz = hx.shape
    hy_zm = bwd_z(hy, column_of(hz_ref[1, 0], b, ny))
    hx_zm = bwd_z(hx, column_of(hz_ref[0, 0], b, ny))
    hz_xm = bwd_x(hz, prv_z)
    hy_xm = bwd_x(hy, prv_y)
    scale = courant * inv_ref[...]
    new_x = e_ref[0] + scale * ((hz - hz_ym) - (hy - hy_zm))
    new_y = e_ref[1] + scale * ((hx - hx_zm) - (hz - hz_xm))
    new_z = e_ref[2] + scale * ((hy - hy_xm) - (hx - hx_ym))
    return new_x, new_y, new_z


def e_kernel(e_ref, h_ref, hp_ref, inv_ref, hx_ref, hy_ref, hz_ref, out_ref, fx_ref, fy_ref, fz_ref):
    new_x, new_y, new_z = e_update(e_ref, h_ref, hp_ref, inv_ref, hx_ref, hy_ref, hz_ref)
    out_ref[0] = new_x
    out_ref[1] = new_y
    out_ref[2] = new_z

    @pl.when(pl.program_id(0) == 0)
    def _():
        fx_ref[0] = out_ref[1, 0:1]
        fx_ref[1] = out_ref[2, 0:1]

    fy_ref[0] = out_ref[0, :, 0:1, :]
    fy_ref[1] = out_ref[2, :, 0:1, :]
    fz_ref[0, 0] = row_of(out_ref[0], slice(0, 128))[0:1]
    fz_ref[1, 0] = row_of(out_ref[1], slice(0, 128))[0:1]


def e_last_kernel(
    e_ref, h_ref, hp_ref, inv_ref, hx_ref, hy_ref, hz_ref, ef_ref, zrow_ref, rrow_ref, out_ref, terms_ref, zhot_ref
):
    new_x, new_y, new_z = e_update(e_ref, h_ref, hp_ref, inv_ref, hx_ref, hy_ref, hz_ref)
    out_ref[0] = new_x
    out_ref[1] = new_y
    out_ref[2] = new_z
    step = pl.program_id(0)
    b, ny, nz = new_x.shape
    count = zhot_ref.shape[1]

    @pl.when(step == 0)
    def _():
        zhot_ref[...] = (lax.broadcasted_iota(jnp.int32, (nz, count), 0) == zrow_ref[...]).astype(jnp.bfloat16)
        terms_ref[...] = jnp.zeros_like(terms_ref)

    inter = (ef_ref[0] * new_x + ef_ref[1] * new_y + ef_ref[2] * new_z).reshape(b * ny, nz)
    hi = inter.astype(jnp.bfloat16)
    rest = inter - hi.astype(jnp.float32)
    mid = rest.astype(jnp.bfloat16)
    lo = (rest - mid.astype(jnp.float32)).astype(jnp.bfloat16)
    zhot = zhot_ref[...]
    picked = (
        jnp.dot(hi, zhot, preferred_element_type=jnp.float32)
        + jnp.dot(mid, zhot, preferred_element_type=jnp.float32)
    ) + jnp.dot(lo, zhot, preferred_element_type=jnp.float32)
    row_at = step * (b * ny) + lax.broadcasted_iota(jnp.int32, picked.shape, 0)
    terms_ref[...] += jnp.sum(jnp.where(row_at == rrow_ref[...], picked, 0.0), axis=0, keepdims=True)


def field_spec(nx, ny, nz, chunk):
    return pl.BlockSpec((3, chunk, ny, nz), lambda i: (0, i, 0, 0))


def face_specs(nx, ny, nz, chunk):
    return [
        pl.BlockSpec((2, 1, ny, nz), lambda i: (0, 0, 0, 0)),
        pl.BlockSpec((2, chunk, 1, nz), lambda i: (0, i, 0, 0)),
        pl.BlockSpec((2, 1, 1, chunk * ny), lambda i: (0, i, 0, 0)),
    ]


def face_shapes(nx, ny, nz, dtype):
    return [
        jax.ShapeDtypeStruct((2, 1, ny, nz), dtype),
        jax.ShapeDtypeStruct((2, nx, 1, nz), dtype),
        jax.ShapeDtypeStruct((2, nx // CHUNK, 1, CHUNK * ny), dtype),
    ]


def faces_kernel(slab_ref, rows_ref, lanes_ref, fx_ref, fy_ref, fz_ref):
    fx_ref[0] = slab_ref[1]
    fx_ref[1] = slab_ref[2]
    fy_ref[0] = rows_ref[0, :, 0:1, :]
    fy_ref[1] = rows_ref[2, :, 0:1, :]
    nx = lanes_ref.shape[1]
    for i in range(nx // CHUNK):
        part = slice(i * CHUNK, (i + 1) * CHUNK)
        fz_ref[0, i] = row_of(lanes_ref[0, part], slice(0, 128))[0:1]
        fz_ref[1, i] = row_of(lanes_ref[1, part], slice(0, 128))[0:1]


def lower_faces_of(e):
    _, nx, ny, nz = e.shape
    return pl.pallas_call(
        faces_kernel,
        grid=(1,),
        in_specs=[
            pl.BlockSpec((3, 1, ny, nz), lambda i: (0, 0, 0, 0)),
            pl.BlockSpec((3, nx, 8, nz), lambda i: (0, 0, 0, 0)),
            pl.BlockSpec((3, nx, ny, 128), lambda i: (0, 0, 0, 0)),
        ],
        out_specs=[
            pl.BlockSpec((2, 1, ny, nz), lambda i: (0, 0, 0, 0)),
            pl.BlockSpec((2, nx, 1, nz), lambda i: (0, 0, 0, 0)),
            pl.BlockSpec((2, nx // CHUNK, 1, CHUNK * ny), lambda i: (0, 0, 0, 0)),
        ],
        out_shape=face_shapes(nx, ny, nz, e.dtype),
    )(e, e, e)


def h_step(e, h, faces):
    _, nx, ny, nz = e.shape
    chunk = CHUNK
    faces_x = toward_lower(faces[0], "gx")
    faces_y = toward_lower(faces[1], "gy")
    faces_z = toward_lower(faces[2], "gz")
    return pl.pallas_call(
        h_kernel,
        grid=(nx // chunk,),
        in_specs=[
            field_spec(nx, ny, nz, chunk),
            pl.BlockSpec((3, 1, ny, nz), lambda i: (0, jnp.minimum((i + 1) * chunk, nx - 1), 0, 0)),
            field_spec(nx, ny, nz, chunk),
            pl.BlockSpec((2, 1, ny, nz), lambda i: (0, 0, 0, 0)),
            pl.BlockSpec((2, chunk, 1, nz), lambda i: (0, i, 0, 0)),
            pl.BlockSpec((2, 1, 1, chunk * ny), lambda i: (0, i, 0, 0)),
        ],
        out_specs=[field_spec(nx, ny, nz, chunk)] + face_specs(nx, ny, nz, chunk),
        out_shape=[jax.ShapeDtypeStruct(h.shape, h.dtype)] + face_shapes(nx, ny, nz, h.dtype),
    )(e, e, h, faces_x, faces_y, faces_z)


def e_step(e, h, faces, inv, ef=None, cells=None):
    _, nx, ny, nz = e.shape
    chunk = CHUNK
    faces_x = toward_upper(faces[0], "gx")
    faces_y = toward_upper(faces[1], "gy")
    faces_z = toward_upper(faces[2], "gz")
    in_specs = [
        field_spec(nx, ny, nz, chunk),
        field_spec(nx, ny, nz, chunk),
        pl.BlockSpec((3, 1, ny, nz), lambda i: (0, jnp.maximum(i * chunk - 1, 0), 0, 0)),
        pl.BlockSpec((chunk, ny, nz), lambda i: (i, 0, 0)),
        pl.BlockSpec((2, 1, ny, nz), lambda i: (0, 0, 0, 0)),
        pl.BlockSpec((2, chunk, 1, nz), lambda i: (0, i, 0, 0)),
        pl.BlockSpec((2, 1, 1, chunk * ny), lambda i: (0, i, 0, 0)),
    ]
    args = [e, h, h, inv, faces_x, faces_y, faces_z]
    if ef is None:
        outs = pl.pallas_call(
            e_kernel,
            grid=(nx // chunk,),
            in_specs=in_specs,
            out_specs=[field_spec(nx, ny, nz, chunk)] + face_specs(nx, ny, nz, chunk),
            out_shape=[jax.ShapeDtypeStruct(e.shape, e.dtype)] + face_shapes(nx, ny, nz, e.dtype),
        )(*args)
        return outs[0], outs[1:]
    count = cells.shape[0]
    zrow = (cells % nz).reshape(1, count)
    rrow = (cells // nz).reshape(1, count)
    return pl.pallas_call(
        e_last_kernel,
        grid=(nx // chunk,),
        in_specs=in_specs
        + [
            field_spec(nx, ny, nz, chunk),
            pl.BlockSpec((1, count), lambda i: (0, 0)),
            pl.BlockSpec((1, count), lambda i: (0, 0)),
        ],
        out_specs=[field_spec(nx, ny, nz, chunk), pl.BlockSpec((1, count), lambda i: (0, 0))],
        out_shape=[jax.ShapeDtypeStruct(e.shape, e.dtype), jax.ShapeDtypeStruct((1, count), jnp.float32)],
        scratch_shapes=[pltpu.VMEM((nz, count), jnp.bfloat16)],
    )(*args, ef, zrow, rrow)


def body(e_forward, e_adjoint, h_adjoint, inv_perm, voxel_cell, voxel_owner, voxel_slot):
    count = voxel_cell.shape[-1]
    voxel_rows = voxel_cell.reshape(count)
    owners = voxel_owner.reshape(count)
    slot_ids = voxel_slot.reshape(count)
    e, h = e_adjoint, h_adjoint
    e_faces = lower_faces_of(e)
    terms = None
    for repeat in range(STEPS):
        h, *h_faces = h_step(e, h, e_faces)
        if repeat == STEPS - 1:
            e, terms = e_step(e, h, h_faces, inv_perm, e_forward, voxel_rows)
        else:
            e, e_faces = e_step(e, h, h_faces, inv_perm)
    terms = terms.reshape(count)
    devices = lax.axis_size("gx") * lax.axis_size("gy") * lax.axis_size("gz")
    owner_hot = (owners[:, None] == lax.broadcasted_iota(jnp.int32, (count, devices), 1)).astype(jnp.float32)
    slot_hot = jnp.where(slot_ids[:, None] == lax.broadcasted_iota(jnp.int32, (count, P_DEV), 1), terms[:, None], 0.0)
    per_owner = jnp.dot(owner_hot.T, slot_hot, precision=lax.Precision.HIGHEST, preferred_element_type=jnp.float32)
    received = lax.all_to_all(per_owner, ("gx", "gy", "gz"), 0, 0, tiled=True)
    gradient = received.sum(axis=0)
    return (e, h, gradient)


def solution(mesh):
    return jax.shard_map(
        body,
        mesh=mesh,
        in_specs=(
            P(None, "gx", "gy", "gz"),
            P(None, "gx", "gy", "gz"),
            P(None, "gx", "gy", "gz"),
            P("gx", "gy", "gz"),
            P("gx", "gy", "gz", None),
            P("gx", "gy", "gz", None, None),
            P("gx", "gy", "gz", None),
        ),
        out_specs=(P(None, "gx", "gy", "gz"), P(None, "gx", "gy", "gz"), P(("gx", "gy", "gz"))),
        check_vma=False,
    )
```

```python
import functools

import jax
import jax.numpy as jnp
from jax import lax
from jax.experimental import pallas as pl
from jax.experimental.pallas import tpu as pltpu
from jax.sharding import PartitionSpec as P

STEPS = 2
P_DEV = 256
CHUNK = 8

courant = 0.5


def toward_lower(x, axis):
    peers = lax.axis_size(axis)
    return lax.ppermute(x, axis, [(j, j - 1) for j in range(1, peers)])


def toward_upper(x, axis):
    peers = lax.axis_size(axis)
    return lax.ppermute(x, axis, [(j, j + 1) for j in range(peers - 1)])


def fwd_y(a, row):
    rolled = pltpu.roll(a, a.shape[-2] - 1, a.ndim - 2)
    at = lax.broadcasted_iota(jnp.int32, a.shape, a.ndim - 2)
    return jnp.where(at == a.shape[-2] - 1, row, rolled)


def fwd_z(a, col):
    rolled = pltpu.roll(a, a.shape[-1] - 1, a.ndim - 1)
    at = lax.broadcasted_iota(jnp.int32, a.shape, a.ndim - 1)
    return jnp.where(at == a.shape[-1] - 1, col, rolled)


def bwd_y(a, row):
    rolled = pltpu.roll(a, 1, a.ndim - 2)
    at = lax.broadcasted_iota(jnp.int32, a.shape, a.ndim - 2)
    return jnp.where(at == 0, row, rolled)


def bwd_z(a, col):
    rolled = pltpu.roll(a, 1, a.ndim - 1)
    at = lax.broadcasted_iota(jnp.int32, a.shape, a.ndim - 1)
    return jnp.where(at == 0, col, rolled)


def column_of(row, b, ny):
    tile = jnp.broadcast_to(row, (128, b * ny))
    return jnp.transpose(tile).reshape(b, ny, 128)[:, :, 0:1]


def row_of(a, lanes):
    b, ny, _ = a.shape
    tile = jnp.transpose(a[:, :, lanes].reshape(b * ny, 128))
    return tile


def fwd_x(a, nxt):
    if a.shape[0] == 1:
        return nxt
    return jnp.concatenate([a[1:], nxt], axis=0)


def bwd_x(a, prv):
    if a.shape[0] == 1:
        return prv
    return jnp.concatenate([prv, a[:-1]], axis=0)


def h_kernel(e_ref, en_ref, h_ref, hx_ref, hy_ref, hz_ref, out_ref, fx_ref, fy_ref, fz_ref):
    last = pl.program_id(0) == pl.num_programs(0) - 1
    _, b, ny, nz = e_ref.shape
    nxt_y = jnp.where(last, hx_ref[0], en_ref[1])
    nxt_z = jnp.where(last, hx_ref[1], en_ref[2])
    col_x = column_of(hz_ref[0, 0], b, ny)
    col_y = column_of(hz_ref[1, 0], b, ny)
    for j in range(b):
        ex, ey, ez = e_ref[0, j], e_ref[1, j], e_ref[2, j]
        ey_xp = e_ref[1, j + 1] if j + 1 < b else nxt_y[0]
        ez_xp = e_ref[2, j + 1] if j + 1 < b else nxt_z[0]
        ez_yp = fwd_y(ez, hy_ref[1, j])
        ex_yp = fwd_y(ex, hy_ref[0, j])
        ey_zp = fwd_z(ey, col_y[j])
        ex_zp = fwd_z(ex, col_x[j])
        out_ref[0, j] = h_ref[0, j] - courant * ((ez_yp - ez) - (ey_zp - ey))
        out_ref[1, j] = h_ref[1, j] - courant * ((ex_zp - ex) - (ez_xp - ez))
        out_ref[2, j] = h_ref[2, j] - courant * ((ey_xp - ey) - (ex_yp - ex))

    @pl.when(last)
    def _():
        fx_ref[0] = out_ref[1, b - 1:b]
        fx_ref[1] = out_ref[2, b - 1:b]

    fy_ref[0] = out_ref[0, :, ny - 1:ny, :]
    fy_ref[1] = out_ref[2, :, ny - 1:ny, :]
    top = slice(nz - 128, nz)
    fz_ref[0, 0] = row_of(out_ref[0], top)[127:128]
    fz_ref[1, 0] = row_of(out_ref[1], top)[127:128]


def e_slabs(e_ref, h_ref, hp_ref, inv_ref, hx_ref, hy_ref, hz_ref, out_ref):
    first = pl.program_id(0) == 0
    _, b, ny, nz = h_ref.shape
    prv_y = jnp.where(first, hx_ref[0], hp_ref[1])
    prv_z = jnp.where(first, hx_ref[1], hp_ref[2])
    col_x = column_of(hz_ref[0, 0], b, ny)
    col_y = column_of(hz_ref[1, 0], b, ny)
    for j in range(b):
        hx, hy, hz = h_ref[0, j], h_ref[1, j], h_ref[2, j]
        hz_xm = h_ref[2, j - 1] if j > 0 else prv_z[0]
        hy_xm = h_ref[1, j - 1] if j > 0 else prv_y[0]
        hz_ym = bwd_y(hz, hy_ref[1, j])
        hx_ym = bwd_y(hx, hy_ref[0, j])
        hy_zm = bwd_z(hy, col_y[j])
        hx_zm = bwd_z(hx, col_x[j])
        scale = courant * inv_ref[j]
        out_ref[0, j] = e_ref[0, j] + scale * ((hz - hz_ym) - (hy - hy_zm))
        out_ref[1, j] = e_ref[1, j] + scale * ((hx - hx_zm) - (hz - hz_xm))
        out_ref[2, j] = e_ref[2, j] + scale * ((hy - hy_xm) - (hx - hx_ym))


def e_kernel(e_ref, h_ref, hp_ref, inv_ref, hx_ref, hy_ref, hz_ref, out_ref, fx_ref, fy_ref, fz_ref):
    e_slabs(e_ref, h_ref, hp_ref, inv_ref, hx_ref, hy_ref, hz_ref, out_ref)

    @pl.when(pl.program_id(0) == 0)
    def _():
        fx_ref[0] = out_ref[1, 0:1]
        fx_ref[1] = out_ref[2, 0:1]

    fy_ref[0] = out_ref[0, :, 0:1, :]
    fy_ref[1] = out_ref[2, :, 0:1, :]
    fz_ref[0, 0] = row_of(out_ref[0], slice(0, 128))[0:1]
    fz_ref[1, 0] = row_of(out_ref[1], slice(0, 128))[0:1]


def e_last_kernel(
    e_ref, h_ref, hp_ref, inv_ref, hx_ref, hy_ref, hz_ref, ef_ref, zrow_ref, rrow_ref, out_ref, terms_ref, zhot_ref
):
    e_slabs(e_ref, h_ref, hp_ref, inv_ref, hx_ref, hy_ref, hz_ref, out_ref)
    new_x, new_y, new_z = out_ref[0], out_ref[1], out_ref[2]
    step = pl.program_id(0)
    b, ny, nz = new_x.shape
    count = zhot_ref.shape[1]

    @pl.when(step == 0)
    def _():
        zhot_ref[...] = (lax.broadcasted_iota(jnp.int32, (nz, count), 0) == zrow_ref[...]).astype(jnp.bfloat16)
        terms_ref[...] = jnp.zeros_like(terms_ref)

    inter = (ef_ref[0] * new_x + ef_ref[1] * new_y + ef_ref[2] * new_z).reshape(b * ny, nz)
    hi = inter.astype(jnp.bfloat16)
    rest = inter - hi.astype(jnp.float32)
    mid = rest.astype(jnp.bfloat16)
    lo = (rest - mid.astype(jnp.float32)).astype(jnp.bfloat16)
    zhot = zhot_ref[...]
    picked = (
        jnp.dot(hi, zhot, preferred_element_type=jnp.float32)
        + jnp.dot(mid, zhot, preferred_element_type=jnp.float32)
    ) + jnp.dot(lo, zhot, preferred_element_type=jnp.float32)
    row_at = step * (b * ny) + lax.broadcasted_iota(jnp.int32, picked.shape, 0)
    terms_ref[...] += jnp.sum(jnp.where(row_at == rrow_ref[...], picked, 0.0), axis=0, keepdims=True)


def field_spec(nx, ny, nz, chunk):
    return pl.BlockSpec((3, chunk, ny, nz), lambda i: (0, i, 0, 0))


def face_specs(nx, ny, nz, chunk):
    return [
        pl.BlockSpec((2, 1, ny, nz), lambda i: (0, 0, 0, 0)),
        pl.BlockSpec((2, chunk, 1, nz), lambda i: (0, i, 0, 0)),
        pl.BlockSpec((2, 1, 1, chunk * ny), lambda i: (0, i, 0, 0)),
    ]


def face_shapes(nx, ny, nz, dtype):
    return [
        jax.ShapeDtypeStruct((2, 1, ny, nz), dtype),
        jax.ShapeDtypeStruct((2, nx, 1, nz), dtype),
        jax.ShapeDtypeStruct((2, nx // CHUNK, 1, CHUNK * ny), dtype),
    ]


def faces_kernel(slab_ref, rows_ref, lanes_ref, fx_ref, fy_ref, fz_ref):
    fx_ref[0] = slab_ref[1]
    fx_ref[1] = slab_ref[2]
    fy_ref[0] = rows_ref[0, :, 0:1, :]
    fy_ref[1] = rows_ref[2, :, 0:1, :]
    nx = lanes_ref.shape[1]
    for i in range(nx // CHUNK):
        part = slice(i * CHUNK, (i + 1) * CHUNK)
        fz_ref[0, i] = row_of(lanes_ref[0, part], slice(0, 128))[0:1]
        fz_ref[1, i] = row_of(lanes_ref[1, part], slice(0, 128))[0:1]


def lower_faces_of(e):
    _, nx, ny, nz = e.shape
    return pl.pallas_call(
        faces_kernel,
        grid=(1,),
        in_specs=[
            pl.BlockSpec((3, 1, ny, nz), lambda i: (0, 0, 0, 0)),
            pl.BlockSpec((3, nx, 8, nz), lambda i: (0, 0, 0, 0)),
            pl.BlockSpec((3, nx, ny, 128), lambda i: (0, 0, 0, 0)),
        ],
        out_specs=[
            pl.BlockSpec((2, 1, ny, nz), lambda i: (0, 0, 0, 0)),
            pl.BlockSpec((2, nx, 1, nz), lambda i: (0, 0, 0, 0)),
            pl.BlockSpec((2, nx // CHUNK, 1, CHUNK * ny), lambda i: (0, 0, 0, 0)),
        ],
        out_shape=face_shapes(nx, ny, nz, e.dtype),
    )(e, e, e)


def h_step(e, h, faces):
    _, nx, ny, nz = e.shape
    chunk = CHUNK
    faces_x = toward_lower(faces[0], "gx")
    faces_y = toward_lower(faces[1], "gy")
    faces_z = toward_lower(faces[2], "gz")
    return pl.pallas_call(
        h_kernel,
        grid=(nx // chunk,),
        in_specs=[
            field_spec(nx, ny, nz, chunk),
            pl.BlockSpec((3, 1, ny, nz), lambda i: (0, jnp.minimum((i + 1) * chunk, nx - 1), 0, 0)),
            field_spec(nx, ny, nz, chunk),
            pl.BlockSpec((2, 1, ny, nz), lambda i: (0, 0, 0, 0)),
            pl.BlockSpec((2, chunk, 1, nz), lambda i: (0, i, 0, 0)),
            pl.BlockSpec((2, 1, 1, chunk * ny), lambda i: (0, i, 0, 0)),
        ],
        out_specs=[field_spec(nx, ny, nz, chunk)] + face_specs(nx, ny, nz, chunk),
        out_shape=[jax.ShapeDtypeStruct(h.shape, h.dtype)] + face_shapes(nx, ny, nz, h.dtype),
    )(e, e, h, faces_x, faces_y, faces_z)


def e_step(e, h, faces, inv, ef=None, cells=None):
    _, nx, ny, nz = e.shape
    chunk = CHUNK
    faces_x = toward_upper(faces[0], "gx")
    faces_y = toward_upper(faces[1], "gy")
    faces_z = toward_upper(faces[2], "gz")
    in_specs = [
        field_spec(nx, ny, nz, chunk),
        field_spec(nx, ny, nz, chunk),
        pl.BlockSpec((3, 1, ny, nz), lambda i: (0, jnp.maximum(i * chunk - 1, 0), 0, 0)),
        pl.BlockSpec((chunk, ny, nz), lambda i: (i, 0, 0)),
        pl.BlockSpec((2, 1, ny, nz), lambda i: (0, 0, 0, 0)),
        pl.BlockSpec((2, chunk, 1, nz), lambda i: (0, i, 0, 0)),
        pl.BlockSpec((2, 1, 1, chunk * ny), lambda i: (0, i, 0, 0)),
    ]
    args = [e, h, h, inv, faces_x, faces_y, faces_z]
    if ef is None:
        outs = pl.pallas_call(
            e_kernel,
            grid=(nx // chunk,),
            in_specs=in_specs,
            out_specs=[field_spec(nx, ny, nz, chunk)] + face_specs(nx, ny, nz, chunk),
            out_shape=[jax.ShapeDtypeStruct(e.shape, e.dtype)] + face_shapes(nx, ny, nz, e.dtype),
        )(*args)
        return outs[0], outs[1:]
    count = cells.shape[0]
    zrow = (cells % nz).reshape(1, count)
    rrow = (cells // nz).reshape(1, count)
    return pl.pallas_call(
        e_last_kernel,
        grid=(nx // chunk,),
        in_specs=in_specs
        + [
            field_spec(nx, ny, nz, chunk),
            pl.BlockSpec((1, count), lambda i: (0, 0)),
            pl.BlockSpec((1, count), lambda i: (0, 0)),
        ],
        out_specs=[field_spec(nx, ny, nz, chunk), pl.BlockSpec((1, count), lambda i: (0, 0))],
        out_shape=[jax.ShapeDtypeStruct(e.shape, e.dtype), jax.ShapeDtypeStruct((1, count), jnp.float32)],
        scratch_shapes=[pltpu.VMEM((nz, count), jnp.bfloat16)],
    )(*args, ef, zrow, rrow)


def body(e_forward, e_adjoint, h_adjoint, inv_perm, voxel_cell, voxel_owner, voxel_slot):
    count = voxel_cell.shape[-1]
    voxel_rows = voxel_cell.reshape(count)
    owners = voxel_owner.reshape(count)
    slot_ids = voxel_slot.reshape(count)
    e, h = e_adjoint, h_adjoint
    e_faces = lower_faces_of(e)
    terms = None
    for repeat in range(STEPS):
        h, *h_faces = h_step(e, h, e_faces)
        if repeat == STEPS - 1:
            e, terms = e_step(e, h, h_faces, inv_perm, e_forward, voxel_rows)
        else:
            e, e_faces = e_step(e, h, h_faces, inv_perm)
    terms = terms.reshape(count)
    devices = lax.axis_size("gx") * lax.axis_size("gy") * lax.axis_size("gz")
    owner_hot = (owners[:, None] == lax.broadcasted_iota(jnp.int32, (count, devices), 1)).astype(jnp.float32)
    slot_hot = jnp.where(slot_ids[:, None] == lax.broadcasted_iota(jnp.int32, (count, P_DEV), 1), terms[:, None], 0.0)
    per_owner = jnp.dot(owner_hot.T, slot_hot, precision=lax.Precision.HIGHEST, preferred_element_type=jnp.float32)
    received = lax.all_to_all(per_owner, ("gx", "gy", "gz"), 0, 0, tiled=True)
    gradient = received.sum(axis=0)
    return (e, h, gradient)


def solution(mesh):
    return jax.shard_map(
        body,
        mesh=mesh,
        in_specs=(
            P(None, "gx", "gy", "gz"),
            P(None, "gx", "gy", "gz"),
            P(None, "gx", "gy", "gz"),
            P("gx", "gy", "gz"),
            P("gx", "gy", "gz", None),
            P("gx", "gy", "gz", None, None),
            P("gx", "gy", "gz", None),
        ),
        out_specs=(P(None, "gx", "gy", "gz"), P(None, "gx", "gy", "gz"), P(("gx", "gy", "gz"))),
        check_vma=False,
    )
```

```python
import functools

import jax
import jax.numpy as jnp
from jax import lax
from jax.experimental import pallas as pl
from jax.experimental.pallas import tpu as pltpu
from jax.sharding import PartitionSpec as P

STEPS = 2
P_DEV = 256
CHUNK = 8

courant = 0.5


def toward_lower(x, axis):
    peers = lax.axis_size(axis)
    return lax.ppermute(x, axis, [(j, j - 1) for j in range(1, peers)])


def toward_upper(x, axis):
    peers = lax.axis_size(axis)
    return lax.ppermute(x, axis, [(j, j + 1) for j in range(peers - 1)])


def fwd_y(a, row):
    rolled = pltpu.roll(a, a.shape[-2] - 1, a.ndim - 2)
    at = lax.broadcasted_iota(jnp.int32, a.shape, a.ndim - 2)
    return jnp.where(at == a.shape[-2] - 1, row, rolled)


def fwd_z(a, col):
    rolled = pltpu.roll(a, a.shape[-1] - 1, a.ndim - 1)
    at = lax.broadcasted_iota(jnp.int32, a.shape, a.ndim - 1)
    return jnp.where(at == a.shape[-1] - 1, col, rolled)


def bwd_y(a, row):
    rolled = pltpu.roll(a, 1, a.ndim - 2)
    at = lax.broadcasted_iota(jnp.int32, a.shape, a.ndim - 2)
    return jnp.where(at == 0, row, rolled)


def bwd_z(a, col):
    rolled = pltpu.roll(a, 1, a.ndim - 1)
    at = lax.broadcasted_iota(jnp.int32, a.shape, a.ndim - 1)
    return jnp.where(at == 0, col, rolled)


def column_of(row, b, ny):
    tile = jnp.broadcast_to(row, (128, b * ny))
    return jnp.transpose(tile).reshape(b, ny, 128)[:, :, 0:1]


def row_of(a, lanes):
    b, ny, _ = a.shape
    tile = jnp.transpose(a[:, :, lanes].reshape(b * ny, 128))
    return tile


def fwd_x(a, nxt):
    if a.shape[0] == 1:
        return nxt
    return jnp.concatenate([a[1:], nxt], axis=0)


def bwd_x(a, prv):
    if a.shape[0] == 1:
        return prv
    return jnp.concatenate([prv, a[:-1]], axis=0)


def h_kernel(e_ref, en_ref, h_ref, hx_ref, hy_ref, hz_ref, out_ref, fx_ref, fy_ref, fz_ref):
    last = pl.program_id(0) == pl.num_programs(0) - 1
    _, b, ny, nz = e_ref.shape
    nxt_y = jnp.where(last, hx_ref[0], en_ref[1])
    nxt_z = jnp.where(last, hx_ref[1], en_ref[2])
    col_x = column_of(hz_ref[0, 0], b, ny)
    col_y = column_of(hz_ref[1, 0], b, ny)
    for j in range(b):
        ex, ey, ez = e_ref[0, j], e_ref[1, j], e_ref[2, j]
        ey_xp = e_ref[1, j + 1] if j + 1 < b else nxt_y[0]
        ez_xp = e_ref[2, j + 1] if j + 1 < b else nxt_z[0]
        ez_yp = fwd_y(ez, hy_ref[1, j])
        ex_yp = fwd_y(ex, hy_ref[0, j])
        ey_zp = fwd_z(ey, col_y[j])
        ex_zp = fwd_z(ex, col_x[j])
        out_ref[0, j] = h_ref[0, j] - courant * ((ez_yp - ez) - (ey_zp - ey))
        out_ref[1, j] = h_ref[1, j] - courant * ((ex_zp - ex) - (ez_xp - ez))
        out_ref[2, j] = h_ref[2, j] - courant * ((ey_xp - ey) - (ex_yp - ex))

    @pl.when(last)
    def _():
        fx_ref[0] = out_ref[1, b - 1:b]
        fx_ref[1] = out_ref[2, b - 1:b]

    fy_ref[0] = out_ref[0, :, ny - 1:ny, :]
    fy_ref[1] = out_ref[2, :, ny - 1:ny, :]
    top = slice(nz - 128, nz)
    fz_ref[0, 0] = row_of(out_ref[0], top)[127:128]
    fz_ref[1, 0] = row_of(out_ref[1], top)[127:128]


def e_slabs(e_ref, h_ref, hp_ref, inv_ref, hx_ref, hy_ref, hz_ref, out_ref):
    first = pl.program_id(0) == 0
    _, b, ny, nz = h_ref.shape
    prv_y = jnp.where(first, hx_ref[0], hp_ref[1])
    prv_z = jnp.where(first, hx_ref[1], hp_ref[2])
    col_x = column_of(hz_ref[0, 0], b, ny)
    col_y = column_of(hz_ref[1, 0], b, ny)
    for j in range(b):
        hx, hy, hz = h_ref[0, j], h_ref[1, j], h_ref[2, j]
        hz_xm = h_ref[2, j - 1] if j > 0 else prv_z[0]
        hy_xm = h_ref[1, j - 1] if j > 0 else prv_y[0]
        hz_ym = bwd_y(hz, hy_ref[1, j])
        hx_ym = bwd_y(hx, hy_ref[0, j])
        hy_zm = bwd_z(hy, col_y[j])
        hx_zm = bwd_z(hx, col_x[j])
        scale = courant * inv_ref[j]
        out_ref[0, j] = e_ref[0, j] + scale * ((hz - hz_ym) - (hy - hy_zm))
        out_ref[1, j] = e_ref[1, j] + scale * ((hx - hx_zm) - (hz - hz_xm))
        out_ref[2, j] = e_ref[2, j] + scale * ((hy - hy_xm) - (hx - hx_ym))


def e_kernel(e_ref, h_ref, hp_ref, inv_ref, hx_ref, hy_ref, hz_ref, out_ref, fx_ref, fy_ref, fz_ref):
    e_slabs(e_ref, h_ref, hp_ref, inv_ref, hx_ref, hy_ref, hz_ref, out_ref)

    @pl.when(pl.program_id(0) == 0)
    def _():
        fx_ref[0] = out_ref[1, 0:1]
        fx_ref[1] = out_ref[2, 0:1]

    fy_ref[0] = out_ref[0, :, 0:1, :]
    fy_ref[1] = out_ref[2, :, 0:1, :]
    fz_ref[0, 0] = row_of(out_ref[0], slice(0, 128))[0:1]
    fz_ref[1, 0] = row_of(out_ref[1], slice(0, 128))[0:1]


def split3(a):
    hi = a.astype(jnp.bfloat16)
    rest = a - hi.astype(jnp.float32)
    mid = rest.astype(jnp.bfloat16)
    lo = (rest - mid.astype(jnp.float32)).astype(jnp.bfloat16)
    return hi, mid, lo


def e_last_kernel(
    e_ref, h_ref, hp_ref, inv_ref, hx_ref, hy_ref, hz_ref, ef_ref, zrow_ref, rrow_ref, orow_ref, srow_ref,
    out_ref, owner_ref, terms_ref, zhot_ref
):
    e_slabs(e_ref, h_ref, hp_ref, inv_ref, hx_ref, hy_ref, hz_ref, out_ref)
    new_x, new_y, new_z = out_ref[0], out_ref[1], out_ref[2]
    step = pl.program_id(0)
    b, ny, nz = new_x.shape
    count = zhot_ref.shape[1]

    @pl.when(step == 0)
    def _():
        zhot_ref[...] = (lax.broadcasted_iota(jnp.int32, (nz, count), 0) == zrow_ref[...]).astype(jnp.bfloat16)
        terms_ref[...] = jnp.zeros_like(terms_ref)

    inter = (ef_ref[0] * new_x + ef_ref[1] * new_y + ef_ref[2] * new_z).reshape(b * ny, nz)
    hi = inter.astype(jnp.bfloat16)
    rest = inter - hi.astype(jnp.float32)
    mid = rest.astype(jnp.bfloat16)
    lo = (rest - mid.astype(jnp.float32)).astype(jnp.bfloat16)
    zhot = zhot_ref[...]
    picked = (
        jnp.dot(hi, zhot, preferred_element_type=jnp.float32)
        + jnp.dot(mid, zhot, preferred_element_type=jnp.float32)
    ) + jnp.dot(lo, zhot, preferred_element_type=jnp.float32)
    row_at = step * (b * ny) + lax.broadcasted_iota(jnp.int32, picked.shape, 0)
    terms_ref[...] += jnp.sum(jnp.where(row_at == rrow_ref[...], picked, 0.0), axis=0, keepdims=True)

    @pl.when(step == pl.num_programs(0) - 1)
    def _():
        owners, slots = owner_ref.shape
        weighted = jnp.where(
            lax.broadcasted_iota(jnp.int32, (owners, count), 0) == orow_ref[...], terms_ref[...], 0.0
        )
        slot_hot = (lax.broadcasted_iota(jnp.int32, (slots, count), 0) == srow_ref[...]).astype(jnp.bfloat16)
        hi, mid, lo = split3(weighted)
        nt = (((1,), (1,)), ((), ()))
        owner_ref[...] = (
            lax.dot_general(hi, slot_hot, nt, preferred_element_type=jnp.float32)
            + lax.dot_general(mid, slot_hot, nt, preferred_element_type=jnp.float32)
        ) + lax.dot_general(lo, slot_hot, nt, preferred_element_type=jnp.float32)


def field_spec(nx, ny, nz, chunk):
    return pl.BlockSpec((3, chunk, ny, nz), lambda i: (0, i, 0, 0))


def face_specs(nx, ny, nz, chunk):
    return [
        pl.BlockSpec((2, 1, ny, nz), lambda i: (0, 0, 0, 0)),
        pl.BlockSpec((2, chunk, 1, nz), lambda i: (0, i, 0, 0)),
        pl.BlockSpec((2, 1, 1, chunk * ny), lambda i: (0, i, 0, 0)),
    ]


def face_shapes(nx, ny, nz, dtype):
    return [
        jax.ShapeDtypeStruct((2, 1, ny, nz), dtype),
        jax.ShapeDtypeStruct((2, nx, 1, nz), dtype),
        jax.ShapeDtypeStruct((2, nx // CHUNK, 1, CHUNK * ny), dtype),
    ]


def faces_kernel(slab_ref, rows_ref, lanes_ref, fx_ref, fy_ref, fz_ref):
    fx_ref[0] = slab_ref[1]
    fx_ref[1] = slab_ref[2]
    fy_ref[0] = rows_ref[0, :, 0:1, :]
    fy_ref[1] = rows_ref[2, :, 0:1, :]
    nx = lanes_ref.shape[1]
    for i in range(nx // CHUNK):
        part = slice(i * CHUNK, (i + 1) * CHUNK)
        fz_ref[0, i] = row_of(lanes_ref[0, part], slice(0, 128))[0:1]
        fz_ref[1, i] = row_of(lanes_ref[1, part], slice(0, 128))[0:1]


def lower_faces_of(e):
    _, nx, ny, nz = e.shape
    return pl.pallas_call(
        faces_kernel,
        grid=(1,),
        in_specs=[
            pl.BlockSpec((3, 1, ny, nz), lambda i: (0, 0, 0, 0)),
            pl.BlockSpec((3, nx, 8, nz), lambda i: (0, 0, 0, 0)),
            pl.BlockSpec((3, nx, ny, 128), lambda i: (0, 0, 0, 0)),
        ],
        out_specs=[
            pl.BlockSpec((2, 1, ny, nz), lambda i: (0, 0, 0, 0)),
            pl.BlockSpec((2, nx, 1, nz), lambda i: (0, 0, 0, 0)),
            pl.BlockSpec((2, nx // CHUNK, 1, CHUNK * ny), lambda i: (0, 0, 0, 0)),
        ],
        out_shape=face_shapes(nx, ny, nz, e.dtype),
    )(e, e, e)


def h_step(e, h, faces):
    _, nx, ny, nz = e.shape
    chunk = CHUNK
    faces_x = toward_lower(faces[0], "gx")
    faces_y = toward_lower(faces[1], "gy")
    faces_z = toward_lower(faces[2], "gz")
    return pl.pallas_call(
        h_kernel,
        grid=(nx // chunk,),
        in_specs=[
            field_spec(nx, ny, nz, chunk),
            pl.BlockSpec((3, 1, ny, nz), lambda i: (0, jnp.minimum((i + 1) * chunk, nx - 1), 0, 0)),
            field_spec(nx, ny, nz, chunk),
            pl.BlockSpec((2, 1, ny, nz), lambda i: (0, 0, 0, 0)),
            pl.BlockSpec((2, chunk, 1, nz), lambda i: (0, i, 0, 0)),
            pl.BlockSpec((2, 1, 1, chunk * ny), lambda i: (0, i, 0, 0)),
        ],
        out_specs=[field_spec(nx, ny, nz, chunk)] + face_specs(nx, ny, nz, chunk),
        out_shape=[jax.ShapeDtypeStruct(h.shape, h.dtype)] + face_shapes(nx, ny, nz, h.dtype),
    )(e, e, h, faces_x, faces_y, faces_z)


def e_step(e, h, faces, inv, ef=None, cells=None, owners=None, slots=None, devices=None):
    _, nx, ny, nz = e.shape
    chunk = CHUNK
    faces_x = toward_upper(faces[0], "gx")
    faces_y = toward_upper(faces[1], "gy")
    faces_z = toward_upper(faces[2], "gz")
    in_specs = [
        field_spec(nx, ny, nz, chunk),
        field_spec(nx, ny, nz, chunk),
        pl.BlockSpec((3, 1, ny, nz), lambda i: (0, jnp.maximum(i * chunk - 1, 0), 0, 0)),
        pl.BlockSpec((chunk, ny, nz), lambda i: (i, 0, 0)),
        pl.BlockSpec((2, 1, ny, nz), lambda i: (0, 0, 0, 0)),
        pl.BlockSpec((2, chunk, 1, nz), lambda i: (0, i, 0, 0)),
        pl.BlockSpec((2, 1, 1, chunk * ny), lambda i: (0, i, 0, 0)),
    ]
    args = [e, h, h, inv, faces_x, faces_y, faces_z]
    if ef is None:
        outs = pl.pallas_call(
            e_kernel,
            grid=(nx // chunk,),
            in_specs=in_specs,
            out_specs=[field_spec(nx, ny, nz, chunk)] + face_specs(nx, ny, nz, chunk),
            out_shape=[jax.ShapeDtypeStruct(e.shape, e.dtype)] + face_shapes(nx, ny, nz, e.dtype),
        )(*args)
        return outs[0], outs[1:]
    count = cells.shape[0]
    zrow = (cells % nz).reshape(1, count)
    rrow = (cells // nz).reshape(1, count)
    return pl.pallas_call(
        e_last_kernel,
        grid=(nx // chunk,),
        in_specs=in_specs
        + [
            field_spec(nx, ny, nz, chunk),
            pl.BlockSpec((1, count), lambda i: (0, 0)),
            pl.BlockSpec((1, count), lambda i: (0, 0)),
            pl.BlockSpec((1, count), lambda i: (0, 0)),
            pl.BlockSpec((1, count), lambda i: (0, 0)),
        ],
        out_specs=[field_spec(nx, ny, nz, chunk), pl.BlockSpec((devices, P_DEV), lambda i: (0, 0))],
        out_shape=[jax.ShapeDtypeStruct(e.shape, e.dtype), jax.ShapeDtypeStruct((devices, P_DEV), jnp.float32)],
        scratch_shapes=[pltpu.VMEM((1, count), jnp.float32), pltpu.VMEM((nz, count), jnp.bfloat16)],
    )(*args, ef, zrow, rrow, owners.reshape(1, count), slots.reshape(1, count))


def body(e_forward, e_adjoint, h_adjoint, inv_perm, voxel_cell, voxel_owner, voxel_slot):
    count = voxel_cell.shape[-1]
    voxel_rows = voxel_cell.reshape(count)
    owners = voxel_owner.reshape(count)
    slot_ids = voxel_slot.reshape(count)
    devices = lax.axis_size("gx") * lax.axis_size("gy") * lax.axis_size("gz")
    e, h = e_adjoint, h_adjoint
    e_faces = lower_faces_of(e)
    per_owner = None
    for repeat in range(STEPS):
        h, *h_faces = h_step(e, h, e_faces)
        if repeat == STEPS - 1:
            e, per_owner = e_step(e, h, h_faces, inv_perm, e_forward, voxel_rows, owners, slot_ids, devices)
        else:
            e, e_faces = e_step(e, h, h_faces, inv_perm)
    received = lax.all_to_all(per_owner, ("gx", "gy", "gz"), 0, 0, tiled=True)
    gradient = received.sum(axis=0)
    return (e, h, gradient)


def solution(mesh):
    return jax.shard_map(
        body,
        mesh=mesh,
        in_specs=(
            P(None, "gx", "gy", "gz"),
            P(None, "gx", "gy", "gz"),
            P(None, "gx", "gy", "gz"),
            P("gx", "gy", "gz"),
            P("gx", "gy", "gz", None),
            P("gx", "gy", "gz", None, None),
            P("gx", "gy", "gz", None),
        ),
        out_specs=(P(None, "gx", "gy", "gz"), P(None, "gx", "gy", "gz"), P(("gx", "gy", "gz"))),
        check_vma=False,
    )
```

```python
import functools

import jax
import jax.numpy as jnp
from jax import lax
from jax.experimental import pallas as pl
from jax.experimental.pallas import tpu as pltpu
from jax.sharding import PartitionSpec as P

STEPS = 2
P_DEV = 256
CHUNK = 8

courant = 0.5


def toward_lower(x, axis):
    peers = lax.axis_size(axis)
    return lax.ppermute(x, axis, [(j, j - 1) for j in range(1, peers)])


def toward_upper(x, axis):
    peers = lax.axis_size(axis)
    return lax.ppermute(x, axis, [(j, j + 1) for j in range(peers - 1)])


def fwd_y(a, row):
    rolled = pltpu.roll(a, a.shape[-2] - 1, a.ndim - 2)
    at = lax.broadcasted_iota(jnp.int32, a.shape, a.ndim - 2)
    return jnp.where(at == a.shape[-2] - 1, row, rolled)


def fwd_z(a, col):
    rolled = pltpu.roll(a, a.shape[-1] - 1, a.ndim - 1)
    at = lax.broadcasted_iota(jnp.int32, a.shape, a.ndim - 1)
    return jnp.where(at == a.shape[-1] - 1, col, rolled)


def bwd_y(a, row):
    rolled = pltpu.roll(a, 1, a.ndim - 2)
    at = lax.broadcasted_iota(jnp.int32, a.shape, a.ndim - 2)
    return jnp.where(at == 0, row, rolled)


def bwd_z(a, col):
    rolled = pltpu.roll(a, 1, a.ndim - 1)
    at = lax.broadcasted_iota(jnp.int32, a.shape, a.ndim - 1)
    return jnp.where(at == 0, col, rolled)


def column_of(row, b, ny):
    tile = jnp.broadcast_to(row, (128, b * ny))
    return jnp.transpose(tile).reshape(b, ny, 128)[:, :, 0:1]


def row_of(a, lanes):
    b, ny, _ = a.shape
    tile = jnp.transpose(a[:, :, lanes].reshape(b * ny, 128))
    return tile


def fwd_x(a, nxt):
    if a.shape[0] == 1:
        return nxt
    return jnp.concatenate([a[1:], nxt], axis=0)


def bwd_x(a, prv):
    if a.shape[0] == 1:
        return prv
    return jnp.concatenate([prv, a[:-1]], axis=0)


def h_kernel(e_ref, en_ref, h_ref, hx_ref, hy_ref, hz_ref, out_ref, fx_ref, fy_ref, fz_ref):
    last = pl.program_id(0) == pl.num_programs(0) - 1
    _, b, ny, nz = e_ref.shape
    nxt_y = jnp.where(last, hx_ref[0], en_ref[1])
    nxt_z = jnp.where(last, hx_ref[1], en_ref[2])
    col_x = column_of(hz_ref[0, 0], b, ny)
    col_y = column_of(hz_ref[1, 0], b, ny)
    for j in range(b):
        ex, ey, ez = e_ref[0, j], e_ref[1, j], e_ref[2, j]
        ey_xp = e_ref[1, j + 1] if j + 1 < b else nxt_y[0]
        ez_xp = e_ref[2, j + 1] if j + 1 < b else nxt_z[0]
        ez_yp = fwd_y(ez, hy_ref[1, j])
        ex_yp = fwd_y(ex, hy_ref[0, j])
        ey_zp = fwd_z(ey, col_y[j])
        ex_zp = fwd_z(ex, col_x[j])
        out_ref[0, j] = h_ref[0, j] - courant * ((ez_yp - ez) - (ey_zp - ey))
        out_ref[1, j] = h_ref[1, j] - courant * ((ex_zp - ex) - (ez_xp - ez))
        out_ref[2, j] = h_ref[2, j] - courant * ((ey_xp - ey) - (ex_yp - ex))

    @pl.when(last)
    def _():
        fx_ref[0] = out_ref[1, b - 1:b]
        fx_ref[1] = out_ref[2, b - 1:b]

    fy_ref[0] = out_ref[0, :, ny - 1:ny, :]
    fy_ref[1] = out_ref[2, :, ny - 1:ny, :]
    top = slice(nz - 128, nz)
    fz_ref[0, 0] = row_of(out_ref[0], top)[127:128]
    fz_ref[1, 0] = row_of(out_ref[1], top)[127:128]


def e_slabs(e_ref, h_ref, hp_ref, inv_ref, hx_ref, hy_ref, hz_ref, out_ref):
    first = pl.program_id(0) == 0
    _, b, ny, nz = h_ref.shape
    prv_y = jnp.where(first, hx_ref[0], hp_ref[1])
    prv_z = jnp.where(first, hx_ref[1], hp_ref[2])
    col_x = column_of(hz_ref[0, 0], b, ny)
    col_y = column_of(hz_ref[1, 0], b, ny)
    for j in range(b):
        hx, hy, hz = h_ref[0, j], h_ref[1, j], h_ref[2, j]
        hz_xm = h_ref[2, j - 1] if j > 0 else prv_z[0]
        hy_xm = h_ref[1, j - 1] if j > 0 else prv_y[0]
        hz_ym = bwd_y(hz, hy_ref[1, j])
        hx_ym = bwd_y(hx, hy_ref[0, j])
        hy_zm = bwd_z(hy, col_y[j])
        hx_zm = bwd_z(hx, col_x[j])
        scale = courant * inv_ref[j]
        out_ref[0, j] = e_ref[0, j] + scale * ((hz - hz_ym) - (hy - hy_zm))
        out_ref[1, j] = e_ref[1, j] + scale * ((hx - hx_zm) - (hz - hz_xm))
        out_ref[2, j] = e_ref[2, j] + scale * ((hy - hy_xm) - (hx - hx_ym))


def e_kernel(e_ref, h_ref, hp_ref, inv_ref, hx_ref, hy_ref, hz_ref, out_ref, fx_ref, fy_ref, fz_ref):
    e_slabs(e_ref, h_ref, hp_ref, inv_ref, hx_ref, hy_ref, hz_ref, out_ref)

    @pl.when(pl.program_id(0) == 0)
    def _():
        fx_ref[0] = out_ref[1, 0:1]
        fx_ref[1] = out_ref[2, 0:1]

    fy_ref[0] = out_ref[0, :, 0:1, :]
    fy_ref[1] = out_ref[2, :, 0:1, :]
    fz_ref[0, 0] = row_of(out_ref[0], slice(0, 128))[0:1]
    fz_ref[1, 0] = row_of(out_ref[1], slice(0, 128))[0:1]


def split3(a):
    hi = a.astype(jnp.bfloat16)
    rest = a - hi.astype(jnp.float32)
    mid = rest.astype(jnp.bfloat16)
    lo = (rest - mid.astype(jnp.float32)).astype(jnp.bfloat16)
    return hi, mid, lo


def e_last_kernel(
    e_ref, h_ref, hp_ref, inv_ref, hx_ref, hy_ref, hz_ref, ef_ref, zrow_ref, rrow_ref, orow_ref, srow_ref,
    out_ref, owner_ref, terms_ref, zhot_ref
):
    e_slabs(e_ref, h_ref, hp_ref, inv_ref, hx_ref, hy_ref, hz_ref, out_ref)
    new_x, new_y, new_z = out_ref[0], out_ref[1], out_ref[2]
    step = pl.program_id(0)
    b, ny, nz = new_x.shape
    count = zhot_ref.shape[1]

    @pl.when(step == 0)
    def _():
        zhot_ref[...] = (lax.broadcasted_iota(jnp.int32, (nz, count), 0) == zrow_ref[...]).astype(jnp.bfloat16)
        terms_ref[...] = jnp.zeros_like(terms_ref)

    inter = (ef_ref[0] * new_x + ef_ref[1] * new_y + ef_ref[2] * new_z).reshape(b * ny, nz)
    hi = inter.astype(jnp.bfloat16)
    mid = (inter - hi.astype(jnp.float32)).astype(jnp.bfloat16)
    zhot = zhot_ref[...]
    picked = jnp.dot(hi, zhot, preferred_element_type=jnp.float32) + jnp.dot(mid, zhot, preferred_element_type=jnp.float32)
    row_at = step * (b * ny) + lax.broadcasted_iota(jnp.int32, picked.shape, 0)
    terms_ref[...] += jnp.sum(jnp.where(row_at == rrow_ref[...], picked, 0.0), axis=0, keepdims=True)

    @pl.when(step == pl.num_programs(0) - 1)
    def _():
        owners, _, slots = owner_ref.shape
        weighted = jnp.where(
            lax.broadcasted_iota(jnp.int32, (owners, count), 0) == orow_ref[...], terms_ref[...], 0.0
        )
        slot_hot = (lax.broadcasted_iota(jnp.int32, (slots, count), 0) == srow_ref[...]).astype(jnp.bfloat16)
        hi, mid, lo = split3(weighted)
        nt = (((1,), (1,)), ((), ()))
        summed = (
            lax.dot_general(hi, slot_hot, nt, preferred_element_type=jnp.float32)
            + lax.dot_general(mid, slot_hot, nt, preferred_element_type=jnp.float32)
        ) + lax.dot_general(lo, slot_hot, nt, preferred_element_type=jnp.float32)
        owner_ref[...] = summed.reshape(owners, 1, slots)


def field_spec(nx, ny, nz, chunk):
    return pl.BlockSpec((3, chunk, ny, nz), lambda i: (0, i, 0, 0))


def face_specs(nx, ny, nz, chunk):
    return [
        pl.BlockSpec((2, 1, ny, nz), lambda i: (0, 0, 0, 0)),
        pl.BlockSpec((2, chunk, 1, nz), lambda i: (0, i, 0, 0)),
        pl.BlockSpec((2, 1, 1, chunk * ny), lambda i: (0, i, 0, 0)),
    ]


def face_shapes(nx, ny, nz, dtype):
    return [
        jax.ShapeDtypeStruct((2, 1, ny, nz), dtype),
        jax.ShapeDtypeStruct((2, nx, 1, nz), dtype),
        jax.ShapeDtypeStruct((2, nx // CHUNK, 1, CHUNK * ny), dtype),
    ]


def faces_kernel(slab_ref, rows_ref, lanes_ref, fx_ref, fy_ref, fz_ref):
    fx_ref[0] = slab_ref[1]
    fx_ref[1] = slab_ref[2]
    fy_ref[0] = rows_ref[0, :, 0:1, :]
    fy_ref[1] = rows_ref[2, :, 0:1, :]
    nx = lanes_ref.shape[1]
    for i in range(nx // CHUNK):
        part = slice(i * CHUNK, (i + 1) * CHUNK)
        fz_ref[0, i] = row_of(lanes_ref[0, part], slice(0, 128))[0:1]
        fz_ref[1, i] = row_of(lanes_ref[1, part], slice(0, 128))[0:1]


def lower_faces_of(e):
    _, nx, ny, nz = e.shape
    return pl.pallas_call(
        faces_kernel,
        grid=(1,),
        in_specs=[
            pl.BlockSpec((3, 1, ny, nz), lambda i: (0, 0, 0, 0)),
            pl.BlockSpec((3, nx, 8, nz), lambda i: (0, 0, 0, 0)),
            pl.BlockSpec((3, nx, ny, 128), lambda i: (0, 0, 0, 0)),
        ],
        out_specs=[
            pl.BlockSpec((2, 1, ny, nz), lambda i: (0, 0, 0, 0)),
            pl.BlockSpec((2, nx, 1, nz), lambda i: (0, 0, 0, 0)),
            pl.BlockSpec((2, nx // CHUNK, 1, CHUNK * ny), lambda i: (0, 0, 0, 0)),
        ],
        out_shape=face_shapes(nx, ny, nz, e.dtype),
    )(e, e, e)


def h_step(e, h, faces):
    _, nx, ny, nz = e.shape
    chunk = CHUNK
    faces_x = toward_lower(faces[0], "gx")
    faces_y = toward_lower(faces[1], "gy")
    faces_z = toward_lower(faces[2], "gz")
    return pl.pallas_call(
        h_kernel,
        grid=(nx // chunk,),
        in_specs=[
            field_spec(nx, ny, nz, chunk),
            pl.BlockSpec((3, 1, ny, nz), lambda i: (0, jnp.minimum((i + 1) * chunk, nx - 1), 0, 0)),
            field_spec(nx, ny, nz, chunk),
            pl.BlockSpec((2, 1, ny, nz), lambda i: (0, 0, 0, 0)),
            pl.BlockSpec((2, chunk, 1, nz), lambda i: (0, i, 0, 0)),
            pl.BlockSpec((2, 1, 1, chunk * ny), lambda i: (0, i, 0, 0)),
        ],
        out_specs=[field_spec(nx, ny, nz, chunk)] + face_specs(nx, ny, nz, chunk),
        out_shape=[jax.ShapeDtypeStruct(h.shape, h.dtype)] + face_shapes(nx, ny, nz, h.dtype),
    )(e, e, h, faces_x, faces_y, faces_z)


def e_step(e, h, faces, inv, ef=None, cells=None, owners=None, slots=None, devices=None):
    _, nx, ny, nz = e.shape
    chunk = CHUNK
    faces_x = toward_upper(faces[0], "gx")
    faces_y = toward_upper(faces[1], "gy")
    faces_z = toward_upper(faces[2], "gz")
    in_specs = [
        field_spec(nx, ny, nz, chunk),
        field_spec(nx, ny, nz, chunk),
        pl.BlockSpec((3, 1, ny, nz), lambda i: (0, jnp.maximum(i * chunk - 1, 0), 0, 0)),
        pl.BlockSpec((chunk, ny, nz), lambda i: (i, 0, 0)),
        pl.BlockSpec((2, 1, ny, nz), lambda i: (0, 0, 0, 0)),
        pl.BlockSpec((2, chunk, 1, nz), lambda i: (0, i, 0, 0)),
        pl.BlockSpec((2, 1, 1, chunk * ny), lambda i: (0, i, 0, 0)),
    ]
    args = [e, h, h, inv, faces_x, faces_y, faces_z]
    if ef is None:
        outs = pl.pallas_call(
            e_kernel,
            grid=(nx // chunk,),
            in_specs=in_specs,
            out_specs=[field_spec(nx, ny, nz, chunk)] + face_specs(nx, ny, nz, chunk),
            out_shape=[jax.ShapeDtypeStruct(e.shape, e.dtype)] + face_shapes(nx, ny, nz, e.dtype),
        )(*args)
        return outs[0], outs[1:]
    count = cells.shape[0]
    zrow = (cells % nz).reshape(1, count)
    rrow = (cells // nz).reshape(1, count)
    return pl.pallas_call(
        e_last_kernel,
        grid=(nx // chunk,),
        in_specs=in_specs
        + [
            field_spec(nx, ny, nz, chunk),
            pl.BlockSpec((1, count), lambda i: (0, 0)),
            pl.BlockSpec((1, count), lambda i: (0, 0)),
            pl.BlockSpec((1, count), lambda i: (0, 0)),
            pl.BlockSpec((1, count), lambda i: (0, 0)),
        ],
        out_specs=[field_spec(nx, ny, nz, chunk), pl.BlockSpec((devices, 1, P_DEV), lambda i: (0, 0, 0))],
        out_shape=[jax.ShapeDtypeStruct(e.shape, e.dtype), jax.ShapeDtypeStruct((devices, 1, P_DEV), jnp.float32)],
        scratch_shapes=[pltpu.VMEM((1, count), jnp.float32), pltpu.VMEM((nz, count), jnp.bfloat16)],
    )(*args, ef, zrow, rrow, owners.reshape(1, count), slots.reshape(1, count))


def body(e_forward, e_adjoint, h_adjoint, inv_perm, voxel_cell, voxel_owner, voxel_slot):
    count = voxel_cell.shape[-1]
    voxel_rows = voxel_cell.reshape(count)
    owners = voxel_owner.reshape(count)
    slot_ids = voxel_slot.reshape(count)
    devices = lax.axis_size("gx") * lax.axis_size("gy") * lax.axis_size("gz")
    e, h = e_adjoint, h_adjoint
    e_faces = lower_faces_of(e)
    per_owner = None
    for repeat in range(STEPS):
        h, *h_faces = h_step(e, h, e_faces)
        if repeat == STEPS - 1:
            e, per_owner = e_step(e, h, h_faces, inv_perm, e_forward, voxel_rows, owners, slot_ids, devices)
        else:
            e, e_faces = e_step(e, h, h_faces, inv_perm)
    received = lax.all_to_all(per_owner, ("gx", "gy", "gz"), 0, 0, tiled=True)
    gradient = received.sum(axis=(0, 1))
    return (e, h, gradient)


def solution(mesh):
    return jax.shard_map(
        body,
        mesh=mesh,
        in_specs=(
            P(None, "gx", "gy", "gz"),
            P(None, "gx", "gy", "gz"),
            P(None, "gx", "gy", "gz"),
            P("gx", "gy", "gz"),
            P("gx", "gy", "gz", None),
            P("gx", "gy", "gz", None, None),
            P("gx", "gy", "gz", None),
        ),
        out_specs=(P(None, "gx", "gy", "gz"), P(None, "gx", "gy", "gz"), P(("gx", "gy", "gz"))),
        check_vma=False,
    )
```

```python
import jax
import jax.numpy as jnp
from jax import lax
from jax.experimental import pallas as pl
from jax.experimental.pallas import tpu as pltpu
from jax.sharding import PartitionSpec as P


STEPS = 2
P_DEV = 256
CHUNK = 8

courant = 0.5


def toward_lower(x, axis):
    peers = lax.axis_size(axis)
    return lax.ppermute(x, axis, [(j, j - 1) for j in range(1, peers)])


def toward_upper(x, axis):
    peers = lax.axis_size(axis)
    return lax.ppermute(x, axis, [(j, j + 1) for j in range(peers - 1)])


def fwd_y(a, row):
    rolled = pltpu.roll(a, a.shape[-2] - 1, a.ndim - 2)
    at = lax.broadcasted_iota(jnp.int32, a.shape, a.ndim - 2)
    return jnp.where(at == a.shape[-2] - 1, row, rolled)


def fwd_z(a, col):
    rolled = pltpu.roll(a, a.shape[-1] - 1, a.ndim - 1)
    at = lax.broadcasted_iota(jnp.int32, a.shape, a.ndim - 1)
    return jnp.where(at == a.shape[-1] - 1, col, rolled)


def bwd_y(a, row):
    rolled = pltpu.roll(a, 1, a.ndim - 2)
    at = lax.broadcasted_iota(jnp.int32, a.shape, a.ndim - 2)
    return jnp.where(at == 0, row, rolled)


def bwd_z(a, col):
    rolled = pltpu.roll(a, 1, a.ndim - 1)
    at = lax.broadcasted_iota(jnp.int32, a.shape, a.ndim - 1)
    return jnp.where(at == 0, col, rolled)


def column_of(row, b, ny):
    tile = jnp.broadcast_to(row, (128, b * ny))
    return jnp.transpose(tile).reshape(b, ny, 128)[:, :, 0:1]


def row_of(a, lanes):
    b, ny, _ = a.shape
    tile = jnp.transpose(a[:, :, lanes].reshape(b * ny, 128))
    return tile


def h_kernel(e_ref, en_ref, h_ref, hx_ref, hy_ref, hz_ref, out_ref, fx_ref, fy_ref, fz_ref):
    last = pl.program_id(0) == pl.num_programs(0) - 1
    _, b, ny, nz = e_ref.shape
    nxt_y = jnp.where(last, hx_ref[0], en_ref[1])
    nxt_z = jnp.where(last, hx_ref[1], en_ref[2])
    col_x = column_of(hz_ref[0, 0], b, ny)
    col_y = column_of(hz_ref[1, 0], b, ny)
    for j in range(b):
        ex, ey, ez = e_ref[0, j], e_ref[1, j], e_ref[2, j]
        ey_xp = e_ref[1, j + 1] if j + 1 < b else nxt_y[0]
        ez_xp = e_ref[2, j + 1] if j + 1 < b else nxt_z[0]
        ez_yp = fwd_y(ez, hy_ref[1, j])
        ex_yp = fwd_y(ex, hy_ref[0, j])
        ey_zp = fwd_z(ey, col_y[j])
        ex_zp = fwd_z(ex, col_x[j])
        out_ref[0, j] = h_ref[0, j] - courant * ((ez_yp - ez) - (ey_zp - ey))
        out_ref[1, j] = h_ref[1, j] - courant * ((ex_zp - ex) - (ez_xp - ez))
        out_ref[2, j] = h_ref[2, j] - courant * ((ey_xp - ey) - (ex_yp - ex))

    @pl.when(last)
    def _():
        fx_ref[0] = out_ref[1, b - 1:b]
        fx_ref[1] = out_ref[2, b - 1:b]

    fy_ref[0] = out_ref[0, :, ny - 1:ny, :]
    fy_ref[1] = out_ref[2, :, ny - 1:ny, :]
    top = slice(nz - 128, nz)
    fz_ref[0, 0] = row_of(out_ref[0], top)[127:128]
    fz_ref[1, 0] = row_of(out_ref[1], top)[127:128]


def e_slabs(e_ref, h_ref, hp_ref, inv_ref, hx_ref, hy_ref, hz_ref, out_ref):
    first = pl.program_id(0) == 0
    _, b, ny, _ = h_ref.shape
    prv_y = jnp.where(first, hx_ref[0], hp_ref[1])
    prv_z = jnp.where(first, hx_ref[1], hp_ref[2])
    col_x = column_of(hz_ref[0, 0], b, ny)
    col_y = column_of(hz_ref[1, 0], b, ny)
    for j in range(b):
        hx, hy, hz = h_ref[0, j], h_ref[1, j], h_ref[2, j]
        hz_xm = h_ref[2, j - 1] if j > 0 else prv_z[0]
        hy_xm = h_ref[1, j - 1] if j > 0 else prv_y[0]
        hz_ym = bwd_y(hz, hy_ref[1, j])
        hx_ym = bwd_y(hx, hy_ref[0, j])
        hy_zm = bwd_z(hy, col_y[j])
        hx_zm = bwd_z(hx, col_x[j])
        scale = courant * inv_ref[j]
        out_ref[0, j] = e_ref[0, j] + scale * ((hz - hz_ym) - (hy - hy_zm))
        out_ref[1, j] = e_ref[1, j] + scale * ((hx - hx_zm) - (hz - hz_xm))
        out_ref[2, j] = e_ref[2, j] + scale * ((hy - hy_xm) - (hx - hx_ym))


def e_kernel(e_ref, h_ref, hp_ref, inv_ref, hx_ref, hy_ref, hz_ref, out_ref, fx_ref, fy_ref, fz_ref):
    e_slabs(e_ref, h_ref, hp_ref, inv_ref, hx_ref, hy_ref, hz_ref, out_ref)

    @pl.when(pl.program_id(0) == 0)
    def _():
        fx_ref[0] = out_ref[1, 0:1]
        fx_ref[1] = out_ref[2, 0:1]

    fy_ref[0] = out_ref[0, :, 0:1, :]
    fy_ref[1] = out_ref[2, :, 0:1, :]
    fz_ref[0, 0] = row_of(out_ref[0], slice(0, 128))[0:1]
    fz_ref[1, 0] = row_of(out_ref[1], slice(0, 128))[0:1]


def split3(a):
    hi = a.astype(jnp.bfloat16)
    rest = a - hi.astype(jnp.float32)
    mid = rest.astype(jnp.bfloat16)
    lo = (rest - mid.astype(jnp.float32)).astype(jnp.bfloat16)
    return hi, mid, lo


def e_last_kernel(
    e_ref, h_ref, hp_ref, inv_ref, hx_ref, hy_ref, hz_ref, ef_ref, zrow_ref, rrow_ref, orow_ref, srow_ref,
    out_ref, owner_ref, terms_ref, zhot_ref
):
    e_slabs(e_ref, h_ref, hp_ref, inv_ref, hx_ref, hy_ref, hz_ref, out_ref)
    new_x, new_y, new_z = out_ref[0], out_ref[1], out_ref[2]
    step = pl.program_id(0)
    b, ny, nz = new_x.shape
    count = zhot_ref.shape[1]

    @pl.when(step == 0)
    def _():
        zhot_ref[...] = (lax.broadcasted_iota(jnp.int32, (nz, count), 0) == zrow_ref[...]).astype(jnp.bfloat16)
        terms_ref[...] = jnp.zeros_like(terms_ref)

    inter = (ef_ref[0] * new_x + ef_ref[1] * new_y + ef_ref[2] * new_z).reshape(b * ny, nz)
    hi = inter.astype(jnp.bfloat16)
    mid = (inter - hi.astype(jnp.float32)).astype(jnp.bfloat16)
    zhot = zhot_ref[...]
    picked = jnp.dot(hi, zhot, preferred_element_type=jnp.float32) + jnp.dot(mid, zhot, preferred_element_type=jnp.float32)
    row_at = step * (b * ny) + lax.broadcasted_iota(jnp.int32, picked.shape, 0)
    terms_ref[...] += jnp.sum(jnp.where(row_at == rrow_ref[...], picked, 0.0), axis=0, keepdims=True)

    @pl.when(step == pl.num_programs(0) - 1)
    def _():
        owners, _, slots = owner_ref.shape
        weighted = jnp.where(
            lax.broadcasted_iota(jnp.int32, (owners, count), 0) == orow_ref[...], terms_ref[...], 0.0
        )
        slot_hot = (lax.broadcasted_iota(jnp.int32, (slots, count), 0) == srow_ref[...]).astype(jnp.bfloat16)
        hi, mid, lo = split3(weighted)
        nt = (((1,), (1,)), ((), ()))
        summed = (
            lax.dot_general(hi, slot_hot, nt, preferred_element_type=jnp.float32)
            + lax.dot_general(mid, slot_hot, nt, preferred_element_type=jnp.float32)
        ) + lax.dot_general(lo, slot_hot, nt, preferred_element_type=jnp.float32)
        owner_ref[...] = summed.reshape(owners, 1, slots)


def field_spec(ny, nz, chunk):
    return pl.BlockSpec((3, chunk, ny, nz), lambda i: (0, i, 0, 0))


def face_specs(ny, nz, chunk):
    return [
        pl.BlockSpec((2, 1, ny, nz), lambda i: (0, 0, 0, 0)),
        pl.BlockSpec((2, chunk, 1, nz), lambda i: (0, i, 0, 0)),
        pl.BlockSpec((2, 1, 1, chunk * ny), lambda i: (0, i, 0, 0)),
    ]


def face_shapes(nx, ny, nz, dtype):
    return [
        jax.ShapeDtypeStruct((2, 1, ny, nz), dtype),
        jax.ShapeDtypeStruct((2, nx, 1, nz), dtype),
        jax.ShapeDtypeStruct((2, nx // CHUNK, 1, CHUNK * ny), dtype),
    ]


def faces_kernel(slab_ref, rows_ref, lanes_ref, fx_ref, fy_ref, fz_ref):
    fx_ref[0] = slab_ref[1]
    fx_ref[1] = slab_ref[2]
    fy_ref[0] = rows_ref[0, :, 0:1, :]
    fy_ref[1] = rows_ref[2, :, 0:1, :]
    nx = lanes_ref.shape[1]
    for i in range(nx // CHUNK):
        part = slice(i * CHUNK, (i + 1) * CHUNK)
        fz_ref[0, i] = row_of(lanes_ref[0, part], slice(0, 128))[0:1]
        fz_ref[1, i] = row_of(lanes_ref[1, part], slice(0, 128))[0:1]


def lower_faces_of(e):
    _, nx, ny, nz = e.shape
    return pl.pallas_call(
        faces_kernel,
        grid=(1,),
        in_specs=[
            pl.BlockSpec((3, 1, ny, nz), lambda i: (0, 0, 0, 0)),
            pl.BlockSpec((3, nx, 8, nz), lambda i: (0, 0, 0, 0)),
            pl.BlockSpec((3, nx, ny, 128), lambda i: (0, 0, 0, 0)),
        ],
        out_specs=[
            pl.BlockSpec((2, 1, ny, nz), lambda i: (0, 0, 0, 0)),
            pl.BlockSpec((2, nx, 1, nz), lambda i: (0, 0, 0, 0)),
            pl.BlockSpec((2, nx // CHUNK, 1, CHUNK * ny), lambda i: (0, 0, 0, 0)),
        ],
        out_shape=face_shapes(nx, ny, nz, e.dtype),
    )(e, e, e)


def h_step(e, h, faces):
    _, nx, ny, nz = e.shape
    chunk = CHUNK
    faces_z = toward_lower(faces[2], "gz")
    faces_y = toward_lower(faces[1], "gy")
    faces_x = toward_lower(faces[0], "gx")
    return pl.pallas_call(
        h_kernel,
        grid=(nx // chunk,),
        in_specs=[
            field_spec(ny, nz, chunk),
            pl.BlockSpec((3, 1, ny, nz), lambda i: (0, jnp.minimum((i + 1) * chunk, nx - 1), 0, 0)),
            field_spec(ny, nz, chunk),
            pl.BlockSpec((2, 1, ny, nz), lambda i: (0, 0, 0, 0)),
            pl.BlockSpec((2, chunk, 1, nz), lambda i: (0, i, 0, 0)),
            pl.BlockSpec((2, 1, 1, chunk * ny), lambda i: (0, i, 0, 0)),
        ],
        out_specs=[field_spec(ny, nz, chunk)] + face_specs(ny, nz, chunk),
        out_shape=[jax.ShapeDtypeStruct(h.shape, h.dtype)] + face_shapes(nx, ny, nz, h.dtype),
    )(e, e, h, faces_x, faces_y, faces_z)


def e_step(e, h, faces, inv, ef=None, cells=None, owners=None, slots=None, devices=None):
    _, nx, ny, nz = e.shape
    chunk = CHUNK
    faces_z = toward_upper(faces[2], "gz")
    faces_y = toward_upper(faces[1], "gy")
    faces_x = toward_upper(faces[0], "gx")
    in_specs = [
        field_spec(ny, nz, chunk),
        field_spec(ny, nz, chunk),
        pl.BlockSpec((3, 1, ny, nz), lambda i: (0, jnp.maximum(i * chunk - 1, 0), 0, 0)),
        pl.BlockSpec((chunk, ny, nz), lambda i: (i, 0, 0)),
        pl.BlockSpec((2, 1, ny, nz), lambda i: (0, 0, 0, 0)),
        pl.BlockSpec((2, chunk, 1, nz), lambda i: (0, i, 0, 0)),
        pl.BlockSpec((2, 1, 1, chunk * ny), lambda i: (0, i, 0, 0)),
    ]
    args = [e, h, h, inv, faces_x, faces_y, faces_z]
    if ef is None:
        outs = pl.pallas_call(
            e_kernel,
            grid=(nx // chunk,),
            in_specs=in_specs,
            out_specs=[field_spec(ny, nz, chunk)] + face_specs(ny, nz, chunk),
            out_shape=[jax.ShapeDtypeStruct(e.shape, e.dtype)] + face_shapes(nx, ny, nz, e.dtype),
        )(*args)
        return outs[0], outs[1:]
    count = cells.shape[0]
    zrow = (cells % nz).reshape(1, count)
    rrow = (cells // nz).reshape(1, count)
    return pl.pallas_call(
        e_last_kernel,
        grid=(nx // chunk,),
        in_specs=in_specs
        + [
            field_spec(ny, nz, chunk),
            pl.BlockSpec((1, count), lambda i: (0, 0)),
            pl.BlockSpec((1, count), lambda i: (0, 0)),
            pl.BlockSpec((1, count), lambda i: (0, 0)),
            pl.BlockSpec((1, count), lambda i: (0, 0)),
        ],
        out_specs=[field_spec(ny, nz, chunk), pl.BlockSpec((devices, 1, P_DEV), lambda i: (0, 0, 0))],
        out_shape=[jax.ShapeDtypeStruct(e.shape, e.dtype), jax.ShapeDtypeStruct((devices, 1, P_DEV), jnp.float32)],
        scratch_shapes=[pltpu.VMEM((1, count), jnp.float32), pltpu.VMEM((nz, count), jnp.bfloat16)],
    )(*args, ef, zrow, rrow, owners.reshape(1, count), slots.reshape(1, count))


def body(e_forward, e_adjoint, h_adjoint, inv_perm, voxel_cell, voxel_owner, voxel_slot):
    count = voxel_cell.shape[-1]
    voxel_rows = voxel_cell.reshape(count)
    owners = voxel_owner.reshape(count)
    slot_ids = voxel_slot.reshape(count)
    devices = lax.axis_size("gx") * lax.axis_size("gy") * lax.axis_size("gz")
    e, h = e_adjoint, h_adjoint
    e_faces = lower_faces_of(e)
    per_owner = None
    for repeat in range(STEPS):
        h, *h_faces = h_step(e, h, e_faces)
        if repeat == STEPS - 1:
            e, per_owner = e_step(e, h, h_faces, inv_perm, e_forward, voxel_rows, owners, slot_ids, devices)
        else:
            e, e_faces = e_step(e, h, h_faces, inv_perm)
    received = lax.all_to_all(per_owner, ("gx", "gy", "gz"), 0, 0, tiled=True)
    gradient = received.sum(axis=(0, 1))
    return (e, h, gradient)


def solution(mesh):
    return jax.shard_map(
        body,
        mesh=mesh,
        in_specs=(
            P(None, "gx", "gy", "gz"),
            P(None, "gx", "gy", "gz"),
            P(None, "gx", "gy", "gz"),
            P("gx", "gy", "gz"),
            P("gx", "gy", "gz", None),
            P("gx", "gy", "gz", None, None),
            P("gx", "gy", "gz", None),
        ),
        out_specs=(P(None, "gx", "gy", "gz"), P(None, "gx", "gy", "gz"), P(("gx", "gy", "gz"))),
        check_vma=False,
    )
```

```python
import jax
import jax.numpy as jnp
from jax import lax
from jax.experimental import pallas as pl
from jax.experimental.pallas import tpu as pltpu
from jax.sharding import PartitionSpec as P


STEPS = 2
P_DEV = 256
CHUNK = 8

courant = 0.5


def toward_lower(x, axis):
    peers = lax.axis_size(axis)
    return lax.ppermute(x, axis, [(j, j - 1) for j in range(1, peers)])


def toward_upper(x, axis):
    peers = lax.axis_size(axis)
    return lax.ppermute(x, axis, [(j, j + 1) for j in range(peers - 1)])


def fwd_y(a, row):
    rolled = pltpu.roll(a, a.shape[-2] - 1, a.ndim - 2)
    at = lax.broadcasted_iota(jnp.int32, a.shape, a.ndim - 2)
    return jnp.where(at == a.shape[-2] - 1, row, rolled)


def fwd_z(a, col):
    rolled = pltpu.roll(a, a.shape[-1] - 1, a.ndim - 1)
    at = lax.broadcasted_iota(jnp.int32, a.shape, a.ndim - 1)
    return jnp.where(at == a.shape[-1] - 1, col, rolled)


def bwd_y(a, row):
    rolled = pltpu.roll(a, 1, a.ndim - 2)
    at = lax.broadcasted_iota(jnp.int32, a.shape, a.ndim - 2)
    return jnp.where(at == 0, row, rolled)


def bwd_z(a, col):
    rolled = pltpu.roll(a, 1, a.ndim - 1)
    at = lax.broadcasted_iota(jnp.int32, a.shape, a.ndim - 1)
    return jnp.where(at == 0, col, rolled)


def column_of(row, b, ny):
    tile = jnp.broadcast_to(row, (128, b * ny))
    return jnp.transpose(tile).reshape(b, ny, 128)[:, :, 0:1]


def row_of(a, lanes):
    b, ny, _ = a.shape
    tile = jnp.transpose(a[:, :, lanes].reshape(b * ny, 128))
    return tile


def h_kernel(e_ref, en_ref, h_ref, hx_ref, hy_ref, hz_ref, out_ref, fx_ref, fy_ref, fz_ref):
    last = pl.program_id(0) == pl.num_programs(0) - 1
    _, b, ny, nz = e_ref.shape
    nxt_y = jnp.where(last, hx_ref[0], en_ref[1])
    nxt_z = jnp.where(last, hx_ref[1], en_ref[2])
    col_x = column_of(hz_ref[0, 0], b, ny)
    col_y = column_of(hz_ref[1, 0], b, ny)
    for j in range(b):
        ex, ey, ez = e_ref[0, j], e_ref[1, j], e_ref[2, j]
        ey_xp = e_ref[1, j + 1] if j + 1 < b else nxt_y[0]
        ez_xp = e_ref[2, j + 1] if j + 1 < b else nxt_z[0]
        ez_yp = fwd_y(ez, hy_ref[1, j])
        ex_yp = fwd_y(ex, hy_ref[0, j])
        ey_zp = fwd_z(ey, col_y[j])
        ex_zp = fwd_z(ex, col_x[j])
        out_ref[0, j] = h_ref[0, j] - courant * ((ez_yp - ez) - (ey_zp - ey))
        out_ref[1, j] = h_ref[1, j] - courant * ((ex_zp - ex) - (ez_xp - ez))
        out_ref[2, j] = h_ref[2, j] - courant * ((ey_xp - ey) - (ex_yp - ex))

    @pl.when(last)
    def _():
        fx_ref[0] = out_ref[1, b - 1:b]
        fx_ref[1] = out_ref[2, b - 1:b]

    fy_ref[0] = out_ref[0, :, ny - 1:ny, :]
    fy_ref[1] = out_ref[2, :, ny - 1:ny, :]
    top = slice(nz - 128, nz)
    fz_ref[0, 0] = row_of(out_ref[0], top)[127:128]
    fz_ref[1, 0] = row_of(out_ref[1], top)[127:128]


def e_slabs(e_ref, h_ref, hp_ref, inv_ref, hx_ref, hy_ref, hz_ref, out_ref):
    first = pl.program_id(0) == 0
    _, b, ny, _ = h_ref.shape
    prv_y = jnp.where(first, hx_ref[0], hp_ref[1])
    prv_z = jnp.where(first, hx_ref[1], hp_ref[2])
    col_x = column_of(hz_ref[0, 0], b, ny)
    col_y = column_of(hz_ref[1, 0], b, ny)
    for j in range(b):
        hx, hy, hz = h_ref[0, j], h_ref[1, j], h_ref[2, j]
        hz_xm = h_ref[2, j - 1] if j > 0 else prv_z[0]
        hy_xm = h_ref[1, j - 1] if j > 0 else prv_y[0]
        hz_ym = bwd_y(hz, hy_ref[1, j])
        hx_ym = bwd_y(hx, hy_ref[0, j])
        hy_zm = bwd_z(hy, col_y[j])
        hx_zm = bwd_z(hx, col_x[j])
        scale = courant * inv_ref[j]
        out_ref[0, j] = e_ref[0, j] + scale * ((hz - hz_ym) - (hy - hy_zm))
        out_ref[1, j] = e_ref[1, j] + scale * ((hx - hx_zm) - (hz - hz_xm))
        out_ref[2, j] = e_ref[2, j] + scale * ((hy - hy_xm) - (hx - hx_ym))


def e_kernel(e_ref, h_ref, hp_ref, inv_ref, hx_ref, hy_ref, hz_ref, out_ref, fx_ref, fy_ref, fz_ref):
    e_slabs(e_ref, h_ref, hp_ref, inv_ref, hx_ref, hy_ref, hz_ref, out_ref)

    @pl.when(pl.program_id(0) == 0)
    def _():
        fx_ref[0] = out_ref[1, 0:1]
        fx_ref[1] = out_ref[2, 0:1]

    fy_ref[0] = out_ref[0, :, 0:1, :]
    fy_ref[1] = out_ref[2, :, 0:1, :]
    fz_ref[0, 0] = row_of(out_ref[0], slice(0, 128))[0:1]
    fz_ref[1, 0] = row_of(out_ref[1], slice(0, 128))[0:1]


def split3(a):
    hi = a.astype(jnp.bfloat16)
    rest = a - hi.astype(jnp.float32)
    mid = rest.astype(jnp.bfloat16)
    lo = (rest - mid.astype(jnp.float32)).astype(jnp.bfloat16)
    return hi, mid, lo


def e_last_kernel(
    e_ref, h_ref, hp_ref, inv_ref, hx_ref, hy_ref, hz_ref, ef_ref, zrow_ref, rrow_ref, orow_ref, srow_ref,
    out_ref, owner_ref, terms_ref, zhot_ref
):
    e_slabs(e_ref, h_ref, hp_ref, inv_ref, hx_ref, hy_ref, hz_ref, out_ref)
    new_x, new_y, new_z = out_ref[0], out_ref[1], out_ref[2]
    step = pl.program_id(0)
    b, ny, nz = new_x.shape
    count = zhot_ref.shape[1]

    @pl.when(step == 0)
    def _():
        zhot_ref[...] = (lax.broadcasted_iota(jnp.int32, (nz, count), 0) == zrow_ref[...]).astype(jnp.bfloat16)
        terms_ref[...] = jnp.zeros_like(terms_ref)

    inter = (ef_ref[0] * new_x + ef_ref[1] * new_y + ef_ref[2] * new_z).reshape(b * ny, nz)
    hi = inter.astype(jnp.bfloat16)
    mid = (inter - hi.astype(jnp.float32)).astype(jnp.bfloat16)
    zhot = zhot_ref[...]
    picked = jnp.dot(hi, zhot, preferred_element_type=jnp.float32) + jnp.dot(mid, zhot, preferred_element_type=jnp.float32)
    row_at = step * (b * ny) + lax.broadcasted_iota(jnp.int32, picked.shape, 0)
    terms_ref[...] += jnp.sum(jnp.where(row_at == rrow_ref[...], picked, 0.0), axis=0, keepdims=True)

    @pl.when(step == pl.num_programs(0) - 1)
    def _():
        owners, _, slots = owner_ref.shape
        weighted = jnp.where(
            lax.broadcasted_iota(jnp.int32, (owners, count), 0) == orow_ref[...], terms_ref[...], 0.0
        )
        slot_hot = (lax.broadcasted_iota(jnp.int32, (slots, count), 0) == srow_ref[...]).astype(jnp.bfloat16)
        hi, mid, lo = split3(weighted)
        nt = (((1,), (1,)), ((), ()))
        summed = (
            lax.dot_general(hi, slot_hot, nt, preferred_element_type=jnp.float32)
            + lax.dot_general(mid, slot_hot, nt, preferred_element_type=jnp.float32)
        ) + lax.dot_general(lo, slot_hot, nt, preferred_element_type=jnp.float32)
        owner_ref[...] = summed.reshape(owners, 1, slots)


def field_spec(ny, nz, chunk):
    return pl.BlockSpec((3, chunk, ny, nz), lambda i: (0, i, 0, 0))


def face_specs(ny, nz, chunk):
    return [
        pl.BlockSpec((2, 1, ny, nz), lambda i: (0, 0, 0, 0)),
        pl.BlockSpec((2, chunk, 1, nz), lambda i: (0, i, 0, 0)),
        pl.BlockSpec((2, 1, 1, chunk * ny), lambda i: (0, i, 0, 0)),
    ]


def face_shapes(nx, ny, nz, dtype):
    return [
        jax.ShapeDtypeStruct((2, 1, ny, nz), dtype),
        jax.ShapeDtypeStruct((2, nx, 1, nz), dtype),
        jax.ShapeDtypeStruct((2, nx // CHUNK, 1, CHUNK * ny), dtype),
    ]


def faces_kernel(rows_ref, lanes_ref, fy_ref, fz_ref):
    fy_ref[0] = rows_ref[0, :, 0:1, :]
    fy_ref[1] = rows_ref[2, :, 0:1, :]
    nx = lanes_ref.shape[1]
    for i in range(nx // CHUNK):
        part = slice(i * CHUNK, (i + 1) * CHUNK)
        fz_ref[0, i] = row_of(lanes_ref[0, part], slice(0, 128))[0:1]
        fz_ref[1, i] = row_of(lanes_ref[1, part], slice(0, 128))[0:1]


def lower_faces_of(e):
    _, nx, ny, nz = e.shape
    face_y, face_z = pl.pallas_call(
    faces_kernel,
    grid=(1,),
    in_specs=[
        pl.BlockSpec((3, nx, 8, nz), lambda i: (0, 0, 0, 0)),
        pl.BlockSpec((2, nx, ny, 128), lambda i: (0, 0, 0, 0)),
    ],
    out_specs=[
        pl.BlockSpec((2, nx, 1, nz), lambda i: (0, 0, 0, 0)),
        pl.BlockSpec((2, nx // CHUNK, 1, CHUNK * ny), lambda i: (0, 0, 0, 0)),
    ],
    out_shape=face_shapes(nx, ny, nz, e.dtype)[1:],
    )(e, e)
    return e[1:3, 0:1], face_y, face_z


def h_step(e, h, faces):
    _, nx, ny, nz = e.shape
    chunk = CHUNK
    faces_x = toward_lower(faces[0], "gx")
    faces_y = toward_lower(faces[1], "gy")
    faces_z = toward_lower(faces[2], "gz")
    return pl.pallas_call(
        h_kernel,
        grid=(nx // chunk,),
        in_specs=[
            field_spec(ny, nz, chunk),
            pl.BlockSpec((3, 1, ny, nz), lambda i: (0, jnp.minimum((i + 1) * chunk, nx - 1), 0, 0)),
            field_spec(ny, nz, chunk),
            pl.BlockSpec((2, 1, ny, nz), lambda i: (0, 0, 0, 0)),
            pl.BlockSpec((2, chunk, 1, nz), lambda i: (0, i, 0, 0)),
            pl.BlockSpec((2, 1, 1, chunk * ny), lambda i: (0, i, 0, 0)),
        ],
        out_specs=[field_spec(ny, nz, chunk)] + face_specs(ny, nz, chunk),
        out_shape=[jax.ShapeDtypeStruct(h.shape, h.dtype)] + face_shapes(nx, ny, nz, h.dtype),
    )(e, e, h, faces_x, faces_y, faces_z)


def e_step(e, h, faces, inv, ef=None, cells=None, owners=None, slots=None, devices=None):
    _, nx, ny, nz = e.shape
    chunk = CHUNK
    faces_x = toward_upper(faces[0], "gx")
    faces_y = toward_upper(faces[1], "gy")
    faces_z = toward_upper(faces[2], "gz")
    in_specs = [
        field_spec(ny, nz, chunk),
        field_spec(ny, nz, chunk),
        pl.BlockSpec((3, 1, ny, nz), lambda i: (0, jnp.maximum(i * chunk - 1, 0), 0, 0)),
        pl.BlockSpec((chunk, ny, nz), lambda i: (i, 0, 0)),
        pl.BlockSpec((2, 1, ny, nz), lambda i: (0, 0, 0, 0)),
        pl.BlockSpec((2, chunk, 1, nz), lambda i: (0, i, 0, 0)),
        pl.BlockSpec((2, 1, 1, chunk * ny), lambda i: (0, i, 0, 0)),
    ]
    args = [e, h, h, inv, faces_x, faces_y, faces_z]
    if ef is None:
        outs = pl.pallas_call(
            e_kernel,
            grid=(nx // chunk,),
            in_specs=in_specs,
            out_specs=[field_spec(ny, nz, chunk)] + face_specs(ny, nz, chunk),
            out_shape=[jax.ShapeDtypeStruct(e.shape, e.dtype)] + face_shapes(nx, ny, nz, e.dtype),
        )(*args)
        return outs[0], outs[1:]
    count = cells.shape[0]
    zrow = (cells % nz).reshape(1, count)
    rrow = (cells // nz).reshape(1, count)
    return pl.pallas_call(
        e_last_kernel,
        grid=(nx // chunk,),
        in_specs=in_specs
        + [
            field_spec(ny, nz, chunk),
            pl.BlockSpec((1, count), lambda i: (0, 0)),
            pl.BlockSpec((1, count), lambda i: (0, 0)),
            pl.BlockSpec((1, count), lambda i: (0, 0)),
            pl.BlockSpec((1, count), lambda i: (0, 0)),
        ],
        out_specs=[field_spec(ny, nz, chunk), pl.BlockSpec((devices, 1, P_DEV), lambda i: (0, 0, 0))],
        out_shape=[jax.ShapeDtypeStruct(e.shape, e.dtype), jax.ShapeDtypeStruct((devices, 1, P_DEV), jnp.float32)],
        scratch_shapes=[pltpu.VMEM((1, count), jnp.float32), pltpu.VMEM((nz, count), jnp.bfloat16)],
    )(*args, ef, zrow, rrow, owners.reshape(1, count), slots.reshape(1, count))


def body(e_forward, e_adjoint, h_adjoint, inv_perm, voxel_cell, voxel_owner, voxel_slot):
    count = voxel_cell.shape[-1]
    voxel_rows = voxel_cell.reshape(count)
    owners = voxel_owner.reshape(count)
    slot_ids = voxel_slot.reshape(count)
    devices = lax.axis_size("gx") * lax.axis_size("gy") * lax.axis_size("gz")
    e, h = e_adjoint, h_adjoint
    per_owner = None
    e_faces = lower_faces_of(e)
    h, *h_faces = h_step(e, h, e_faces)
    for repeat in range(STEPS):
        if repeat > 0:
            h, *h_faces = h_step(e, h, e_faces)
        if repeat == STEPS - 1:
            e, per_owner = e_step(e, h, h_faces, inv_perm, e_forward, voxel_rows, owners, slot_ids, devices)
        else:
            e, e_faces = e_step(e, h, h_faces, inv_perm)
    received = lax.all_to_all(per_owner, ("gx", "gy", "gz"), 0, 0, tiled=True)
    gradient = received.sum(axis=(0, 1))
    return (e, h, gradient)


def solution(mesh):
    return jax.shard_map(
        body,
        mesh=mesh,
        in_specs=(
            P(None, "gx", "gy", "gz"),
            P(None, "gx", "gy", "gz"),
            P(None, "gx", "gy", "gz"),
            P("gx", "gy", "gz"),
            P("gx", "gy", "gz", None),
            P("gx", "gy", "gz", None, None),
            P("gx", "gy", "gz", None),
        ),
        out_specs=(P(None, "gx", "gy", "gz"), P(None, "gx", "gy", "gz"), P(("gx", "gy", "gz"))),
        check_vma=False,
    )
```

```python
import functools

import jax
import jax.numpy as jnp
from jax import lax
from jax.experimental import pallas as pl
from jax.experimental.pallas import tpu as pltpu
from jax.sharding import PartitionSpec as P

STEPS = 2
P_DEV = 256
CHUNK = 8

courant = 0.5


def toward_lower(x, axis):
    peers = lax.axis_size(axis)
    return lax.ppermute(x, axis, [(j, j - 1) for j in range(1, peers)])


def toward_upper(x, axis):
    peers = lax.axis_size(axis)
    return lax.ppermute(x, axis, [(j, j + 1) for j in range(peers - 1)])


def fwd_y(a, row):
    rolled = pltpu.roll(a, a.shape[-2] - 1, a.ndim - 2)
    at = lax.broadcasted_iota(jnp.int32, a.shape, a.ndim - 2)
    return jnp.where(at == a.shape[-2] - 1, row, rolled)


def fwd_z(a, col):
    rolled = pltpu.roll(a, a.shape[-1] - 1, a.ndim - 1)
    at = lax.broadcasted_iota(jnp.int32, a.shape, a.ndim - 1)
    return jnp.where(at == a.shape[-1] - 1, col, rolled)


def bwd_y(a, row):
    rolled = pltpu.roll(a, 1, a.ndim - 2)
    at = lax.broadcasted_iota(jnp.int32, a.shape, a.ndim - 2)
    return jnp.where(at == 0, row, rolled)


def bwd_z(a, col):
    rolled = pltpu.roll(a, 1, a.ndim - 1)
    at = lax.broadcasted_iota(jnp.int32, a.shape, a.ndim - 1)
    return jnp.where(at == 0, col, rolled)


def column_of(row, b, ny):
    tile = jnp.broadcast_to(row, (128, b * ny))
    return jnp.transpose(tile).reshape(b, ny, 128)[:, :, 0:1]


def row_of(a, lanes):
    b, ny, _ = a.shape
    tile = jnp.transpose(a[:, :, lanes].reshape(b * ny, 128))
    return tile


def fwd_x(a, nxt):
    if a.shape[0] == 1:
        return nxt
    return jnp.concatenate([a[1:], nxt], axis=0)


def bwd_x(a, prv):
    if a.shape[0] == 1:
        return prv
    return jnp.concatenate([prv, a[:-1]], axis=0)


def h_kernel(e_ref, en_ref, h_ref, hx_ref, hy_ref, hz_ref, out_ref, fx_ref, fy_ref, fz_ref):
    last = pl.program_id(0) == pl.num_programs(0) - 1
    _, b, ny, nz = e_ref.shape
    nxt_y = jnp.where(last, hx_ref[0], en_ref[1])
    nxt_z = jnp.where(last, hx_ref[1], en_ref[2])
    col_x = column_of(hz_ref[0, 0], b, ny)
    col_y = column_of(hz_ref[1, 0], b, ny)
    for j in range(b):
        ex, ey, ez = e_ref[0, j], e_ref[1, j], e_ref[2, j]
        ey_xp = e_ref[1, j + 1] if j + 1 < b else nxt_y[0]
        ez_xp = e_ref[2, j + 1] if j + 1 < b else nxt_z[0]
        ez_yp = fwd_y(ez, hy_ref[1, j])
        ex_yp = fwd_y(ex, hy_ref[0, j])
        ey_zp = fwd_z(ey, col_y[j])
        ex_zp = fwd_z(ex, col_x[j])
        out_ref[0, j] = h_ref[0, j] - courant * ((ez_yp - ez) - (ey_zp - ey))
        out_ref[1, j] = h_ref[1, j] - courant * ((ex_zp - ex) - (ez_xp - ez))
        out_ref[2, j] = h_ref[2, j] - courant * ((ey_xp - ey) - (ex_yp - ex))

    @pl.when(last)
    def _():
        fx_ref[0] = out_ref[1, b - 1:b]
        fx_ref[1] = out_ref[2, b - 1:b]

    fy_ref[0] = out_ref[0, :, ny - 1:ny, :]
    fy_ref[1] = out_ref[2, :, ny - 1:ny, :]
    top = slice(nz - 128, nz)
    fz_ref[0, 0] = row_of(out_ref[0], top)[127:128]
    fz_ref[1, 0] = row_of(out_ref[1], top)[127:128]


def e_slabs(e_ref, h_ref, hp_ref, inv_ref, hx_ref, hy_ref, hz_ref, out_ref):
    first = pl.program_id(0) == 0
    _, b, ny, nz = h_ref.shape
    prv_y = jnp.where(first, hx_ref[0], hp_ref[1])
    prv_z = jnp.where(first, hx_ref[1], hp_ref[2])
    col_x = column_of(hz_ref[0, 0], b, ny)
    col_y = column_of(hz_ref[1, 0], b, ny)
    for j in range(b):
        hx, hy, hz = h_ref[0, j], h_ref[1, j], h_ref[2, j]
        hz_xm = h_ref[2, j - 1] if j > 0 else prv_z[0]
        hy_xm = h_ref[1, j - 1] if j > 0 else prv_y[0]
        hz_ym = bwd_y(hz, hy_ref[1, j])
        hx_ym = bwd_y(hx, hy_ref[0, j])
        hy_zm = bwd_z(hy, col_y[j])
        hx_zm = bwd_z(hx, col_x[j])
        scale = courant * inv_ref[j]
        out_ref[0, j] = e_ref[0, j] + scale * ((hz - hz_ym) - (hy - hy_zm))
        out_ref[1, j] = e_ref[1, j] + scale * ((hx - hx_zm) - (hz - hz_xm))
        out_ref[2, j] = e_ref[2, j] + scale * ((hy - hy_xm) - (hx - hx_ym))


def e_kernel(e_ref, h_ref, hp_ref, inv_ref, hx_ref, hy_ref, hz_ref, out_ref, fx_ref, fy_ref, fz_ref):
    e_slabs(e_ref, h_ref, hp_ref, inv_ref, hx_ref, hy_ref, hz_ref, out_ref)

    @pl.when(pl.program_id(0) == 0)
    def _():
        fx_ref[0] = out_ref[1, 0:1]
        fx_ref[1] = out_ref[2, 0:1]

    fy_ref[0] = out_ref[0, :, 0:1, :]
    fy_ref[1] = out_ref[2, :, 0:1, :]
    fz_ref[0, 0] = row_of(out_ref[0], slice(0, 128))[0:1]
    fz_ref[1, 0] = row_of(out_ref[1], slice(0, 128))[0:1]


def split3(a):
    hi = a.astype(jnp.bfloat16)
    rest = a - hi.astype(jnp.float32)
    mid = rest.astype(jnp.bfloat16)
    lo = (rest - mid.astype(jnp.float32)).astype(jnp.bfloat16)
    return hi, mid, lo


def e_last_kernel(
    e_ref, h_ref, hp_ref, inv_ref, hx_ref, hy_ref, hz_ref, ef_ref, zrow_ref, rrow_ref, orow_ref, srow_ref,
    out_ref, owner_ref, terms_ref, zhot_ref
):
    e_slabs(e_ref, h_ref, hp_ref, inv_ref, hx_ref, hy_ref, hz_ref, out_ref)
    new_x, new_y, new_z = out_ref[0], out_ref[1], out_ref[2]
    step = pl.program_id(0)
    b, ny, nz = new_x.shape

    count = zhot_ref.shape[0]

    @pl.when(step == 0)
    def _():
        zhot_ref[...] = (lax.broadcasted_iota(jnp.int32, (count, nz), 1) == zrow_ref[...]).astype(jnp.bfloat16)
        terms_ref[...] = jnp.zeros_like(terms_ref)

    inter = (ef_ref[0] * new_x + ef_ref[1] * new_y + ef_ref[2] * new_z).reshape(b * ny, nz)
    hi = inter.astype(jnp.bfloat16)
    mid = (inter - hi.astype(jnp.float32)).astype(jnp.bfloat16)
    zhot = zhot_ref[...]
    nt = (((1,), (1,)), ((), ()))
    picked = lax.dot_general(zhot, hi, nt, preferred_element_type=jnp.float32) + lax.dot_general(
        zhot, mid, nt, preferred_element_type=jnp.float32
    )
    row_at = step * (b * ny) + lax.broadcasted_iota(jnp.int32, picked.shape, 1)
    terms_ref[...] += jnp.sum(jnp.where(row_at == rrow_ref[...], picked, 0.0), axis=1, keepdims=True)

    @pl.when(step == pl.num_programs(0) - 1)
    def _():
        owners, _, slots = owner_ref.shape
        terms_row = jnp.transpose(jnp.broadcast_to(terms_ref[...], (count, 128)))[0:1]
        weighted = jnp.where(
            lax.broadcasted_iota(jnp.int32, (owners, count), 0) == orow_ref[...], terms_row, 0.0
        )
        slot_hot = (lax.broadcasted_iota(jnp.int32, (slots, count), 0) == srow_ref[...]).astype(jnp.bfloat16)
        hi, mid, lo = split3(weighted)
        nt = (((1,), (1,)), ((), ()))
        summed = (
            lax.dot_general(hi, slot_hot, nt, preferred_element_type=jnp.float32)
            + lax.dot_general(mid, slot_hot, nt, preferred_element_type=jnp.float32)
        ) + lax.dot_general(lo, slot_hot, nt, preferred_element_type=jnp.float32)
        owner_ref[...] = summed.reshape(owners, 1, slots)


def field_spec(nx, ny, nz, chunk):
    return pl.BlockSpec((3, chunk, ny, nz), lambda i: (0, i, 0, 0))


def face_specs(nx, ny, nz, chunk):
    return [
        pl.BlockSpec((2, 1, ny, nz), lambda i: (0, 0, 0, 0)),
        pl.BlockSpec((2, chunk, 1, nz), lambda i: (0, i, 0, 0)),
        pl.BlockSpec((2, 1, 1, chunk * ny), lambda i: (0, i, 0, 0)),
    ]


def face_shapes(nx, ny, nz, dtype):
    return [
        jax.ShapeDtypeStruct((2, 1, ny, nz), dtype),
        jax.ShapeDtypeStruct((2, nx, 1, nz), dtype),
        jax.ShapeDtypeStruct((2, nx // CHUNK, 1, CHUNK * ny), dtype),
    ]


def faces_kernel(slab_ref, rows_ref, lanes_ref, fx_ref, fy_ref, fz_ref):
    fx_ref[0] = slab_ref[1]
    fx_ref[1] = slab_ref[2]
    fy_ref[0] = rows_ref[0, :, 0:1, :]
    fy_ref[1] = rows_ref[2, :, 0:1, :]
    nx = lanes_ref.shape[1]
    for i in range(nx // CHUNK):
        part = slice(i * CHUNK, (i + 1) * CHUNK)
        fz_ref[0, i] = row_of(lanes_ref[0, part], slice(0, 128))[0:1]
        fz_ref[1, i] = row_of(lanes_ref[1, part], slice(0, 128))[0:1]


def lower_faces_of(e):
    _, nx, ny, nz = e.shape
    return pl.pallas_call(
        faces_kernel,
        grid=(1,),
        in_specs=[
            pl.BlockSpec((3, 1, ny, nz), lambda i: (0, 0, 0, 0)),
            pl.BlockSpec((3, nx, 8, nz), lambda i: (0, 0, 0, 0)),
            pl.BlockSpec((3, nx, ny, 128), lambda i: (0, 0, 0, 0)),
        ],
        out_specs=[
            pl.BlockSpec((2, 1, ny, nz), lambda i: (0, 0, 0, 0)),
            pl.BlockSpec((2, nx, 1, nz), lambda i: (0, 0, 0, 0)),
            pl.BlockSpec((2, nx // CHUNK, 1, CHUNK * ny), lambda i: (0, 0, 0, 0)),
        ],
        out_shape=face_shapes(nx, ny, nz, e.dtype),
    )(e, e, e)


def h_step(e, h, faces):
    _, nx, ny, nz = e.shape
    chunk = CHUNK
    faces_x = toward_lower(faces[0], "gx")
    faces_y = toward_lower(faces[1], "gy")
    faces_z = toward_lower(faces[2], "gz")
    return pl.pallas_call(
        h_kernel,
        grid=(nx // chunk,),
        in_specs=[
            field_spec(nx, ny, nz, chunk),
            pl.BlockSpec((3, 1, ny, nz), lambda i: (0, jnp.minimum((i + 1) * chunk, nx - 1), 0, 0)),
            field_spec(nx, ny, nz, chunk),
            pl.BlockSpec((2, 1, ny, nz), lambda i: (0, 0, 0, 0)),
            pl.BlockSpec((2, chunk, 1, nz), lambda i: (0, i, 0, 0)),
            pl.BlockSpec((2, 1, 1, chunk * ny), lambda i: (0, i, 0, 0)),
        ],
        out_specs=[field_spec(nx, ny, nz, chunk)] + face_specs(nx, ny, nz, chunk),
        out_shape=[jax.ShapeDtypeStruct(h.shape, h.dtype)] + face_shapes(nx, ny, nz, h.dtype),
    )(e, e, h, faces_x, faces_y, faces_z)


def e_step(e, h, faces, inv, ef=None, cells=None, owners=None, slots=None, devices=None):
    _, nx, ny, nz = e.shape
    chunk = CHUNK
    faces_x = toward_upper(faces[0], "gx")
    faces_y = toward_upper(faces[1], "gy")
    faces_z = toward_upper(faces[2], "gz")
    in_specs = [
        field_spec(nx, ny, nz, chunk),
        field_spec(nx, ny, nz, chunk),
        pl.BlockSpec((3, 1, ny, nz), lambda i: (0, jnp.maximum(i * chunk - 1, 0), 0, 0)),
        pl.BlockSpec((chunk, ny, nz), lambda i: (i, 0, 0)),
        pl.BlockSpec((2, 1, ny, nz), lambda i: (0, 0, 0, 0)),
        pl.BlockSpec((2, chunk, 1, nz), lambda i: (0, i, 0, 0)),
        pl.BlockSpec((2, 1, 1, chunk * ny), lambda i: (0, i, 0, 0)),
    ]
    args = [e, h, h, inv, faces_x, faces_y, faces_z]
    if ef is None:
        outs = pl.pallas_call(
            e_kernel,
            grid=(nx // chunk,),
            in_specs=in_specs,
            out_specs=[field_spec(nx, ny, nz, chunk)] + face_specs(nx, ny, nz, chunk),
            out_shape=[jax.ShapeDtypeStruct(e.shape, e.dtype)] + face_shapes(nx, ny, nz, e.dtype),
        )(*args)
        return outs[0], outs[1:]
    count = cells.shape[0]
    zrow = (cells % nz).reshape(count, 1)
    rrow = (cells // nz).reshape(count, 1)
    return pl.pallas_call(
        e_last_kernel,
        grid=(nx // chunk,),
        in_specs=in_specs
        + [
            field_spec(nx, ny, nz, chunk),
            pl.BlockSpec((count, 1), lambda i: (0, 0)),
            pl.BlockSpec((count, 1), lambda i: (0, 0)),
            pl.BlockSpec((1, count), lambda i: (0, 0)),
            pl.BlockSpec((1, count), lambda i: (0, 0)),
        ],
        out_specs=[field_spec(nx, ny, nz, chunk), pl.BlockSpec((devices, 1, P_DEV), lambda i: (0, 0, 0))],
        out_shape=[jax.ShapeDtypeStruct(e.shape, e.dtype), jax.ShapeDtypeStruct((devices, 1, P_DEV), jnp.float32)],
        scratch_shapes=[pltpu.VMEM((count, 1), jnp.float32), pltpu.VMEM((count, nz), jnp.bfloat16)],
    )(*args, ef, zrow, rrow, owners.reshape(1, count), slots.reshape(1, count))


def body(e_forward, e_adjoint, h_adjoint, inv_perm, voxel_cell, voxel_owner, voxel_slot):
    count = voxel_cell.shape[-1]
    voxel_rows = voxel_cell.reshape(count)
    owners = voxel_owner.reshape(count)
    slot_ids = voxel_slot.reshape(count)
    devices = lax.axis_size("gx") * lax.axis_size("gy") * lax.axis_size("gz")
    e, h = e_adjoint, h_adjoint
    e_faces = lower_faces_of(e)
    per_owner = None
    for repeat in range(STEPS):
        h, *h_faces = h_step(e, h, e_faces)
        if repeat == STEPS - 1:
            e, per_owner = e_step(e, h, h_faces, inv_perm, e_forward, voxel_rows, owners, slot_ids, devices)
        else:
            e, e_faces = e_step(e, h, h_faces, inv_perm)
    received = lax.all_to_all(per_owner, ("gx", "gy", "gz"), 0, 0, tiled=True)
    gradient = received.sum(axis=(0, 1))
    return (e, h, gradient)


def solution(mesh):
    return jax.shard_map(
        body,
        mesh=mesh,
        in_specs=(
            P(None, "gx", "gy", "gz"),
            P(None, "gx", "gy", "gz"),
            P(None, "gx", "gy", "gz"),
            P("gx", "gy", "gz"),
            P("gx", "gy", "gz", None),
            P("gx", "gy", "gz", None, None),
            P("gx", "gy", "gz", None),
        ),
        out_specs=(P(None, "gx", "gy", "gz"), P(None, "gx", "gy", "gz"), P(("gx", "gy", "gz"))),
        check_vma=False,
    )
```

```python
import functools

import jax
import jax.numpy as jnp
from jax import lax
from jax.experimental import pallas as pl
from jax.experimental.pallas import tpu as pltpu
from jax.sharding import PartitionSpec as P

STEPS = 2
P_DEV = 256
CHUNK = 8

courant = 0.5


def toward_lower(x, axis):
    peers = lax.axis_size(axis)
    return lax.ppermute(x, axis, [(j, j - 1) for j in range(1, peers)])


def toward_upper(x, axis):
    peers = lax.axis_size(axis)
    return lax.ppermute(x, axis, [(j, j + 1) for j in range(peers - 1)])


def fwd_y(a, row):
    rolled = pltpu.roll(a, a.shape[-2] - 1, a.ndim - 2)
    at = lax.broadcasted_iota(jnp.int32, a.shape, a.ndim - 2)
    return jnp.where(at == a.shape[-2] - 1, row, rolled)


def fwd_z(a, col):
    rolled = pltpu.roll(a, a.shape[-1] - 1, a.ndim - 1)
    at = lax.broadcasted_iota(jnp.int32, a.shape, a.ndim - 1)
    return jnp.where(at == a.shape[-1] - 1, col, rolled)


def bwd_y(a, row):
    rolled = pltpu.roll(a, 1, a.ndim - 2)
    at = lax.broadcasted_iota(jnp.int32, a.shape, a.ndim - 2)
    return jnp.where(at == 0, row, rolled)


def bwd_z(a, col):
    rolled = pltpu.roll(a, 1, a.ndim - 1)
    at = lax.broadcasted_iota(jnp.int32, a.shape, a.ndim - 1)
    return jnp.where(at == 0, col, rolled)


def column_of(row, b, ny):
    tile = jnp.broadcast_to(row, (128, b * ny))
    return jnp.transpose(tile).reshape(b, ny, 128)[:, :, 0:1]


def row_of(a, lanes):
    b, ny, _ = a.shape
    tile = jnp.transpose(a[:, :, lanes].reshape(b * ny, 128))
    return tile


def fwd_x(a, nxt):
    if a.shape[0] == 1:
        return nxt
    return jnp.concatenate([a[1:], nxt], axis=0)


def bwd_x(a, prv):
    if a.shape[0] == 1:
        return prv
    return jnp.concatenate([prv, a[:-1]], axis=0)


def h_kernel(e_ref, en_ref, h_ref, hx_ref, hy_ref, hz_ref, out_ref, fx_ref, fy_ref, fz_ref):
    last = pl.program_id(0) == pl.num_programs(0) - 1
    _, b, ny, nz = e_ref.shape
    nxt_y = jnp.where(last, hx_ref[0], en_ref[1])
    nxt_z = jnp.where(last, hx_ref[1], en_ref[2])
    col_x = column_of(hz_ref[0, 0], b, ny)
    col_y = column_of(hz_ref[1, 0], b, ny)
    for j in range(b):
        ex, ey, ez = e_ref[0, j], e_ref[1, j], e_ref[2, j]
        ey_xp = e_ref[1, j + 1] if j + 1 < b else nxt_y[0]
        ez_xp = e_ref[2, j + 1] if j + 1 < b else nxt_z[0]
        ez_yp = fwd_y(ez, hy_ref[1, j])
        ex_yp = fwd_y(ex, hy_ref[0, j])
        ey_zp = fwd_z(ey, col_y[j])
        ex_zp = fwd_z(ex, col_x[j])
        out_ref[0, j] = h_ref[0, j] - courant * ((ez_yp - ez) - (ey_zp - ey))
        out_ref[1, j] = h_ref[1, j] - courant * ((ex_zp - ex) - (ez_xp - ez))
        out_ref[2, j] = h_ref[2, j] - courant * ((ey_xp - ey) - (ex_yp - ex))

    @pl.when(last)
    def _():
        fx_ref[0] = out_ref[1, b - 1:b]
        fx_ref[1] = out_ref[2, b - 1:b]

    fy_ref[0] = out_ref[0, :, ny - 1:ny, :]
    fy_ref[1] = out_ref[2, :, ny - 1:ny, :]
    top = slice(nz - 128, nz)
    fz_ref[0, 0] = row_of(out_ref[0], top)[127:128]
    fz_ref[1, 0] = row_of(out_ref[1], top)[127:128]


def e_slabs(e_ref, h_ref, hp_ref, inv_ref, hx_ref, hy_ref, hz_ref, out_ref):
    first = pl.program_id(0) == 0
    _, b, ny, nz = h_ref.shape
    prv_y = jnp.where(first, hx_ref[0], hp_ref[1])
    prv_z = jnp.where(first, hx_ref[1], hp_ref[2])
    col_x = column_of(hz_ref[0, 0], b, ny)
    col_y = column_of(hz_ref[1, 0], b, ny)
    for j in range(b):
        hx, hy, hz = h_ref[0, j], h_ref[1, j], h_ref[2, j]
        hz_xm = h_ref[2, j - 1] if j > 0 else prv_z[0]
        hy_xm = h_ref[1, j - 1] if j > 0 else prv_y[0]
        hz_ym = bwd_y(hz, hy_ref[1, j])
        hx_ym = bwd_y(hx, hy_ref[0, j])
        hy_zm = bwd_z(hy, col_y[j])
        hx_zm = bwd_z(hx, col_x[j])
        scale = courant * inv_ref[j]
        out_ref[0, j] = e_ref[0, j] + scale * ((hz - hz_ym) - (hy - hy_zm))
        out_ref[1, j] = e_ref[1, j] + scale * ((hx - hx_zm) - (hz - hz_xm))
        out_ref[2, j] = e_ref[2, j] + scale * ((hy - hy_xm) - (hx - hx_ym))


def e_kernel(e_ref, h_ref, hp_ref, inv_ref, hx_ref, hy_ref, hz_ref, out_ref, fx_ref, fy_ref, fz_ref):
    e_slabs(e_ref, h_ref, hp_ref, inv_ref, hx_ref, hy_ref, hz_ref, out_ref)

    @pl.when(pl.program_id(0) == 0)
    def _():
        fx_ref[0] = out_ref[1, 0:1]
        fx_ref[1] = out_ref[2, 0:1]

    fy_ref[0] = out_ref[0, :, 0:1, :]
    fy_ref[1] = out_ref[2, :, 0:1, :]
    fz_ref[0, 0] = row_of(out_ref[0], slice(0, 128))[0:1]
    fz_ref[1, 0] = row_of(out_ref[1], slice(0, 128))[0:1]


def split3(a):
    hi = a.astype(jnp.bfloat16)
    rest = a - hi.astype(jnp.float32)
    mid = rest.astype(jnp.bfloat16)
    lo = (rest - mid.astype(jnp.float32)).astype(jnp.bfloat16)
    return hi, mid, lo


def e_last_kernel(
    e_ref, h_ref, hp_ref, inv_ref, hx_ref, hy_ref, hz_ref, ef_ref, zrow_ref, rrow_ref, orow_ref, srow_ref,
    out_ref, owner_ref, terms_ref, zhot_ref
):
    e_slabs(e_ref, h_ref, hp_ref, inv_ref, hx_ref, hy_ref, hz_ref, out_ref)
    new_x, new_y, new_z = out_ref[0], out_ref[1], out_ref[2]
    step = pl.program_id(0)
    b, ny, nz = new_x.shape
    count = zhot_ref.shape[1]

    @pl.when(step == 0)
    def _():
        zhot_ref[...] = (lax.broadcasted_iota(jnp.int32, (nz, count), 0) == zrow_ref[...]).astype(jnp.bfloat16)
        terms_ref[...] = jnp.zeros_like(terms_ref)

    inter = (ef_ref[0] * new_x + ef_ref[1] * new_y + ef_ref[2] * new_z).reshape(b * ny, nz)
    hi = inter.astype(jnp.bfloat16)
    mid = (inter - hi.astype(jnp.float32)).astype(jnp.bfloat16)
    zhot = zhot_ref[...]
    picked = jnp.dot(hi, zhot, preferred_element_type=jnp.float32) + jnp.dot(mid, zhot, preferred_element_type=jnp.float32)
    row_at = step * (b * ny) + lax.broadcasted_iota(jnp.int32, picked.shape, 0)
    terms_ref[...] += jnp.sum(jnp.where(row_at == rrow_ref[...], picked, 0.0), axis=0, keepdims=True)

    @pl.when(step == pl.num_programs(0) - 1)
    def _():
        owners, _, slots = owner_ref.shape
        weighted = jnp.where(
            lax.broadcasted_iota(jnp.int32, (owners, count), 0) == orow_ref[...], terms_ref[...], 0.0
        )
        slot_hot = (lax.broadcasted_iota(jnp.int32, (slots, count), 0) == srow_ref[...]).astype(jnp.bfloat16)
        hi, mid, lo = split3(weighted)
        nt = (((1,), (1,)), ((), ()))
        summed = (
            lax.dot_general(hi, slot_hot, nt, preferred_element_type=jnp.float32)
            + lax.dot_general(mid, slot_hot, nt, preferred_element_type=jnp.float32)
        ) + lax.dot_general(lo, slot_hot, nt, preferred_element_type=jnp.float32)
        owner_ref[...] = summed.reshape(owners, 1, slots)


def field_spec(nx, ny, nz, chunk):
    return pl.BlockSpec((3, chunk, ny, nz), lambda i: (0, i, 0, 0))


def face_specs(nx, ny, nz, chunk):
    return [
        pl.BlockSpec((2, 1, ny, nz), lambda i: (0, 0, 0, 0)),
        pl.BlockSpec((2, chunk, 1, nz), lambda i: (0, i, 0, 0)),
        pl.BlockSpec((2, 1, 1, chunk * ny), lambda i: (0, i, 0, 0)),
    ]


def face_shapes(nx, ny, nz, dtype):
    return [
        jax.ShapeDtypeStruct((2, 1, ny, nz), dtype),
        jax.ShapeDtypeStruct((2, nx, 1, nz), dtype),
        jax.ShapeDtypeStruct((2, nx // CHUNK, 1, CHUNK * ny), dtype),
    ]


def faces_kernel(slab_y_ref, slab_z_ref, rows_x_ref, rows_z_ref, lanes_ref, fx_ref, fy_ref, fz_ref):
    fx_ref[0] = slab_y_ref[0]
    fx_ref[1] = slab_z_ref[0]
    fy_ref[0] = rows_x_ref[0, :, 0:1, :]
    fy_ref[1] = rows_z_ref[0, :, 0:1, :]
    nx = lanes_ref.shape[1]
    for i in range(nx // CHUNK):
        part = slice(i * CHUNK, (i + 1) * CHUNK)
        fz_ref[0, i] = row_of(lanes_ref[0, part], slice(0, 128))[0:1]
        fz_ref[1, i] = row_of(lanes_ref[1, part], slice(0, 128))[0:1]


def lower_faces_of(e):
    _, nx, ny, nz = e.shape
    return pl.pallas_call(
        faces_kernel,
        grid=(1,),
        in_specs=[
            pl.BlockSpec((1, 1, ny, nz), lambda i: (1, 0, 0, 0)),
            pl.BlockSpec((1, 1, ny, nz), lambda i: (2, 0, 0, 0)),
            pl.BlockSpec((1, nx, 8, nz), lambda i: (0, 0, 0, 0)),
            pl.BlockSpec((1, nx, 8, nz), lambda i: (2, 0, 0, 0)),
            pl.BlockSpec((2, nx, ny, 128), lambda i: (0, 0, 0, 0)),
        ],
        out_specs=[
            pl.BlockSpec((2, 1, ny, nz), lambda i: (0, 0, 0, 0)),
            pl.BlockSpec((2, nx, 1, nz), lambda i: (0, 0, 0, 0)),
            pl.BlockSpec((2, nx // CHUNK, 1, CHUNK * ny), lambda i: (0, 0, 0, 0)),
        ],
        out_shape=face_shapes(nx, ny, nz, e.dtype),
    )(e, e, e, e, e)


def h_step(e, h, faces):
    _, nx, ny, nz = e.shape
    chunk = CHUNK
    faces_x = toward_lower(faces[0], "gx")
    faces_y = toward_lower(faces[1], "gy")
    faces_z = toward_lower(faces[2], "gz")
    return pl.pallas_call(
        h_kernel,
        grid=(nx // chunk,),
        in_specs=[
            field_spec(nx, ny, nz, chunk),
            pl.BlockSpec((3, 1, ny, nz), lambda i: (0, jnp.minimum((i + 1) * chunk, nx - 1), 0, 0)),
            field_spec(nx, ny, nz, chunk),
            pl.BlockSpec((2, 1, ny, nz), lambda i: (0, 0, 0, 0)),
            pl.BlockSpec((2, chunk, 1, nz), lambda i: (0, i, 0, 0)),
            pl.BlockSpec((2, 1, 1, chunk * ny), lambda i: (0, i, 0, 0)),
        ],
        out_specs=[field_spec(nx, ny, nz, chunk)] + face_specs(nx, ny, nz, chunk),
        out_shape=[jax.ShapeDtypeStruct(h.shape, h.dtype)] + face_shapes(nx, ny, nz, h.dtype),
    )(e, e, h, faces_x, faces_y, faces_z)


def e_step(e, h, faces, inv, ef=None, cells=None, owners=None, slots=None, devices=None):
    _, nx, ny, nz = e.shape
    chunk = CHUNK
    faces_x = toward_upper(faces[0], "gx")
    faces_y = toward_upper(faces[1], "gy")
    faces_z = toward_upper(faces[2], "gz")
    in_specs = [
        field_spec(nx, ny, nz, chunk),
        field_spec(nx, ny, nz, chunk),
        pl.BlockSpec((3, 1, ny, nz), lambda i: (0, jnp.maximum(i * chunk - 1, 0), 0, 0)),
        pl.BlockSpec((chunk, ny, nz), lambda i: (i, 0, 0)),
        pl.BlockSpec((2, 1, ny, nz), lambda i: (0, 0, 0, 0)),
        pl.BlockSpec((2, chunk, 1, nz), lambda i: (0, i, 0, 0)),
        pl.BlockSpec((2, 1, 1, chunk * ny), lambda i: (0, i, 0, 0)),
    ]
    args = [e, h, h, inv, faces_x, faces_y, faces_z]
    if ef is None:
        outs = pl.pallas_call(
            e_kernel,
            grid=(nx // chunk,),
            in_specs=in_specs,
            out_specs=[field_spec(nx, ny, nz, chunk)] + face_specs(nx, ny, nz, chunk),
            out_shape=[jax.ShapeDtypeStruct(e.shape, e.dtype)] + face_shapes(nx, ny, nz, e.dtype),
        )(*args)
        return outs[0], outs[1:]
    count = cells.shape[0]
    zrow = (cells % nz).reshape(1, count)
    rrow = (cells // nz).reshape(1, count)
    return pl.pallas_call(
        e_last_kernel,
        grid=(nx // chunk,),
        in_specs=in_specs
        + [
            field_spec(nx, ny, nz, chunk),
            pl.BlockSpec((1, count), lambda i: (0, 0)),
            pl.BlockSpec((1, count), lambda i: (0, 0)),
            pl.BlockSpec((1, count), lambda i: (0, 0)),
            pl.BlockSpec((1, count), lambda i: (0, 0)),
        ],
        out_specs=[field_spec(nx, ny, nz, chunk), pl.BlockSpec((devices, 1, P_DEV), lambda i: (0, 0, 0))],
        out_shape=[jax.ShapeDtypeStruct(e.shape, e.dtype), jax.ShapeDtypeStruct((devices, 1, P_DEV), jnp.float32)],
        scratch_shapes=[pltpu.VMEM((1, count), jnp.float32), pltpu.VMEM((nz, count), jnp.bfloat16)],
    )(*args, ef, zrow, rrow, owners.reshape(1, count), slots.reshape(1, count))


def body(e_forward, e_adjoint, h_adjoint, inv_perm, voxel_cell, voxel_owner, voxel_slot):
    count = voxel_cell.shape[-1]
    voxel_rows = voxel_cell.reshape(count)
    owners = voxel_owner.reshape(count)
    slot_ids = voxel_slot.reshape(count)
    devices = lax.axis_size("gx") * lax.axis_size("gy") * lax.axis_size("gz")
    e, h = e_adjoint, h_adjoint
    e_faces = lower_faces_of(e)
    per_owner = None
    for repeat in range(STEPS):
        h, *h_faces = h_step(e, h, e_faces)
        if repeat == STEPS - 1:
            e, per_owner = e_step(e, h, h_faces, inv_perm, e_forward, voxel_rows, owners, slot_ids, devices)
        else:
            e, e_faces = e_step(e, h, h_faces, inv_perm)
    received = lax.all_to_all(per_owner, ("gx", "gy", "gz"), 0, 0, tiled=True)
    gradient = received.sum(axis=(0, 1))
    return (e, h, gradient)


def solution(mesh):
    return jax.shard_map(
        body,
        mesh=mesh,
        in_specs=(
            P(None, "gx", "gy", "gz"),
            P(None, "gx", "gy", "gz"),
            P(None, "gx", "gy", "gz"),
            P("gx", "gy", "gz"),
            P("gx", "gy", "gz", None),
            P("gx", "gy", "gz", None, None),
            P("gx", "gy", "gz", None),
        ),
        out_specs=(P(None, "gx", "gy", "gz"), P(None, "gx", "gy", "gz"), P(("gx", "gy", "gz"))),
        check_vma=False,
    )
```

```python
import functools

import jax
import jax.numpy as jnp
from jax import lax
from jax.experimental import pallas as pl
from jax.experimental.pallas import tpu as pltpu
from jax.sharding import PartitionSpec as P

STEPS = 2
P_DEV = 256
CHUNK = 8

courant = 0.5


def toward_lower(x, axis):
    peers = lax.axis_size(axis)
    return lax.ppermute(x, axis, [(j, j - 1) for j in range(1, peers)])


def toward_upper(x, axis):
    peers = lax.axis_size(axis)
    return lax.ppermute(x, axis, [(j, j + 1) for j in range(peers - 1)])


def fwd_y(a, row):
    rolled = pltpu.roll(a, a.shape[-2] - 1, a.ndim - 2)
    at = lax.broadcasted_iota(jnp.int32, a.shape, a.ndim - 2)
    return jnp.where(at == a.shape[-2] - 1, row, rolled)


def fwd_z(a, col):
    rolled = pltpu.roll(a, a.shape[-1] - 1, a.ndim - 1)
    at = lax.broadcasted_iota(jnp.int32, a.shape, a.ndim - 1)
    return jnp.where(at == a.shape[-1] - 1, col, rolled)


def bwd_y(a, row):
    rolled = pltpu.roll(a, 1, a.ndim - 2)
    at = lax.broadcasted_iota(jnp.int32, a.shape, a.ndim - 2)
    return jnp.where(at == 0, row, rolled)


def bwd_z(a, col):
    rolled = pltpu.roll(a, 1, a.ndim - 1)
    at = lax.broadcasted_iota(jnp.int32, a.shape, a.ndim - 1)
    return jnp.where(at == 0, col, rolled)


def column_of(row, b, ny):
    tile = jnp.broadcast_to(row, (128, b * ny))
    return jnp.transpose(tile).reshape(b, ny, 128)[:, :, 0:1]


def row_of(a, lanes):
    b, ny, _ = a.shape
    tile = jnp.transpose(a[:, :, lanes].reshape(b * ny, 128))
    return tile


def fwd_x(a, nxt):
    if a.shape[0] == 1:
        return nxt
    return jnp.concatenate([a[1:], nxt], axis=0)


def bwd_x(a, prv):
    if a.shape[0] == 1:
        return prv
    return jnp.concatenate([prv, a[:-1]], axis=0)


def h_kernel(e_ref, en_ref, h_ref, hx_ref, hy_ref, hz_ref, out_ref, fx_ref, fy_ref, fz_ref):
    last = pl.program_id(0) == pl.num_programs(0) - 1
    _, b, ny, nz = e_ref.shape
    nxt_y = jnp.where(last, hx_ref[0], en_ref[1])
    nxt_z = jnp.where(last, hx_ref[1], en_ref[2])
    col_x = column_of(hz_ref[0, 0], b, ny)
    col_y = column_of(hz_ref[1, 0], b, ny)
    for j in range(b):
        ex, ey, ez = e_ref[0, j], e_ref[1, j], e_ref[2, j]
        ey_xp = e_ref[1, j + 1] if j + 1 < b else nxt_y[0]
        ez_xp = e_ref[2, j + 1] if j + 1 < b else nxt_z[0]
        ez_yp = fwd_y(ez, hy_ref[1, j])
        ex_yp = fwd_y(ex, hy_ref[0, j])
        ey_zp = fwd_z(ey, col_y[j])
        ex_zp = fwd_z(ex, col_x[j])
        out_ref[0, j] = h_ref[0, j] - courant * ((ez_yp - ez) - (ey_zp - ey))
        out_ref[1, j] = h_ref[1, j] - courant * ((ex_zp - ex) - (ez_xp - ez))
        out_ref[2, j] = h_ref[2, j] - courant * ((ey_xp - ey) - (ex_yp - ex))

    @pl.when(last)
    def _():
        fx_ref[0] = out_ref[1, b - 1:b]
        fx_ref[1] = out_ref[2, b - 1:b]

    fy_ref[0] = out_ref[0, :, ny - 1:ny, :]
    fy_ref[1] = out_ref[2, :, ny - 1:ny, :]
    top = slice(nz - 128, nz)
    fz_ref[0, 0] = row_of(out_ref[0], top)[127:128]
    fz_ref[1, 0] = row_of(out_ref[1], top)[127:128]


def e_slabs(e_ref, h_ref, hp_ref, inv_ref, hx_ref, hy_ref, hz_ref, out_ref):
    first = pl.program_id(0) == 0
    _, b, ny, nz = h_ref.shape
    prv_y = jnp.where(first, hx_ref[0], hp_ref[1])
    prv_z = jnp.where(first, hx_ref[1], hp_ref[2])
    col_x = column_of(hz_ref[0, 0], b, ny)
    col_y = column_of(hz_ref[1, 0], b, ny)
    for j in range(b):
        hx, hy, hz = h_ref[0, j], h_ref[1, j], h_ref[2, j]
        hz_xm = h_ref[2, j - 1] if j > 0 else prv_z[0]
        hy_xm = h_ref[1, j - 1] if j > 0 else prv_y[0]
        hz_ym = bwd_y(hz, hy_ref[1, j])
        hx_ym = bwd_y(hx, hy_ref[0, j])
        hy_zm = bwd_z(hy, col_y[j])
        hx_zm = bwd_z(hx, col_x[j])
        scale = courant * inv_ref[j]
        out_ref[0, j] = e_ref[0, j] + scale * ((hz - hz_ym) - (hy - hy_zm))
        out_ref[1, j] = e_ref[1, j] + scale * ((hx - hx_zm) - (hz - hz_xm))
        out_ref[2, j] = e_ref[2, j] + scale * ((hy - hy_xm) - (hx - hx_ym))


def e_kernel(e_ref, h_ref, hp_ref, inv_ref, hx_ref, hy_ref, hz_ref, out_ref, fx_ref, fy_ref, fz_ref):
    e_slabs(e_ref, h_ref, hp_ref, inv_ref, hx_ref, hy_ref, hz_ref, out_ref)

    @pl.when(pl.program_id(0) == 0)
    def _():
        fx_ref[0] = out_ref[1, 0:1]
        fx_ref[1] = out_ref[2, 0:1]

    fy_ref[0] = out_ref[0, :, 0:1, :]
    fy_ref[1] = out_ref[2, :, 0:1, :]
    fz_ref[0, 0] = row_of(out_ref[0], slice(0, 128))[0:1]
    fz_ref[1, 0] = row_of(out_ref[1], slice(0, 128))[0:1]


def split3(a):
    hi = a.astype(jnp.bfloat16)
    rest = a - hi.astype(jnp.float32)
    mid = rest.astype(jnp.bfloat16)
    lo = (rest - mid.astype(jnp.float32)).astype(jnp.bfloat16)
    return hi, mid, lo


def e_last_kernel(
    e_ref, h_ref, hp_ref, inv_ref, hx_ref, hy_ref, hz_ref, ef_ref, zrow_ref, rrow_ref, orow_ref, srow_ref,
    out_ref, owner_ref, terms_ref, zhot_ref
):
    e_slabs(e_ref, h_ref, hp_ref, inv_ref, hx_ref, hy_ref, hz_ref, out_ref)
    new_x, new_y, new_z = out_ref[0], out_ref[1], out_ref[2]
    step = pl.program_id(0)
    b, ny, nz = new_x.shape
    count = zhot_ref.shape[1]

    @pl.when(step == 0)
    def _():
        zhot_ref[...] = (lax.broadcasted_iota(jnp.int32, (nz, count), 0) == zrow_ref[...]).astype(jnp.bfloat16)
        terms_ref[...] = jnp.zeros_like(terms_ref)

    inter = (ef_ref[0] * new_x + ef_ref[1] * new_y + ef_ref[2] * new_z).reshape(b * ny, nz)
    hi = inter.astype(jnp.bfloat16)
    mid = (inter - hi.astype(jnp.float32)).astype(jnp.bfloat16)
    zhot = zhot_ref[...]
    picked = jnp.dot(hi, zhot, preferred_element_type=jnp.float32) + jnp.dot(mid, zhot, preferred_element_type=jnp.float32)
    row_at = step * (b * ny) + lax.broadcasted_iota(jnp.int32, picked.shape, 0)
    terms_ref[...] += jnp.sum(jnp.where(row_at == rrow_ref[...], picked, 0.0), axis=0, keepdims=True)

    @pl.when(step == pl.num_programs(0) - 1)
    def _():
        owners, _, slots = owner_ref.shape
        weighted = jnp.where(
            lax.broadcasted_iota(jnp.int32, (owners, count), 0) == orow_ref[...], terms_ref[...], 0.0
        )
        slot_hot = (lax.broadcasted_iota(jnp.int32, (slots, count), 0) == srow_ref[...]).astype(jnp.bfloat16)
        hi = weighted.astype(jnp.bfloat16)
        mid = (weighted - hi.astype(jnp.float32)).astype(jnp.bfloat16)
        nt = (((1,), (1,)), ((), ()))
        summed = lax.dot_general(hi, slot_hot, nt, preferred_element_type=jnp.float32) + lax.dot_general(
            mid, slot_hot, nt, preferred_element_type=jnp.float32
        )
        owner_ref[...] = summed.reshape(owners, 1, slots)


def field_spec(nx, ny, nz, chunk):
    return pl.BlockSpec((3, chunk, ny, nz), lambda i: (0, i, 0, 0))


def face_specs(nx, ny, nz, chunk):
    return [
        pl.BlockSpec((2, 1, ny, nz), lambda i: (0, 0, 0, 0)),
        pl.BlockSpec((2, chunk, 1, nz), lambda i: (0, i, 0, 0)),
        pl.BlockSpec((2, 1, 1, chunk * ny), lambda i: (0, i, 0, 0)),
    ]


def face_shapes(nx, ny, nz, dtype):
    return [
        jax.ShapeDtypeStruct((2, 1, ny, nz), dtype),
        jax.ShapeDtypeStruct((2, nx, 1, nz), dtype),
        jax.ShapeDtypeStruct((2, nx // CHUNK, 1, CHUNK * ny), dtype),
    ]


def faces_kernel(slab_ref, rows_ref, lanes_ref, fx_ref, fy_ref, fz_ref):
    fx_ref[0] = slab_ref[1]
    fx_ref[1] = slab_ref[2]
    fy_ref[0] = rows_ref[0, :, 0:1, :]
    fy_ref[1] = rows_ref[2, :, 0:1, :]
    nx = lanes_ref.shape[1]
    for i in range(nx // CHUNK):
        part = slice(i * CHUNK, (i + 1) * CHUNK)
        fz_ref[0, i] = row_of(lanes_ref[0, part], slice(0, 128))[0:1]
        fz_ref[1, i] = row_of(lanes_ref[1, part], slice(0, 128))[0:1]


def lower_faces_of(e):
    _, nx, ny, nz = e.shape
    return pl.pallas_call(
        faces_kernel,
        grid=(1,),
        in_specs=[
            pl.BlockSpec((3, 1, ny, nz), lambda i: (0, 0, 0, 0)),
            pl.BlockSpec((3, nx, 8, nz), lambda i: (0, 0, 0, 0)),
            pl.BlockSpec((3, nx, ny, 128), lambda i: (0, 0, 0, 0)),
        ],
        out_specs=[
            pl.BlockSpec((2, 1, ny, nz), lambda i: (0, 0, 0, 0)),
            pl.BlockSpec((2, nx, 1, nz), lambda i: (0, 0, 0, 0)),
            pl.BlockSpec((2, nx // CHUNK, 1, CHUNK * ny), lambda i: (0, 0, 0, 0)),
        ],
        out_shape=face_shapes(nx, ny, nz, e.dtype),
    )(e, e, e)


def h_step(e, h, faces):
    _, nx, ny, nz = e.shape
    chunk = CHUNK
    faces_x = toward_lower(faces[0], "gx")
    faces_y = toward_lower(faces[1], "gy")
    faces_z = toward_lower(faces[2], "gz")
    return pl.pallas_call(
        h_kernel,
        grid=(nx // chunk,),
        in_specs=[
            field_spec(nx, ny, nz, chunk),
            pl.BlockSpec((3, 1, ny, nz), lambda i: (0, jnp.minimum((i + 1) * chunk, nx - 1), 0, 0)),
            field_spec(nx, ny, nz, chunk),
            pl.BlockSpec((2, 1, ny, nz), lambda i: (0, 0, 0, 0)),
            pl.BlockSpec((2, chunk, 1, nz), lambda i: (0, i, 0, 0)),
            pl.BlockSpec((2, 1, 1, chunk * ny), lambda i: (0, i, 0, 0)),
        ],
        out_specs=[field_spec(nx, ny, nz, chunk)] + face_specs(nx, ny, nz, chunk),
        out_shape=[jax.ShapeDtypeStruct(h.shape, h.dtype)] + face_shapes(nx, ny, nz, h.dtype),
    )(e, e, h, faces_x, faces_y, faces_z)


def e_step(e, h, faces, inv, ef=None, cells=None, owners=None, slots=None, devices=None):
    _, nx, ny, nz = e.shape
    chunk = CHUNK
    faces_x = toward_upper(faces[0], "gx")
    faces_y = toward_upper(faces[1], "gy")
    faces_z = toward_upper(faces[2], "gz")
    in_specs = [
        field_spec(nx, ny, nz, chunk),
        field_spec(nx, ny, nz, chunk),
        pl.BlockSpec((3, 1, ny, nz), lambda i: (0, jnp.maximum(i * chunk - 1, 0), 0, 0)),
        pl.BlockSpec((chunk, ny, nz), lambda i: (i, 0, 0)),
        pl.BlockSpec((2, 1, ny, nz), lambda i: (0, 0, 0, 0)),
        pl.BlockSpec((2, chunk, 1, nz), lambda i: (0, i, 0, 0)),
        pl.BlockSpec((2, 1, 1, chunk * ny), lambda i: (0, i, 0, 0)),
    ]
    args = [e, h, h, inv, faces_x, faces_y, faces_z]
    if ef is None:
        outs = pl.pallas_call(
            e_kernel,
            grid=(nx // chunk,),
            in_specs=in_specs,
            out_specs=[field_spec(nx, ny, nz, chunk)] + face_specs(nx, ny, nz, chunk),
            out_shape=[jax.ShapeDtypeStruct(e.shape, e.dtype)] + face_shapes(nx, ny, nz, e.dtype),
        )(*args)
        return outs[0], outs[1:]
    count = cells.shape[0]
    zrow = (cells % nz).reshape(1, count)
    rrow = (cells // nz).reshape(1, count)
    return pl.pallas_call(
        e_last_kernel,
        grid=(nx // chunk,),
        in_specs=in_specs
        + [
            field_spec(nx, ny, nz, chunk),
            pl.BlockSpec((1, count), lambda i: (0, 0)),
            pl.BlockSpec((1, count), lambda i: (0, 0)),
            pl.BlockSpec((1, count), lambda i: (0, 0)),
            pl.BlockSpec((1, count), lambda i: (0, 0)),
        ],
        out_specs=[field_spec(nx, ny, nz, chunk), pl.BlockSpec((devices, 1, P_DEV), lambda i: (0, 0, 0))],
        out_shape=[jax.ShapeDtypeStruct(e.shape, e.dtype), jax.ShapeDtypeStruct((devices, 1, P_DEV), jnp.float32)],
        scratch_shapes=[pltpu.VMEM((1, count), jnp.float32), pltpu.VMEM((nz, count), jnp.bfloat16)],
    )(*args, ef, zrow, rrow, owners.reshape(1, count), slots.reshape(1, count))


def body(e_forward, e_adjoint, h_adjoint, inv_perm, voxel_cell, voxel_owner, voxel_slot):
    count = voxel_cell.shape[-1]
    voxel_rows = voxel_cell.reshape(count)
    owners = voxel_owner.reshape(count)
    slot_ids = voxel_slot.reshape(count)
    devices = lax.axis_size("gx") * lax.axis_size("gy") * lax.axis_size("gz")
    e, h = e_adjoint, h_adjoint
    e_faces = lower_faces_of(e)
    per_owner = None
    for repeat in range(STEPS):
        h, *h_faces = h_step(e, h, e_faces)
        if repeat == STEPS - 1:
            e, per_owner = e_step(e, h, h_faces, inv_perm, e_forward, voxel_rows, owners, slot_ids, devices)
        else:
            e, e_faces = e_step(e, h, h_faces, inv_perm)
    received = lax.all_to_all(per_owner, ("gx", "gy", "gz"), 0, 0, tiled=True)
    gradient = received.sum(axis=(0, 1))
    return (e, h, gradient)


def solution(mesh):
    return jax.shard_map(
        body,
        mesh=mesh,
        in_specs=(
            P(None, "gx", "gy", "gz"),
            P(None, "gx", "gy", "gz"),
            P(None, "gx", "gy", "gz"),
            P("gx", "gy", "gz"),
            P("gx", "gy", "gz", None),
            P("gx", "gy", "gz", None, None),
            P("gx", "gy", "gz", None),
        ),
        out_specs=(P(None, "gx", "gy", "gz"), P(None, "gx", "gy", "gz"), P(("gx", "gy", "gz"))),
        check_vma=False,
    )
```
